32 devices in a mesh: ctx: 8 (over y, x, core), head: 4 (over z).
Axes of the slice: x: 2, y: 2, z: 4, core: 2. Of those that a mesh axis runs over, the one named last changes fastest.
Arguments:
- doc_lengths: int32 [6], replicated, may hold values from 1 to 512, 1024 in all
- lin_q: bfloat16 [1024, 8192], P('ctx', 'head'), may hold values from -6 to 6
- lin_k: bfloat16 [1024, 8192], P('ctx', 'head'), may hold values from -6 to 6
- lin_v: bfloat16 [1024, 8192], P('ctx', 'head'), may hold values from -6 to 6
- log_decay: float32 [64, 1024], P('head', 'ctx'), may hold values from -0.8 to 0
- out_gate: bfloat16 [1024, 8192], P('ctx', 'head'), may hold values from -6 to 6
- lin_gain: float32 [8192], P('head'), may hold values from 0.5 to 1.5
- soft_q: bfloat16 [1024, 8192], P('ctx', 'head'), may hold values from -200 to 200
- soft_k: bfloat16 [1024, 1024], P('ctx', 'head'), may hold values from -7 to 7
- soft_v: bfloat16 [1024, 1024], P('ctx', 'head'), may hold values from -6 to 6
Outputs:
- lin_out: bfloat16 [1024, 8192], P('ctx', 'head')
- soft_out: bfloat16 [1024, 8192], P('ctx', 'head')
The draws below stay inside these ranges and needn't reach their ends.
Inputs may be any that keep to these rules, and one draw needn't show every extreme that they name: `doc_lengths`: the documents lie end to end and fill all 1024 positions; the longest has exactly 512 positions.
All inputs are finite; a program needn't handle non-finite values.
Results may differ from the reference program's by a relative error of at most 0.0054.
Values may be sent and summed in bfloat16 or wider, within the bound.
No kernel may reach another device: no remote copies, remote signals or barrier semaphores. Data moves between devices by JAX's collectives and lax.ppermute only.
A program may use at most 64 MiB of HBM per device.

```python
import math
import jax
import jax.numpy as jnp
import numpy as np
from jax import lax

ATTENDER_TOTAL = 64
DH = 128
KV_HEADS = 8
TOK_DEV = 128
SPAN = 4
PACKED_SPAN = 1024
LONGEST_PASSAGE = 512
DOCS = 6
N_CTX = 8


def draw_log_decay(key, part):
    lookup_array = jax.random.split(jax.random.fold_in(key, 11), 6)
    share = 0.5
    fast = jax.random.uniform(lookup_array[0], (ATTENDER_TOTAL, 1)) < share
    fast_rate = jax.random.uniform(lookup_array[1], (ATTENDER_TOTAL, 1), minval=1.0 / 50.0, maxval=1.0 / 30.0)
    slow_rate = jnp.exp(jax.random.uniform(lookup_array[2], (ATTENDER_TOTAL, 1), minval=math.log(0.05), maxval=math.log(0.5))) / LONGEST_PASSAGE
    forgetting_speed = jnp.where(fast, fast_rate, slow_rate)
    shrinkage_multiplier = jnp.exp(jax.random.uniform(lookup_array[3], (1, PACKED_SPAN // TOK_DEV), minval=math.log(0.5), maxval=math.log(2.0)))
    shrinkage_multiplier = jnp.repeat(shrinkage_multiplier, TOK_DEV, axis=1)
    rough_guess = jax.random.uniform(lookup_array[4], (ATTENDER_TOTAL, PACKED_SPAN), minval=0.5, maxval=1.5)
    spike_chance = 1.0 / (2.0 * LONGEST_PASSAGE)
    pick_spike = jax.random.uniform(lookup_array[5], (ATTENDER_TOTAL, PACKED_SPAN))
    spike_extent = jnp.where(pick_spike < spike_chance, jnp.log(0.5 + 0.3 * pick_spike / spike_chance), 0.0)
    return (-forgetting_speed * shrinkage_multiplier * rough_guess + spike_extent).astype(jnp.float32)


def soft_pair(key):
    lookup_array = jax.random.split(jax.random.fold_in(key, 23), 2)
    group = ATTENDER_TOTAL // KV_HEADS
    key_rows = jnp.clip(jax.random.normal(lookup_array[0], (PACKED_SPAN, KV_HEADS, DH)), -6.0, 6.0)
    query = jnp.clip(jax.random.normal(lookup_array[1], (PACKED_SPAN, KV_HEADS, group, DH)), -6.0, 6.0)
    return (query.reshape(PACKED_SPAN, ATTENDER_TOTAL * DH), key_rows.reshape(PACKED_SPAN, KV_HEADS * DH))


def draw_soft_q(key, part):
    return soft_pair(key)[0].astype(jnp.bfloat16)


def draw_soft_k(key, part):
    return soft_pair(key)[1].astype(jnp.bfloat16)


def block_scale(key, shape, shards, least, high):
    factor_of = 1.0
    for dim, blocks in shards:
        steps = jax.random.uniform(jax.random.fold_in(jax.random.fold_in(key, 6), dim), (blocks,), jnp.float32, least / len(shards), high / len(shards))
        factor_of = factor_of * jnp.repeat(jnp.exp(steps), shape[dim] // blocks).reshape((-1,) + (1,) * (len(shape) - 1 - dim))
    return factor_of


def profile(number_of, total, reach, lean):
    weights = [(1 << 20) // math.isqrt(grade ** lean) + 1 for grade in range(2, number_of + 1)]
    surplus, given = total - reach - (number_of - 1), [1] * (number_of - 1)
    while surplus > 0:
        movable = [i for i in range(number_of - 1) if given[i] < reach]
        pool, left = sum([weights[i] for i in movable]), surplus
        for i in movable:
            more = min(reach - given[i], max(1, left * weights[i] // pool), surplus)
            given[i] = given[i] + more
            surplus = surplus - more
    return np.array([reach] + given)


def ragged(stream_key, amount, total, most, lean):
    if amount == 2:
        one = jax.random.randint(stream_key, (), max(1, total - most), min(most, total - 1) + 1)
        return jnp.stack([one, total - one])
    lengths = jnp.asarray(profile(amount, total, most, lean), jnp.int32)
    pairs = (amount - 1) // 2
    giver, sink = lengths[1:1 + 2 * pairs:2], lengths[2:2 + 2 * pairs:2]
    margin = jnp.minimum(giver - 1, most - sink)
    shifted = jax.random.randint(jax.random.fold_in(stream_key, 1), (pairs,), 0, 1 << 20) % (margin + 1)
    lengths = lengths.at[1:1 + 2 * pairs:2].set(giver - shifted).at[2:2 + 2 * pairs:2].set(sink + shifted)
    return lengths[jax.random.permutation(jax.random.fold_in(stream_key, 2), amount)]


def noise(key, extent, width, bound, shards=(), held_as=jnp.bfloat16):
    loudness = block_scale(key, extent, shards, -0.22, 0.18) if shards else 1.0
    array = jax.random.normal(key, extent, jnp.float32) * width * loudness
    return jnp.minimum(jnp.maximum(array, -bound), bound).astype(held_as)


def setup_inputs(seed: int = 0) -> dict:
    arg_keys = jax.random.split(jax.random.key(seed), 11)
    doc_lengths = ragged(arg_keys[0], DOCS, PACKED_SPAN, LONGEST_PASSAGE, 2).astype(jnp.int32)
    lin_q = noise(arg_keys[1], (PACKED_SPAN, ATTENDER_TOTAL * DH), 1.0, 6.0, ((0, 8), (1, 4)))
    lin_k = noise(arg_keys[2], (PACKED_SPAN, ATTENDER_TOTAL * DH), 1.0, 6.0, ((0, 8), (1, 4)))
    lin_v = noise(arg_keys[3], (PACKED_SPAN, ATTENDER_TOTAL * DH), 1.0, 6.0, ((0, 8), (1, 4)))
    log_decay = draw_log_decay(jax.random.fold_in(arg_keys[10], 71), 0)
    out_gate = noise(arg_keys[5], (PACKED_SPAN, ATTENDER_TOTAL * DH), 1.5, 6.0, ((0, 8), (1, 4)))
    lin_gain = jnp.clip(1.0 + 0.1 * jax.random.normal(arg_keys[6], (ATTENDER_TOTAL * DH,), jnp.float32), 0.5, 1.5)
    soft_q = draw_soft_q(jax.random.fold_in(arg_keys[10], 71), 0)
    soft_k = draw_soft_k(jax.random.fold_in(arg_keys[10], 71), 0)
    soft_v = noise(arg_keys[9], (PACKED_SPAN, KV_HEADS * DH), 1.0, 6.0, ((0, 8), (1, 4)))
    return dict(doc_lengths=doc_lengths, lin_q=lin_q, lin_k=lin_k, lin_v=lin_v, log_decay=log_decay, out_gate=out_gate, lin_gain=lin_gain, soft_q=soft_q, soft_k=soft_k, soft_v=soft_v)


def document_of(positions, doc_lengths):
    ends = jnp.cumsum(doc_lengths).astype(jnp.int32)
    return lax.optimization_barrier(jnp.sum((ends[None, :] <= positions[:, None]).astype(jnp.int32), axis=1)).astype(jnp.int32)

def light_block(query, lookup_array, values, decay, docs, before):
    rows = docs.shape[0]
    level = jnp.cumsum(decay, axis=1)
    order = jnp.arange(rows)
    same = (docs[:, None] == docs[None, :]) & (order[None, :] <= order[:, None])
    scores = jnp.einsum('thd,shd->hts', query.astype(jnp.float32), lookup_array.astype(jnp.float32))
    fade = jnp.exp(jnp.minimum(level[:, :, None] - level[:, None, :], 0.0))
    weights = jnp.where(same[None], scores * fade, 0.0).astype(jnp.bfloat16)
    weights = lax.optimization_barrier(weights).astype(jnp.float32)
    inner = jnp.einsum('hts,shd->thd', weights, values.astype(jnp.float32))
    carried = docs == before
    closing = (docs == docs[-1]).astype(jnp.float32)
    tail = jnp.exp(level[:, -1:] - level) * closing[None, :]
    weighted = (lookup_array.astype(jnp.float32) * tail.T[:, :, None]).astype(jnp.bfloat16)
    weighted = lax.optimization_barrier(weighted).astype(jnp.float32)
    state = jnp.einsum('shd,she->hde', weighted, values.astype(jnp.float32))
    shrinkage_multiplier = jnp.exp(level[:, -1]) * carried[-1].astype(jnp.float32)
    return (inner, level, carried, shrinkage_multiplier, state)

def reference(doc_lengths, lin_q, lin_k, lin_v, log_decay, out_gate, lin_gain, soft_q, soft_k, soft_v):
    positions = jnp.arange(PACKED_SPAN, dtype=jnp.int32)
    docs = document_of(positions, doc_lengths)
    blocks = N_CTX
    q_blocks = lin_q.reshape(blocks, TOK_DEV, ATTENDER_TOTAL, DH)
    k_blocks = lin_k.reshape(blocks, TOK_DEV, ATTENDER_TOTAL, DH)
    v_blocks = lin_v.reshape(blocks, TOK_DEV, ATTENDER_TOTAL, DH)
    d_blocks = log_decay.reshape(ATTENDER_TOTAL, blocks, TOK_DEV).transpose(1, 0, 2)
    g_blocks = out_gate.reshape(blocks, TOK_DEV, ATTENDER_TOTAL * DH)
    doc_blocks = docs.reshape(blocks, TOK_DEV)
    before_blocks = jnp.concatenate([jnp.full((1,), -1, jnp.int32), doc_blocks[:-1, -1]])

    def light_step(incoming, pieces):
        query, lookup_array, values, decay, block_docs, before, gate = pieces
        inner, level, carried, shrinkage_multiplier, state = light_block(query, lookup_array, values, decay, block_docs, before)
        rounded = lax.optimization_barrier(incoming.astype(jnp.bfloat16)).astype(jnp.float32)
        outer = jnp.einsum('thd,hde->the', query.astype(jnp.float32), rounded)
        outer = outer * (jnp.exp(level).T * carried[:, None].astype(jnp.float32))[:, :, None]
        mixed = inner + outer
        mean_sq = lax.optimization_barrier(jnp.mean(mixed * mixed, axis=(1, 2)))
        flat = mixed.reshape(TOK_DEV, ATTENDER_TOTAL * DH)
        normed = flat * lax.rsqrt(mean_sq + 1e-06)[:, None] * lin_gain[None, :] * jax.nn.sigmoid(gate.astype(jnp.float32))
        return (shrinkage_multiplier[:, None, None] * incoming + state, normed.astype(jnp.bfloat16))
    start_state = jnp.zeros((ATTENDER_TOTAL, DH, DH), jnp.float32)
    _, lin_blocks = lax.scan(light_step, start_state, (q_blocks, k_blocks, v_blocks, d_blocks, doc_blocks, before_blocks, g_blocks))
    lin_out = lin_blocks.reshape(PACKED_SPAN, ATTENDER_TOTAL * DH)
    group = ATTENDER_TOTAL // KV_HEADS
    window = (SPAN + 1) * TOK_DEV
    pad_rows = SPAN * TOK_DEV
    keys_pad = jnp.concatenate([jnp.zeros((pad_rows, KV_HEADS * DH), soft_k.dtype), soft_k]).reshape(-1, KV_HEADS, DH)
    values_pad = jnp.concatenate([jnp.zeros((pad_rows, KV_HEADS * DH), soft_v.dtype), soft_v]).reshape(-1, KV_HEADS, DH)
    docs_pad = jnp.concatenate([jnp.full((pad_rows,), -1, jnp.int32), docs])
    q_soft = soft_q.reshape(blocks, TOK_DEV, KV_HEADS, group, DH)

    def soft_step(index):
        start = (index * TOK_DEV).astype(jnp.int32)
        query = q_soft[index]
        lookup_array = lax.dynamic_slice(keys_pad, (start, jnp.int32(0), jnp.int32(0)), (window, KV_HEADS, DH))
        values = lax.dynamic_slice(values_pad, (start, jnp.int32(0), jnp.int32(0)), (window, KV_HEADS, DH))
        key_docs = lax.dynamic_slice(docs_pad, (start,), (window,))
        key_pos = start - pad_rows + jnp.arange(window, dtype=jnp.int32)
        query_pos = start + jnp.arange(TOK_DEV, dtype=jnp.int32)
        query_docs = lax.dynamic_slice(docs, (start,), (TOK_DEV,))
        allowed = (key_docs[None, :] == query_docs[:, None]) & (key_pos[None, :] <= query_pos[:, None])
        scores = jnp.einsum('tkgd,skd->kgts', query.astype(jnp.float32), lookup_array.astype(jnp.float32)) * DH ** (-0.5)
        top = lax.optimization_barrier(jnp.max(jnp.where(allowed, scores, -1e+30), axis=-1, keepdims=True))
        expd = jnp.where(allowed, jnp.exp(jnp.minimum(scores - top, 0.0)), 0.0)
        total = lax.optimization_barrier(jnp.sum(expd, axis=-1))
        probs = lax.optimization_barrier(expd.astype(jnp.bfloat16)).astype(jnp.float32)
        out = jnp.einsum('kgts,skd->tkgd', probs, values.astype(jnp.float32)) / total.transpose(2, 0, 1)[..., None]
        return out.reshape(TOK_DEV, ATTENDER_TOTAL * DH).astype(jnp.bfloat16)
    soft_blocks = lax.map(soft_step, jnp.arange(blocks, dtype=jnp.int32))
    soft_out = soft_blocks.reshape(PACKED_SPAN, ATTENDER_TOTAL * DH)
    return (lin_out, soft_out)
```

```python
import jax
import jax.numpy as jnp
from jax import lax
from jax.sharding import PartitionSpec as P

DH = 128
SPAN = 4


def from_behind(shard, axis, by):
    count = lax.axis_size(axis)
    pairs = [(i, i + by) for i in range(count) if 0 <= i + by < count]
    return lax.ppermute(shard, axis, pairs)


def all_sum(x, axis):
    count = lax.axis_size(axis)
    me = lax.axis_index(axis)
    parts = [x]
    for by in range(1, count):
        parts.append(lax.ppermute(x, axis, [(i, (i + by) % count) for i in range(count)]))
    stacked = jnp.stack(parts)
    order = (me - jnp.arange(count)) % count
    return jnp.sum(stacked[order], axis=0)


def document_of(positions, doc_lengths):
    ends = jnp.cumsum(doc_lengths)
    return jnp.sum((ends[None, :] <= positions[:, None]).astype(jnp.int32), axis=1)


def block_terms(query, lookup_array, values, decay, docs, before):
    rows = docs.shape[0]
    level = jnp.cumsum(decay, axis=1)
    order = jnp.arange(rows)
    same = (docs[:, None] == docs[None, :]) & (order[None, :] <= order[:, None])
    scores = jnp.einsum("thd,shd->hts", query, lookup_array, preferred_element_type=jnp.float32)
    fade = jnp.exp(jnp.minimum(level[:, :, None] - level[:, None, :], 0.0))
    weights = jnp.where(same[None], scores * fade, 0.0).astype(jnp.bfloat16)
    inner = jnp.einsum("hts,shd->thd", weights, values, preferred_element_type=jnp.float32)
    carried = docs == before
    closing = (docs == docs[-1]).astype(jnp.float32)
    tail = jnp.exp(level[:, -1:] - level) * closing[None, :]
    weighted = (lookup_array.astype(jnp.float32) * tail.T[:, :, None]).astype(jnp.bfloat16)
    state = jnp.einsum("shd,she->hde", weighted, values, preferred_element_type=jnp.float32)
    shrinkage_multiplier = jnp.exp(level[:, -1]) * carried[-1].astype(jnp.float32)
    return (inner, level, carried, shrinkage_multiplier, state)


def local(doc_lengths, lin_q, lin_k, lin_v, log_decay, out_gate, lin_gain, soft_q, soft_k, soft_v):
    rows = lin_q.shape[0]
    heads_here = lin_q.shape[1] // DH
    kv_here = soft_k.shape[1] // DH
    group = soft_q.shape[1] // (kv_here * DH)
    shard = lax.axis_index("ctx")
    positions = shard * rows + jnp.arange(rows, dtype=jnp.int32)
    docs = document_of(positions, doc_lengths)
    before = jnp.where(shard > 0, document_of(positions[:1] - 1, doc_lengths)[0], -1)
    query = lin_q.reshape(rows, heads_here, DH)
    lookup_array = lin_k.reshape(rows, heads_here, DH)
    values = lin_v.reshape(rows, heads_here, DH)
    inner, level, carried, shrinkage_multiplier, state = block_terms(
        query, lookup_array, values, log_decay, docs, before
    )
    kv_width = soft_k.shape[1]
    pair = jnp.concatenate([soft_k, soft_v], axis=1)
    state_b = state.astype(jnp.bfloat16)
    key_blocks = [soft_k]
    value_blocks = [soft_v]
    incoming = jnp.zeros((heads_here, DH, DH), jnp.float32)
    running = jnp.ones((heads_here,), jnp.float32)
    for step in range(1, SPAN + 1):
        far_pair, far_factor, far_state = from_behind((pair, shrinkage_multiplier, state_b), "ctx", step)
        key_blocks.append(far_pair[:, :kv_width])
        value_blocks.append(far_pair[:, kv_width:])
        incoming = incoming + running[:, None, None] * far_state.astype(jnp.float32)
        running = running * far_factor
    outer = jnp.einsum(
        "thd,hde->the", query, incoming.astype(jnp.bfloat16), preferred_element_type=jnp.float32
    )
    outer = outer * (jnp.exp(level).T * carried[:, None].astype(jnp.float32))[:, :, None]
    mixed = inner + outer
    local_sq = jnp.sum(mixed * mixed, axis=(1, 2))
    total_sq = all_sum(local_sq, "head")
    mean_sq = total_sq / (lax.axis_size("head") * heads_here * DH)
    flat = mixed.reshape(rows, heads_here * DH)
    normed = (
        flat
        * lax.rsqrt(mean_sq + 1e-06)[:, None]
        * lin_gain[None, :]
        * jax.nn.sigmoid(out_gate.astype(jnp.float32))
    )
    lin_out = normed.astype(jnp.bfloat16)
    span_rows = (SPAN + 1) * rows
    all_keys = jnp.concatenate(key_blocks[::-1], axis=0).reshape(span_rows, kv_here, DH)
    all_values = jnp.concatenate(value_blocks[::-1], axis=0).reshape(span_rows, kv_here, DH)
    key_pos = shard * rows - SPAN * rows + jnp.arange(span_rows, dtype=jnp.int32)
    key_docs = jnp.where(key_pos >= 0, document_of(key_pos, doc_lengths), -1)
    allowed = (key_docs[None, :] == docs[:, None]) & (key_pos[None, :] <= positions[:, None])
    soft_query = soft_q.reshape(rows, kv_here, group, DH)
    scores = jnp.einsum(
        "tkgd,skd->kgts", soft_query, all_keys, preferred_element_type=jnp.float32
    ) * DH ** (-0.5)
    top = jnp.max(jnp.where(allowed, scores, -1e30), axis=-1, keepdims=True)
    expd = jnp.where(allowed, jnp.exp(jnp.minimum(scores - top, 0.0)), 0.0)
    total = jnp.sum(expd, axis=-1)
    attended = jnp.einsum(
        "kgts,skd->tkgd", expd.astype(jnp.bfloat16), all_values, preferred_element_type=jnp.float32
    )
    attended = attended / total.transpose(2, 0, 1)[..., None]
    soft_out = attended.reshape(rows, kv_here * group * DH).astype(jnp.bfloat16)
    return (lin_out, soft_out)


def solution(mesh):
    in_specs = (
        P(),
        P("ctx", "head"),
        P("ctx", "head"),
        P("ctx", "head"),
        P("head", "ctx"),
        P("ctx", "head"),
        P("head"),
        P("ctx", "head"),
        P("ctx", "head"),
        P("ctx", "head"),
    )
    out_specs = (P("ctx", "head"), P("ctx", "head"))
    return jax.shard_map(local, mesh=mesh, in_specs=in_specs, out_specs=out_specs, check_vma=False)
```

```python
import jax
import jax.numpy as jnp
from jax import lax
from jax.sharding import PartitionSpec as P

DH = 128
SPAN = 4


def from_behind(shard, axis, by):
    count = lax.axis_size(axis)
    pairs = [(i, i + by) for i in range(count) if 0 <= i + by < count]
    return lax.ppermute(shard, axis, pairs)


def all_sum(x, axis):
    count = lax.axis_size(axis)
    me = lax.axis_index(axis)
    parts = [x]
    for by in range(1, count):
        parts.append(lax.ppermute(x, axis, [(i, (i + by) % count) for i in range(count)]))
    stacked = jnp.stack(parts)
    order = (me - jnp.arange(count)) % count
    return jnp.sum(stacked[order], axis=0)


def document_of(positions, doc_lengths):
    ends = jnp.cumsum(doc_lengths)
    return jnp.sum((ends[None, :] <= positions[:, None]).astype(jnp.int32), axis=1)


def block_terms(query, lookup_array, values, decay, docs, before):
    rows = docs.shape[0]
    level = jnp.cumsum(decay, axis=1)
    order = jnp.arange(rows)
    same = (docs[:, None] == docs[None, :]) & (order[None, :] <= order[:, None])
    scores = jnp.einsum("thd,shd->hts", query, lookup_array, preferred_element_type=jnp.float32)
    fade = jnp.exp(jnp.minimum(level[:, :, None] - level[:, None, :], 0.0))
    weights = jnp.where(same[None], scores * fade, 0.0).astype(jnp.bfloat16)
    inner = jnp.einsum("hts,shd->thd", weights, values, preferred_element_type=jnp.float32)
    carried = docs == before
    closing = (docs == docs[-1]).astype(jnp.float32)
    tail = jnp.exp(level[:, -1:] - level) * closing[None, :]
    weighted = (lookup_array.astype(jnp.float32) * tail.T[:, :, None]).astype(jnp.bfloat16)
    state = jnp.einsum("shd,she->hde", weighted, values, preferred_element_type=jnp.float32)
    shrinkage_multiplier = jnp.exp(level[:, -1]) * carried[-1].astype(jnp.float32)
    return (inner, level, carried, shrinkage_multiplier, state)


def local(doc_lengths, lin_q, lin_k, lin_v, log_decay, out_gate, lin_gain, soft_q, soft_k, soft_v):
    rows = lin_q.shape[0]
    heads_here = lin_q.shape[1] // DH
    kv_here = soft_k.shape[1] // DH
    group = soft_q.shape[1] // (kv_here * DH)
    shard = lax.axis_index("ctx")
    positions = shard * rows + jnp.arange(rows, dtype=jnp.int32)
    docs = document_of(positions, doc_lengths)
    before = jnp.where(shard > 0, document_of(positions[:1] - 1, doc_lengths)[0], -1)
    query = lin_q.reshape(rows, heads_here, DH)
    lookup_array = lin_k.reshape(rows, heads_here, DH)
    values = lin_v.reshape(rows, heads_here, DH)
    inner, level, carried, shrinkage_multiplier, state = block_terms(
        query, lookup_array, values, log_decay, docs, before
    )
    count = lax.axis_size("ctx")
    odd = (shard % 2) == 1
    pair = jnp.concatenate([soft_k, soft_v], axis=1)
    kv_width = soft_k.shape[1]
    n_state = state.size
    n_factor = heads_here
    evens = [(i, i + 1) for i in range(0, count, 2)]
    first = jnp.concatenate(
        [state.reshape(-1), shrinkage_multiplier, pair.astype(jnp.float32).reshape(-1)]
    )
    got = lax.ppermute(first, "ctx", evens)
    state_prev = got[:n_state].reshape(state.shape)
    factor_prev = got[n_state : n_state + n_factor]
    pair_prev = got[n_state + n_factor :].reshape(pair.shape).astype(jnp.bfloat16)
    chip_state = shrinkage_multiplier[:, None, None] * state_prev + state
    chip_factor = shrinkage_multiplier * factor_prev
    factor_hi = chip_factor.astype(jnp.bfloat16)
    factor_lo = (chip_factor - factor_hi.astype(jnp.float32)).astype(jnp.bfloat16)
    packet = jnp.concatenate(
        [chip_state.astype(jnp.bfloat16).reshape(-1), factor_hi, factor_lo,
         pair_prev.reshape(-1), pair.reshape(-1)]
    )
    near = lax.ppermute(packet, "ctx", [(i, i + 1) for i in range(1, count - 1, 2)])
    far = lax.ppermute(packet, "ctx", [(i, i + 3) for i in range(1, count - 3, 2)])

    def unpack(got_packet):
        chip = got_packet[:n_state].reshape(state.shape).astype(jnp.float32)
        hi = got_packet[n_state : n_state + n_factor].astype(jnp.float32)
        lo = got_packet[n_state + n_factor : n_state + 2 * n_factor].astype(jnp.float32)
        blocks = got_packet[n_state + 2 * n_factor :].reshape((2,) + pair.shape)
        return chip, hi + lo, blocks

    state_near, factor_near, pairs_near = unpack(near)
    state_far, _, pairs_far = unpack(far)
    incoming_even = state_near + factor_near[:, None, None] * state_far
    onward = shrinkage_multiplier[:, None, None] * incoming_even + state
    fourth = jnp.concatenate(
        [onward.reshape(-1), pairs_far[1].astype(jnp.float32).reshape(-1),
         pairs_near.astype(jnp.float32).reshape(-1)]
    )
    back = lax.ppermute(fourth, "ctx", evens)
    incoming_odd = back[:n_state].reshape(state.shape)
    pairs_odd = back[n_state:].reshape((3,) + pair.shape).astype(jnp.bfloat16)
    incoming = jnp.where(odd, incoming_odd, incoming_even)
    window_even = jnp.concatenate([pairs_far[0], pairs_far[1], pairs_near[0], pairs_near[1]], axis=0)
    window_odd = jnp.concatenate([pairs_odd[0], pairs_odd[1], pairs_odd[2], pair_prev], axis=0)
    window = jnp.concatenate([jnp.where(odd, window_odd, window_even), pair], axis=0)
    outer = jnp.einsum(
        "thd,hde->the", query, incoming.astype(jnp.bfloat16), preferred_element_type=jnp.float32
    )
    outer = outer * (jnp.exp(level).T * carried[:, None].astype(jnp.float32))[:, :, None]
    mixed = inner + outer
    local_sq = jnp.sum(mixed * mixed, axis=(1, 2))
    total_sq = all_sum(local_sq, "head")
    mean_sq = total_sq / (lax.axis_size("head") * heads_here * DH)
    flat = mixed.reshape(rows, heads_here * DH)
    normed = (
        flat
        * lax.rsqrt(mean_sq + 1e-06)[:, None]
        * lin_gain[None, :]
        * jax.nn.sigmoid(out_gate.astype(jnp.float32))
    )
    lin_out = normed.astype(jnp.bfloat16)
    span_rows = (SPAN + 1) * rows
    all_keys = window[:, :kv_width].reshape(span_rows, kv_here, DH)
    all_values = window[:, kv_width:].reshape(span_rows, kv_here, DH)
    key_pos = shard * rows - SPAN * rows + jnp.arange(span_rows, dtype=jnp.int32)
    key_docs = jnp.where(key_pos >= 0, document_of(key_pos, doc_lengths), -1)
    allowed = (key_docs[None, :] == docs[:, None]) & (key_pos[None, :] <= positions[:, None])
    soft_query = soft_q.reshape(rows, kv_here, group, DH)
    scores = jnp.einsum(
        "tkgd,skd->kgts", soft_query, all_keys, preferred_element_type=jnp.float32
    ) * DH ** (-0.5)
    top = jnp.max(jnp.where(allowed, scores, -1e30), axis=-1, keepdims=True)
    expd = jnp.where(allowed, jnp.exp(jnp.minimum(scores - top, 0.0)), 0.0)
    total = jnp.sum(expd, axis=-1)
    attended = jnp.einsum(
        "kgts,skd->tkgd", expd.astype(jnp.bfloat16), all_values, preferred_element_type=jnp.float32
    )
    attended = attended / total.transpose(2, 0, 1)[..., None]
    soft_out = attended.reshape(rows, kv_here * group * DH).astype(jnp.bfloat16)
    return (lin_out, soft_out)


def solution(mesh):
    in_specs = (
        P(),
        P("ctx", "head"),
        P("ctx", "head"),
        P("ctx", "head"),
        P("head", "ctx"),
        P("ctx", "head"),
        P("head"),
        P("ctx", "head"),
        P("ctx", "head"),
        P("ctx", "head"),
    )
    out_specs = (P("ctx", "head"), P("ctx", "head"))
    return jax.shard_map(local, mesh=mesh, in_specs=in_specs, out_specs=out_specs, check_vma=False)
```

```python
import jax
import jax.numpy as jnp
from jax import lax
from jax.sharding import PartitionSpec as P

DH = 128
SPAN = 4


def from_behind(shard, axis, by):
    count = lax.axis_size(axis)
    pairs = [(i, i + by) for i in range(count) if 0 <= i + by < count]
    return lax.ppermute(shard, axis, pairs)


def all_sum(x, axis):
    count = lax.axis_size(axis)
    me = lax.axis_index(axis)
    parts = [x]
    for by in range(1, count):
        parts.append(lax.ppermute(x, axis, [(i, (i + by) % count) for i in range(count)]))
    stacked = jnp.stack(parts)
    order = (me - jnp.arange(count)) % count
    return jnp.sum(stacked[order], axis=0)


def document_of(positions, doc_lengths):
    ends = jnp.cumsum(doc_lengths)
    return jnp.sum((ends[None, :] <= positions[:, None]).astype(jnp.int32), axis=1)


def block_terms(query, lookup_array, values, decay, docs, before):
    rows = docs.shape[0]
    level = jnp.cumsum(decay, axis=1)
    order = jnp.arange(rows)
    same = (docs[:, None] == docs[None, :]) & (order[None, :] <= order[:, None])
    scores = jnp.einsum("thd,shd->hts", query, lookup_array, preferred_element_type=jnp.float32)
    fade = jnp.exp(jnp.minimum(level[:, :, None] - level[:, None, :], 0.0))
    weights = jnp.where(same[None], scores * fade, 0.0).astype(jnp.bfloat16)
    inner = jnp.einsum("hts,shd->thd", weights, values, preferred_element_type=jnp.float32)
    carried = docs == before
    closing = (docs == docs[-1]).astype(jnp.float32)
    tail = jnp.exp(level[:, -1:] - level) * closing[None, :]
    weighted = (lookup_array.astype(jnp.float32) * tail.T[:, :, None]).astype(jnp.bfloat16)
    state = jnp.einsum("shd,she->hde", weighted, values, preferred_element_type=jnp.float32)
    shrinkage_multiplier = jnp.exp(level[:, -1]) * carried[-1].astype(jnp.float32)
    return (inner, level, carried, shrinkage_multiplier, state)


def local(doc_lengths, lin_q, lin_k, lin_v, log_decay, out_gate, lin_gain, soft_q, soft_k, soft_v):
    rows = lin_q.shape[0]
    heads_here = lin_q.shape[1] // DH
    kv_here = soft_k.shape[1] // DH
    group = soft_q.shape[1] // (kv_here * DH)
    shard = lax.axis_index("ctx")
    positions = shard * rows + jnp.arange(rows, dtype=jnp.int32)
    docs = document_of(positions, doc_lengths)
    before = jnp.where(shard > 0, document_of(positions[:1] - 1, doc_lengths)[0], -1)
    query = lin_q.reshape(rows, heads_here, DH)
    lookup_array = lin_k.reshape(rows, heads_here, DH)
    values = lin_v.reshape(rows, heads_here, DH)
    inner, level, carried, shrinkage_multiplier, state = block_terms(
        query, lookup_array, values, log_decay, docs, before
    )
    count = lax.axis_size("ctx")
    odd = (shard % 2) == 1
    pair = jnp.concatenate(
        [soft_k.reshape(rows, kv_here, DH).transpose(1, 0, 2),
         soft_v.reshape(rows, kv_here, DH).transpose(1, 0, 2)],
        axis=0,
    ).reshape(-1, DH)
    n_pair = pair.shape[0]
    n_state = heads_here * DH
    state_rows = state.reshape(n_state, DH)
    factor_rows = jnp.pad(shrinkage_multiplier[None, :], ((0, 7), (0, DH - heads_here)))
    first = jnp.concatenate([state_rows, factor_rows, pair.astype(jnp.float32)], axis=0)
    got = lax.ppermute(first, "ctx", [(i, i ^ 1) for i in range(count)])
    state_mate = got[:n_state]
    factor_mate = got[n_state, :heads_here]
    pair_mate = got[n_state + 8 :].astype(jnp.bfloat16)
    state_lo = jnp.where(odd, state_mate, state_rows).reshape(state.shape)
    state_hi = jnp.where(odd, state_rows, state_mate).reshape(state.shape)
    factor_lo = jnp.where(odd, factor_mate, shrinkage_multiplier)
    factor_hi = jnp.where(odd, shrinkage_multiplier, factor_mate)
    pair_lo = jnp.where(odd, pair_mate, pair)
    pair_hi = jnp.where(odd, pair, pair_mate)
    chip_state = factor_hi[:, None, None] * state_lo + state_hi
    chip_factor = factor_hi * factor_lo
    chip_top = chip_factor.astype(jnp.bfloat16)
    chip_rest = (chip_factor - chip_top.astype(jnp.float32)).astype(jnp.bfloat16)
    chip_rows = jnp.pad(jnp.stack([chip_top, chip_rest]), ((0, 14), (0, DH - heads_here)))
    packet = jnp.concatenate(
        [chip_state.astype(jnp.bfloat16).reshape(n_state, DH), chip_rows, pair_lo, pair_hi], axis=0
    )
    near = lax.ppermute(packet, "ctx", [(i, i + 1) for i in range(1, count - 1, 2)])
    far = lax.ppermute(packet, "ctx", [(i, i + 4) for i in range(0, count - 4, 2)])

    def unpack(got_packet):
        chip = got_packet[:n_state].reshape(state.shape).astype(jnp.float32)
        mult = got_packet[n_state, :heads_here].astype(jnp.float32) + got_packet[
            n_state + 1, :heads_here
        ].astype(jnp.float32)
        low = got_packet[n_state + 16 : n_state + 16 + n_pair]
        high = got_packet[n_state + 16 + n_pair :]
        return chip, mult, low, high

    state_near, factor_near, near_lo, near_hi = unpack(near)
    state_far, _, far_lo, far_hi = unpack(far)
    incoming_even = state_near + factor_near[:, None, None] * state_far
    onward = shrinkage_multiplier[:, None, None] * incoming_even + state
    fourth = jnp.concatenate(
        [onward.astype(jnp.bfloat16).reshape(n_state, DH), far_hi, near_lo, near_hi], axis=0
    )
    back = lax.ppermute(fourth, "ctx", [(i, i + 1) for i in range(0, count, 2)])
    incoming_odd = back[:n_state].reshape(state.shape)
    incoming_b = jnp.where(odd, incoming_odd, incoming_even.astype(jnp.bfloat16))
    window_even = jnp.concatenate([far_lo, far_hi, near_lo, near_hi], axis=0)
    window_odd = jnp.concatenate([back[n_state:], pair_mate], axis=0)
    window = jnp.concatenate([jnp.where(odd, window_odd, window_even), pair], axis=0)
    window = window.reshape(SPAN + 1, 2 * kv_here, rows, DH)
    outer = jnp.einsum(
        "thd,hde->the", query, incoming_b, preferred_element_type=jnp.float32
    )
    outer = outer * (jnp.exp(level).T * carried[:, None].astype(jnp.float32))[:, :, None]
    mixed = inner + outer
    local_sq = jnp.sum(mixed * mixed, axis=(1, 2))
    total_sq = all_sum(local_sq, "head")
    mean_sq = total_sq / (lax.axis_size("head") * heads_here * DH)
    flat = mixed.reshape(rows, heads_here * DH)
    normed = (
        flat
        * lax.rsqrt(mean_sq + 1e-06)[:, None]
        * lin_gain[None, :]
        * jax.nn.sigmoid(out_gate.astype(jnp.float32))
    )
    lin_out = normed.astype(jnp.bfloat16)
    span_rows = (SPAN + 1) * rows
    key_pos = shard * rows - SPAN * rows + jnp.arange(span_rows, dtype=jnp.int32)
    key_docs = jnp.where(key_pos >= 0, document_of(key_pos, doc_lengths), -1)
    allowed = (key_docs[None, :] == docs[:, None]) & (key_pos[None, :] <= positions[:, None])
    soft_query = soft_q.reshape(rows, kv_here, group, DH)
    scores = jnp.einsum(
        "tkgd,bksd->kgtbs", soft_query, window[:, :kv_here], preferred_element_type=jnp.float32
    ).reshape(kv_here, group, rows, span_rows) * DH ** (-0.5)
    top = jnp.max(jnp.where(allowed, scores, -1e30), axis=-1, keepdims=True)
    expd = jnp.where(allowed, jnp.exp(jnp.minimum(scores - top, 0.0)), 0.0)
    total = jnp.sum(expd, axis=-1)
    attended = jnp.einsum(
        "kgtbs,bksd->tkgd",
        expd.astype(jnp.bfloat16).reshape(kv_here, group, rows, SPAN + 1, rows),
        window[:, kv_here:],
        preferred_element_type=jnp.float32,
    )
    attended = attended / total.transpose(2, 0, 1)[..., None]
    soft_out = attended.reshape(rows, kv_here * group * DH).astype(jnp.bfloat16)
    return (lin_out, soft_out)


def solution(mesh):
    in_specs = (
        P(),
        P("ctx", "head"),
        P("ctx", "head"),
        P("ctx", "head"),
        P("head", "ctx"),
        P("ctx", "head"),
        P("head"),
        P("ctx", "head"),
        P("ctx", "head"),
        P("ctx", "head"),
    )
    out_specs = (P("ctx", "head"), P("ctx", "head"))
    return jax.shard_map(local, mesh=mesh, in_specs=in_specs, out_specs=out_specs, check_vma=False)
```

```python
import jax
import jax.numpy as jnp
from jax import lax
from jax.sharding import PartitionSpec as P

DH = 128
SPAN = 4


def from_behind(shard, axis, by):
    count = lax.axis_size(axis)
    pairs = [(i, i + by) for i in range(count) if 0 <= i + by < count]
    return lax.ppermute(shard, axis, pairs)


def all_sum(x, axis):
    count = lax.axis_size(axis)
    me = lax.axis_index(axis)
    parts = [x]
    for by in range(1, count):
        parts.append(lax.ppermute(x, axis, [(i, (i + by) % count) for i in range(count)]))
    stacked = jnp.stack(parts)
    order = (me - jnp.arange(count)) % count
    return jnp.sum(stacked[order], axis=0)


def document_of(positions, doc_lengths):
    ends = jnp.cumsum(doc_lengths)
    return jnp.sum((ends[None, :] <= positions[:, None]).astype(jnp.int32), axis=1)


def block_terms(query, lookup_array, values, decay, docs, before):
    rows = docs.shape[0]
    level = jnp.cumsum(decay, axis=1)
    order = jnp.arange(rows)
    same = (docs[:, None] == docs[None, :]) & (order[None, :] <= order[:, None])
    scores = jnp.einsum("thd,shd->hts", query, lookup_array, preferred_element_type=jnp.float32)
    fade = jnp.exp(jnp.minimum(level[:, :, None] - level[:, None, :], 0.0))
    weights = jnp.where(same[None], scores * fade, 0.0).astype(jnp.bfloat16)
    inner = jnp.einsum("hts,shd->thd", weights, values, preferred_element_type=jnp.float32)
    carried = docs == before
    closing = (docs == docs[-1]).astype(jnp.float32)
    tail = jnp.exp(level[:, -1:] - level) * closing[None, :]
    weighted = (lookup_array.astype(jnp.float32) * tail.T[:, :, None]).astype(jnp.bfloat16)
    state = jnp.einsum("shd,she->hde", weighted, values, preferred_element_type=jnp.float32)
    shrinkage_multiplier = jnp.exp(level[:, -1]) * carried[-1].astype(jnp.float32)
    return (inner, level, carried, shrinkage_multiplier, state)


def local(doc_lengths, lin_q, lin_k, lin_v, log_decay, out_gate, lin_gain, soft_q, soft_k, soft_v):
    rows = lin_q.shape[0]
    heads_here = lin_q.shape[1] // DH
    kv_here = soft_k.shape[1] // DH
    group = soft_q.shape[1] // (kv_here * DH)
    shard = lax.axis_index("ctx")
    positions = shard * rows + jnp.arange(rows, dtype=jnp.int32)
    docs = document_of(positions, doc_lengths)
    before = jnp.where(shard > 0, document_of(positions[:1] - 1, doc_lengths)[0], -1)
    query = lin_q.reshape(rows, heads_here, DH)
    lookup_array = lin_k.reshape(rows, heads_here, DH)
    values = lin_v.reshape(rows, heads_here, DH)
    inner, level, carried, shrinkage_multiplier, state = block_terms(
        query, lookup_array, values, log_decay, docs, before
    )
    count = lax.axis_size("ctx")
    odd = (shard % 2) == 1
    pair = jnp.concatenate(
        [soft_k.reshape(rows, kv_here, DH).transpose(1, 0, 2),
         soft_v.reshape(rows, kv_here, DH).transpose(1, 0, 2)],
        axis=0,
    ).reshape(-1, DH)
    n_pair = pair.shape[0]
    n_state = heads_here * DH
    state_rows = state.reshape(n_state, DH)
    factor_rows = jnp.pad(shrinkage_multiplier[None, :], ((0, 7), (0, DH - heads_here)))
    first = jnp.concatenate([state_rows, factor_rows, pair.astype(jnp.float32)], axis=0)
    got = lax.ppermute(first, "ctx", [(i, i ^ 1) for i in range(count)])
    state_mate = got[:n_state]
    factor_mate = got[n_state, :heads_here]
    pair_mate = got[n_state + 8 :].astype(jnp.bfloat16)
    state_lo = jnp.where(odd, state_mate, state_rows).reshape(state.shape)
    state_hi = jnp.where(odd, state_rows, state_mate).reshape(state.shape)
    factor_lo = jnp.where(odd, factor_mate, shrinkage_multiplier)
    factor_hi = jnp.where(odd, shrinkage_multiplier, factor_mate)
    pair_lo = jnp.where(odd, pair_mate, pair)
    pair_hi = jnp.where(odd, pair, pair_mate)
    chip_state = factor_hi[:, None, None] * state_lo + state_hi
    chip_factor = factor_hi * factor_lo
    chip_top = chip_factor.astype(jnp.bfloat16)
    chip_rest = (chip_factor - chip_top.astype(jnp.float32)).astype(jnp.bfloat16)
    chip_rows = jnp.pad(jnp.stack([chip_top, chip_rest]), ((0, 14), (0, DH - heads_here)))
    packet = jnp.concatenate(
        [chip_state.astype(jnp.bfloat16).reshape(n_state, DH), chip_rows, pair_lo, pair_hi], axis=0
    )
    near = lax.ppermute(packet, "ctx", [(i, i + 1) for i in range(1, count - 1, 2)])
    far = lax.ppermute(packet, "ctx", [(i, i + 4) for i in range(0, count - 4, 2)])

    def unpack(got_packet):
        chip = got_packet[:n_state].reshape(state.shape).astype(jnp.float32)
        mult = got_packet[n_state, :heads_here].astype(jnp.float32) + got_packet[
            n_state + 1, :heads_here
        ].astype(jnp.float32)
        low = got_packet[n_state + 16 : n_state + 16 + n_pair]
        high = got_packet[n_state + 16 + n_pair :]
        return chip, mult, low, high

    state_near, factor_near, near_lo, near_hi = unpack(near)
    state_far, _, far_lo, far_hi = unpack(far)
    incoming_even = state_near + factor_near[:, None, None] * state_far
    onward = shrinkage_multiplier[:, None, None] * incoming_even + state
    fourth = jnp.concatenate(
        [onward.astype(jnp.bfloat16).reshape(n_state, DH), far_hi, near_lo, near_hi], axis=0
    )
    back = lax.ppermute(fourth, "ctx", [(i, i + 1) for i in range(0, count, 2)])
    incoming_odd = back[:n_state].reshape(state.shape)
    incoming_b = jnp.where(odd, incoming_odd, incoming_even.astype(jnp.bfloat16))
    window_even = jnp.concatenate([far_lo, far_hi, near_lo, near_hi], axis=0)
    window_odd = jnp.concatenate([back[n_state:], pair_mate], axis=0)
    window = jnp.concatenate([jnp.where(odd, window_odd, window_even), pair], axis=0)
    window = window.reshape(SPAN + 1, 2 * kv_here, rows, DH)
    outer = jnp.einsum(
        "thd,hde->the", query, incoming_b, preferred_element_type=jnp.float32
    )
    outer = outer * (jnp.exp(level).T * carried[:, None].astype(jnp.float32))[:, :, None]
    mixed = inner + outer
    local_sq = jnp.sum(mixed * mixed, axis=(1, 2))
    total_sq = lax.psum(local_sq, "head")
    mean_sq = total_sq / (lax.axis_size("head") * heads_here * DH)
    flat = mixed.reshape(rows, heads_here * DH)
    normed = (
        flat
        * lax.rsqrt(mean_sq + 1e-06)[:, None]
        * lin_gain[None, :]
        * jax.nn.sigmoid(out_gate.astype(jnp.float32))
    )
    lin_out = normed.astype(jnp.bfloat16)
    span_rows = (SPAN + 1) * rows
    key_pos = shard * rows - SPAN * rows + jnp.arange(span_rows, dtype=jnp.int32)
    key_docs = jnp.where(key_pos >= 0, document_of(key_pos, doc_lengths), -1)
    allowed = (key_docs[None, :] == docs[:, None]) & (key_pos[None, :] <= positions[:, None])
    soft_query = soft_q.reshape(rows, kv_here, group, DH)
    scores = jnp.einsum(
        "tkgd,bksd->kgtbs", soft_query, window[:, :kv_here], preferred_element_type=jnp.float32
    ).reshape(kv_here, group, rows, span_rows) * DH ** (-0.5)
    top = jnp.max(jnp.where(allowed, scores, -1e30), axis=-1, keepdims=True)
    expd = jnp.where(allowed, jnp.exp(jnp.minimum(scores - top, 0.0)), 0.0)
    total = jnp.sum(expd, axis=-1)
    attended = jnp.einsum(
        "kgtbs,bksd->tkgd",
        expd.astype(jnp.bfloat16).reshape(kv_here, group, rows, SPAN + 1, rows),
        window[:, kv_here:],
        preferred_element_type=jnp.float32,
    )
    attended = attended / total.transpose(2, 0, 1)[..., None]
    soft_out = attended.reshape(rows, kv_here * group * DH).astype(jnp.bfloat16)
    return (lin_out, soft_out)


def solution(mesh):
    in_specs = (
        P(),
        P("ctx", "head"),
        P("ctx", "head"),
        P("ctx", "head"),
        P("head", "ctx"),
        P("ctx", "head"),
        P("head"),
        P("ctx", "head"),
        P("ctx", "head"),
        P("ctx", "head"),
    )
    out_specs = (P("ctx", "head"), P("ctx", "head"))
    return jax.shard_map(local, mesh=mesh, in_specs=in_specs, out_specs=out_specs, check_vma=False)
```

```python
import jax
import jax.numpy as jnp
from jax import lax
from jax.sharding import PartitionSpec as P

DH = 128
SPAN = 4


def from_behind(shard, axis, by):
    count = lax.axis_size(axis)
    pairs = [(i, i + by) for i in range(count) if 0 <= i + by < count]
    return lax.ppermute(shard, axis, pairs)


def all_sum(x, axis):
    count = lax.axis_size(axis)
    me = lax.axis_index(axis)
    parts = [x]
    for by in range(1, count):
        parts.append(lax.ppermute(x, axis, [(i, (i + by) % count) for i in range(count)]))
    stacked = jnp.stack(parts)
    order = (me - jnp.arange(count)) % count
    return jnp.sum(stacked[order], axis=0)


def document_of(positions, doc_lengths):
    ends = jnp.cumsum(doc_lengths)
    return jnp.sum((ends[None, :] <= positions[:, None]).astype(jnp.int32), axis=1)


def block_terms(query, lookup_array, values, decay, docs, before):
    rows = docs.shape[0]
    level = jnp.cumsum(decay, axis=1)
    order = jnp.arange(rows)
    same = (docs[:, None] == docs[None, :]) & (order[None, :] <= order[:, None])
    scores = jnp.einsum("thd,shd->hts", query, lookup_array, preferred_element_type=jnp.float32)
    fade = jnp.exp(jnp.minimum(level[:, :, None] - level[:, None, :], 0.0))
    weights = jnp.where(same[None], scores * fade, 0.0).astype(jnp.bfloat16)
    inner = jnp.einsum("hts,shd->thd", weights, values, preferred_element_type=jnp.float32)
    carried = docs == before
    closing = (docs == docs[-1]).astype(jnp.float32)
    tail = jnp.exp(level[:, -1:] - level) * closing[None, :]
    weighted = (lookup_array.astype(jnp.float32) * tail.T[:, :, None]).astype(jnp.bfloat16)
    state = jnp.einsum("shd,she->hde", weighted, values, preferred_element_type=jnp.float32)
    shrinkage_multiplier = jnp.exp(level[:, -1]) * carried[-1].astype(jnp.float32)
    return (inner, level, carried, shrinkage_multiplier, state)


def local(doc_lengths, lin_q, lin_k, lin_v, log_decay, out_gate, lin_gain, soft_q, soft_k, soft_v):
    rows = lin_q.shape[0]
    heads_here = lin_q.shape[1] // DH
    kv_here = soft_k.shape[1] // DH
    group = soft_q.shape[1] // (kv_here * DH)
    shard = lax.axis_index("ctx")
    positions = shard * rows + jnp.arange(rows, dtype=jnp.int32)
    docs = document_of(positions, doc_lengths)
    before = jnp.where(shard > 0, document_of(positions[:1] - 1, doc_lengths)[0], -1)
    query = lin_q.reshape(rows, heads_here, DH)
    lookup_array = lin_k.reshape(rows, heads_here, DH)
    values = lin_v.reshape(rows, heads_here, DH)
    inner, level, carried, shrinkage_multiplier, state = block_terms(
        query, lookup_array, values, log_decay, docs, before
    )
    count = lax.axis_size("ctx")
    odd = (shard % 2) == 1
    pair = jnp.concatenate(
        [soft_k.reshape(rows, kv_here, DH).transpose(1, 0, 2),
         soft_v.reshape(rows, kv_here, DH).transpose(1, 0, 2)],
        axis=0,
    ).reshape(-1, DH)
    n_pair = pair.shape[0]
    n_state = heads_here * DH
    state_rows = state.reshape(n_state, DH)
    factor_rows = jnp.pad(shrinkage_multiplier[None, :], ((0, 7), (0, DH - heads_here)))
    first = jnp.concatenate([state_rows, factor_rows, pair.astype(jnp.float32)], axis=0)
    got = lax.ppermute(first, "ctx", [(i, i ^ 1) for i in range(count)])
    state_mate = got[:n_state]
    factor_mate = got[n_state, :heads_here]
    pair_mate = got[n_state + 8 :].astype(jnp.bfloat16)
    state_cube = state_rows.reshape(state.shape)
    mate_cube = state_mate.reshape(state.shape)
    chip_state = jnp.where(
        odd,
        shrinkage_multiplier[:, None, None] * mate_cube + state_cube,
        factor_mate[:, None, None] * state_cube + mate_cube,
    )
    chip_factor = shrinkage_multiplier * factor_mate
    pair_lo = jnp.where(odd, pair_mate, pair)
    pair_hi = jnp.where(odd, pair, pair_mate)
    chip_top = chip_factor.astype(jnp.bfloat16)
    chip_rest = (chip_factor - chip_top.astype(jnp.float32)).astype(jnp.bfloat16)
    chip_rows = jnp.pad(jnp.stack([chip_top, chip_rest]), ((0, 14), (0, DH - heads_here)))
    packet = jnp.concatenate(
        [chip_state.astype(jnp.bfloat16).reshape(n_state, DH), chip_rows, pair_lo, pair_hi], axis=0
    )
    routes = [(i, i + 1) for i in range(1, count - 1, 2)] + [(i, i + 5) for i in range(0, count - 5, 2)]
    received = lax.ppermute(packet, "ctx", routes)
    mate_packet = lax.ppermute(received, "ctx", [(i, i ^ 1) for i in range(count)])
    near = jnp.where(odd, mate_packet, received)
    far = jnp.where(odd, received, mate_packet)

    def unpack(got_packet):
        chip = got_packet[:n_state].reshape(state.shape).astype(jnp.float32)
        mult = got_packet[n_state, :heads_here].astype(jnp.float32) + got_packet[
            n_state + 1, :heads_here
        ].astype(jnp.float32)
        low = got_packet[n_state + 16 : n_state + 16 + n_pair]
        high = got_packet[n_state + 16 + n_pair :]
        return chip, mult, low, high

    state_near, factor_near, near_lo, near_hi = unpack(near)
    state_far, _, far_lo, far_hi = unpack(far)
    incoming_even = state_near + factor_near[:, None, None] * state_far
    incoming = jnp.where(odd, factor_mate[:, None, None] * incoming_even + mate_cube, incoming_even)
    incoming_b = incoming.astype(jnp.bfloat16)
    window_even = jnp.concatenate([far_lo, far_hi, near_lo, near_hi], axis=0)
    window_odd = jnp.concatenate([far_hi, near_lo, near_hi, pair_mate], axis=0)
    window = jnp.concatenate([jnp.where(odd, window_odd, window_even), pair], axis=0)
    window = window.reshape(SPAN + 1, 2 * kv_here, rows, DH)
    outer = jnp.einsum(
        "thd,hde->the", query, incoming_b, preferred_element_type=jnp.float32
    )
    outer = outer * (jnp.exp(level).T * carried[:, None].astype(jnp.float32))[:, :, None]
    mixed = inner + outer
    local_sq = jnp.sum(mixed * mixed, axis=(1, 2))
    total_sq = all_sum(local_sq, "head")
    mean_sq = total_sq / (lax.axis_size("head") * heads_here * DH)
    flat = mixed.reshape(rows, heads_here * DH)
    normed = (
        flat
        * lax.rsqrt(mean_sq + 1e-06)[:, None]
        * lin_gain[None, :]
        * jax.nn.sigmoid(out_gate.astype(jnp.float32))
    )
    lin_out = normed.astype(jnp.bfloat16)
    span_rows = (SPAN + 1) * rows
    key_pos = shard * rows - SPAN * rows + jnp.arange(span_rows, dtype=jnp.int32)
    key_docs = jnp.where(key_pos >= 0, document_of(key_pos, doc_lengths), -1)
    allowed = (key_docs[None, :] == docs[:, None]) & (key_pos[None, :] <= positions[:, None])
    soft_query = soft_q.reshape(rows, kv_here, group, DH)
    scores = jnp.einsum(
        "tkgd,bksd->kgtbs", soft_query, window[:, :kv_here], preferred_element_type=jnp.float32
    ).reshape(kv_here, group, rows, span_rows) * DH ** (-0.5)
    top = jnp.max(jnp.where(allowed, scores, -1e30), axis=-1, keepdims=True)
    expd = jnp.where(allowed, jnp.exp(jnp.minimum(scores - top, 0.0)), 0.0)
    total = jnp.sum(expd, axis=-1)
    attended = jnp.einsum(
        "kgtbs,bksd->tkgd",
        expd.astype(jnp.bfloat16).reshape(kv_here, group, rows, SPAN + 1, rows),
        window[:, kv_here:],
        preferred_element_type=jnp.float32,
    )
    attended = attended / total.transpose(2, 0, 1)[..., None]
    soft_out = attended.reshape(rows, kv_here * group * DH).astype(jnp.bfloat16)
    return (lin_out, soft_out)


def solution(mesh):
    in_specs = (
        P(),
        P("ctx", "head"),
        P("ctx", "head"),
        P("ctx", "head"),
        P("head", "ctx"),
        P("ctx", "head"),
        P("head"),
        P("ctx", "head"),
        P("ctx", "head"),
        P("ctx", "head"),
    )
    out_specs = (P("ctx", "head"), P("ctx", "head"))
    return jax.shard_map(local, mesh=mesh, in_specs=in_specs, out_specs=out_specs, check_vma=False)
```

```python
import jax
import jax.numpy as jnp
from jax import lax
from jax.sharding import PartitionSpec as P

DH = 128
SPAN = 4


def from_behind(shard, axis, by):
    count = lax.axis_size(axis)
    pairs = [(i, i + by) for i in range(count) if 0 <= i + by < count]
    return lax.ppermute(shard, axis, pairs)


def all_sum(x, axis):
    count = lax.axis_size(axis)
    if count & (count - 1):
        me = lax.axis_index(axis)
        parts = [x]
        for by in range(1, count):
            parts.append(lax.ppermute(x, axis, [(i, (i + by) % count) for i in range(count)]))
        stacked = jnp.stack(parts)
        order = (me - jnp.arange(count)) % count
        return jnp.sum(stacked[order], axis=0)
    bit = 1
    while bit < count:
        x = x + lax.ppermute(x, axis, [(i, i ^ bit) for i in range(count)])
        bit *= 2
    return x


def document_of(positions, doc_lengths):
    ends = jnp.cumsum(doc_lengths)
    return jnp.sum((ends[None, :] <= positions[:, None]).astype(jnp.int32), axis=1)


def block_terms(query, lookup_array, values, decay, docs, before):
    rows = docs.shape[0]
    level = jnp.cumsum(decay, axis=1)
    order = jnp.arange(rows)
    same = (docs[:, None] == docs[None, :]) & (order[None, :] <= order[:, None])
    scores = jnp.einsum("thd,shd->hts", query, lookup_array, preferred_element_type=jnp.float32)
    fade = jnp.exp(jnp.minimum(level[:, :, None] - level[:, None, :], 0.0))
    weights = jnp.where(same[None], scores * fade, 0.0).astype(jnp.bfloat16)
    inner = jnp.einsum("hts,shd->thd", weights, values, preferred_element_type=jnp.float32)
    carried = docs == before
    closing = (docs == docs[-1]).astype(jnp.float32)
    tail = jnp.exp(level[:, -1:] - level) * closing[None, :]
    weighted = (lookup_array.astype(jnp.float32) * tail.T[:, :, None]).astype(jnp.bfloat16)
    state = jnp.einsum("shd,she->hde", weighted, values, preferred_element_type=jnp.float32)
    shrinkage_multiplier = jnp.exp(level[:, -1]) * carried[-1].astype(jnp.float32)
    return (inner, level, carried, shrinkage_multiplier, state)


def local(doc_lengths, lin_q, lin_k, lin_v, log_decay, out_gate, lin_gain, soft_q, soft_k, soft_v):
    rows = lin_q.shape[0]
    heads_here = lin_q.shape[1] // DH
    kv_here = soft_k.shape[1] // DH
    group = soft_q.shape[1] // (kv_here * DH)
    shard = lax.axis_index("ctx")
    positions = shard * rows + jnp.arange(rows, dtype=jnp.int32)
    docs = document_of(positions, doc_lengths)
    before = jnp.where(shard > 0, document_of(positions[:1] - 1, doc_lengths)[0], -1)
    query = lin_q.reshape(rows, heads_here, DH)
    lookup_array = lin_k.reshape(rows, heads_here, DH)
    values = lin_v.reshape(rows, heads_here, DH)
    inner, level, carried, shrinkage_multiplier, state = block_terms(
        query, lookup_array, values, log_decay, docs, before
    )
    count = lax.axis_size("ctx")
    odd = (shard % 2) == 1
    pair = jnp.concatenate(
        [soft_k.reshape(rows, kv_here, DH).transpose(1, 0, 2),
         soft_v.reshape(rows, kv_here, DH).transpose(1, 0, 2)],
        axis=0,
    ).reshape(-1, DH)
    n_pair = pair.shape[0]
    n_state = heads_here * DH
    state_rows = state.reshape(n_state, DH)
    factor_rows = jnp.pad(shrinkage_multiplier[None, :], ((0, 7), (0, DH - heads_here)))
    first = jnp.concatenate([state_rows, factor_rows, pair.astype(jnp.float32)], axis=0)
    got = lax.ppermute(first, "ctx", [(i, i ^ 1) for i in range(count)])
    state_mate = got[:n_state]
    factor_mate = got[n_state, :heads_here]
    pair_mate = got[n_state + 8 :].astype(jnp.bfloat16)
    state_cube = state_rows.reshape(state.shape)
    mate_cube = state_mate.reshape(state.shape)
    chip_state = jnp.where(
        odd,
        shrinkage_multiplier[:, None, None] * mate_cube + state_cube,
        factor_mate[:, None, None] * state_cube + mate_cube,
    )
    chip_factor = shrinkage_multiplier * factor_mate
    pair_lo = jnp.where(odd, pair_mate, pair)
    pair_hi = jnp.where(odd, pair, pair_mate)
    chip_top = chip_factor.astype(jnp.bfloat16)
    chip_rest = (chip_factor - chip_top.astype(jnp.float32)).astype(jnp.bfloat16)
    chip_rows = jnp.pad(jnp.stack([chip_top, chip_rest]), ((0, 14), (0, DH - heads_here)))
    packet = jnp.concatenate(
        [chip_state.astype(jnp.bfloat16).reshape(n_state, DH), chip_rows, pair_lo, pair_hi], axis=0
    )
    routes = [(i, i + 1) for i in range(1, count - 1, 2)] + [(i, i + 5) for i in range(0, count - 5, 2)]
    received = lax.ppermute(packet, "ctx", routes)
    mate_packet = lax.ppermute(received, "ctx", [(i, i ^ 1) for i in range(count)])
    near = jnp.where(odd, mate_packet, received)
    far = jnp.where(odd, received, mate_packet)

    def unpack(got_packet):
        chip = got_packet[:n_state].reshape(state.shape).astype(jnp.float32)
        mult = got_packet[n_state, :heads_here].astype(jnp.float32) + got_packet[
            n_state + 1, :heads_here
        ].astype(jnp.float32)
        low = got_packet[n_state + 16 : n_state + 16 + n_pair]
        high = got_packet[n_state + 16 + n_pair :]
        return chip, mult, low, high

    state_near, factor_near, near_lo, near_hi = unpack(near)
    state_far, _, far_lo, far_hi = unpack(far)
    incoming_even = state_near + factor_near[:, None, None] * state_far
    incoming = jnp.where(odd, factor_mate[:, None, None] * incoming_even + mate_cube, incoming_even)
    incoming_b = incoming.astype(jnp.bfloat16)
    window_even = jnp.concatenate([far_lo, far_hi, near_lo, near_hi], axis=0)
    window_odd = jnp.concatenate([far_hi, near_lo, near_hi, pair_mate], axis=0)
    window = jnp.concatenate([jnp.where(odd, window_odd, window_even), pair], axis=0)
    window = window.reshape(SPAN + 1, 2 * kv_here, rows, DH)
    outer = jnp.einsum(
        "thd,hde->the", query, incoming_b, preferred_element_type=jnp.float32
    )
    outer = outer * (jnp.exp(level).T * carried[:, None].astype(jnp.float32))[:, :, None]
    mixed = inner + outer
    local_sq = jnp.sum(mixed * mixed, axis=(1, 2))
    total_sq = all_sum(local_sq, "head")
    mean_sq = total_sq / (lax.axis_size("head") * heads_here * DH)
    flat = mixed.reshape(rows, heads_here * DH)
    normed = (
        flat
        * lax.rsqrt(mean_sq + 1e-06)[:, None]
        * lin_gain[None, :]
        * jax.nn.sigmoid(out_gate.astype(jnp.float32))
    )
    lin_out = normed.astype(jnp.bfloat16)
    span_rows = (SPAN + 1) * rows
    key_pos = shard * rows - SPAN * rows + jnp.arange(span_rows, dtype=jnp.int32)
    key_docs = jnp.where(key_pos >= 0, document_of(key_pos, doc_lengths), -1)
    allowed = (key_docs[None, :] == docs[:, None]) & (key_pos[None, :] <= positions[:, None])
    soft_query = soft_q.reshape(rows, kv_here, group, DH)
    scores = jnp.einsum(
        "tkgd,bksd->kgtbs", soft_query, window[:, :kv_here], preferred_element_type=jnp.float32
    ).reshape(kv_here, group, rows, span_rows) * DH ** (-0.5)
    top = jnp.max(jnp.where(allowed, scores, -1e30), axis=-1, keepdims=True)
    expd = jnp.where(allowed, jnp.exp(jnp.minimum(scores - top, 0.0)), 0.0)
    total = jnp.sum(expd, axis=-1)
    attended = jnp.einsum(
        "kgtbs,bksd->tkgd",
        expd.astype(jnp.bfloat16).reshape(kv_here, group, rows, SPAN + 1, rows),
        window[:, kv_here:],
        preferred_element_type=jnp.float32,
    )
    attended = attended / total.transpose(2, 0, 1)[..., None]
    soft_out = attended.reshape(rows, kv_here * group * DH).astype(jnp.bfloat16)
    return (lin_out, soft_out)


def solution(mesh):
    in_specs = (
        P(),
        P("ctx", "head"),
        P("ctx", "head"),
        P("ctx", "head"),
        P("head", "ctx"),
        P("ctx", "head"),
        P("head"),
        P("ctx", "head"),
        P("ctx", "head"),
        P("ctx", "head"),
    )
    out_specs = (P("ctx", "head"), P("ctx", "head"))
    return jax.shard_map(local, mesh=mesh, in_specs=in_specs, out_specs=out_specs, check_vma=False)
```

```python
import jax
import jax.numpy as jnp
from jax import lax
from jax.sharding import PartitionSpec as P

DH = 128
SPAN = 4


def from_behind(shard, axis, by):
    count = lax.axis_size(axis)
    pairs = [(i, i + by) for i in range(count) if 0 <= i + by < count]
    return lax.ppermute(shard, axis, pairs)


def all_sum(x, axis):
    count = lax.axis_size(axis)
    if count & (count - 1):
        me = lax.axis_index(axis)
        parts = [x]
        for by in range(1, count):
            parts.append(lax.ppermute(x, axis, [(i, (i + by) % count) for i in range(count)]))
        stacked = jnp.stack(parts)
        order = (me - jnp.arange(count)) % count
        return jnp.sum(stacked[order], axis=0)
    bit = 1
    while bit < count:
        x = x + lax.ppermute(x, axis, [(i, i ^ bit) for i in range(count)])
        bit *= 2
    return x


def document_of(positions, doc_lengths):
    ends = jnp.cumsum(doc_lengths)
    return jnp.sum((ends[None, :] <= positions[:, None]).astype(jnp.int32), axis=1)


def block_terms(query, lookup_array, values, decay, docs, before):
    rows = docs.shape[0]
    level = jnp.cumsum(decay, axis=1)
    order = jnp.arange(rows)
    same = (docs[:, None] == docs[None, :]) & (order[None, :] <= order[:, None])
    scores = jnp.einsum("thd,shd->hts", query, lookup_array, preferred_element_type=jnp.float32)
    fade = jnp.exp(jnp.minimum(level[:, :, None] - level[:, None, :], 0.0))
    weights = jnp.where(same[None], scores * fade, 0.0).astype(jnp.bfloat16)
    inner = jnp.einsum("hts,shd->thd", weights, values, preferred_element_type=jnp.float32)
    carried = docs == before
    closing = (docs == docs[-1]).astype(jnp.float32)
    tail = jnp.exp(level[:, -1:] - level) * closing[None, :]
    weighted = (lookup_array.astype(jnp.float32) * tail.T[:, :, None]).astype(jnp.bfloat16)
    state = jnp.einsum("shd,she->hde", weighted, values, preferred_element_type=jnp.float32)
    shrinkage_multiplier = jnp.exp(level[:, -1]) * carried[-1].astype(jnp.float32)
    return (inner, level, carried, shrinkage_multiplier, state)


def local(doc_lengths, lin_q, lin_k, lin_v, log_decay, out_gate, lin_gain, soft_q, soft_k, soft_v):
    rows = lin_q.shape[0]
    heads_here = lin_q.shape[1] // DH
    kv_here = soft_k.shape[1] // DH
    group = soft_q.shape[1] // (kv_here * DH)
    shard = lax.axis_index("ctx")
    positions = shard * rows + jnp.arange(rows, dtype=jnp.int32)
    docs = document_of(positions, doc_lengths)
    before = jnp.where(shard > 0, document_of(positions[:1] - 1, doc_lengths)[0], -1)
    query = lin_q.reshape(rows, heads_here, DH)
    lookup_array = lin_k.reshape(rows, heads_here, DH)
    values = lin_v.reshape(rows, heads_here, DH)
    inner, level, carried, shrinkage_multiplier, state = block_terms(
        query, lookup_array, values, log_decay, docs, before
    )
    count = lax.axis_size("ctx")
    odd = (shard % 2) == 1
    pair = jnp.concatenate(
        [soft_k.reshape(rows, kv_here, DH).transpose(1, 0, 2),
         soft_v.reshape(rows, kv_here, DH).transpose(1, 0, 2)],
        axis=0,
    ).reshape(-1, DH)
    n_pair = pair.shape[0]
    n_state = heads_here * DH
    state_rows = state.reshape(n_state, DH)
    factor_rows = jnp.pad(shrinkage_multiplier[None, :], ((0, 7), (0, DH - heads_here)))
    window = jnp.concatenate(
        [from_behind(pair, "ctx", step) for step in range(SPAN, 0, -1)] + [pair], axis=0
    ).reshape(SPAN + 1, 2 * kv_here, rows, DH)
    first = jnp.concatenate([state_rows, factor_rows], axis=0)
    got = lax.ppermute(first, "ctx", [(i, i ^ 1) for i in range(count)])
    state_mate = got[:n_state]
    factor_mate = got[n_state, :heads_here]
    state_cube = state_rows.reshape(state.shape)
    mate_cube = state_mate.reshape(state.shape)
    chip_state = jnp.where(
        odd,
        shrinkage_multiplier[:, None, None] * mate_cube + state_cube,
        factor_mate[:, None, None] * state_cube + mate_cube,
    )
    chip_factor = shrinkage_multiplier * factor_mate
    chip_top = chip_factor.astype(jnp.bfloat16)
    chip_rest = (chip_factor - chip_top.astype(jnp.float32)).astype(jnp.bfloat16)
    chip_rows = jnp.pad(jnp.stack([chip_top, chip_rest]), ((0, 14), (0, DH - heads_here)))
    packet = jnp.concatenate(
        [chip_state.astype(jnp.bfloat16).reshape(n_state, DH), chip_rows], axis=0
    )
    routes = [(i, i + 1) for i in range(1, count - 1, 2)] + [(i, i + 5) for i in range(0, count - 5, 2)]
    received = lax.ppermute(packet, "ctx", routes)
    mate_packet = lax.ppermute(received, "ctx", [(i, i ^ 1) for i in range(count)])
    near = jnp.where(odd, mate_packet, received)
    far = jnp.where(odd, received, mate_packet)

    def unpack(got_packet):
        chip = got_packet[:n_state].reshape(state.shape).astype(jnp.float32)
        mult = got_packet[n_state, :heads_here].astype(jnp.float32) + got_packet[
            n_state + 1, :heads_here
        ].astype(jnp.float32)
        return chip, mult

    state_near, factor_near = unpack(near)
    state_far, _ = unpack(far)
    incoming_even = state_near + factor_near[:, None, None] * state_far
    incoming = jnp.where(odd, factor_mate[:, None, None] * incoming_even + mate_cube, incoming_even)
    incoming_b = incoming.astype(jnp.bfloat16)
    outer = jnp.einsum(
        "thd,hde->the", query, incoming_b, preferred_element_type=jnp.float32
    )
    outer = outer * (jnp.exp(level).T * carried[:, None].astype(jnp.float32))[:, :, None]
    mixed = inner + outer
    local_sq = jnp.sum(mixed * mixed, axis=(1, 2))
    total_sq = all_sum(local_sq, "head")
    mean_sq = total_sq / (lax.axis_size("head") * heads_here * DH)
    flat = mixed.reshape(rows, heads_here * DH)
    normed = (
        flat
        * lax.rsqrt(mean_sq + 1e-06)[:, None]
        * lin_gain[None, :]
        * jax.nn.sigmoid(out_gate.astype(jnp.float32))
    )
    lin_out = normed.astype(jnp.bfloat16)
    span_rows = (SPAN + 1) * rows
    key_pos = shard * rows - SPAN * rows + jnp.arange(span_rows, dtype=jnp.int32)
    key_docs = jnp.where(key_pos >= 0, document_of(key_pos, doc_lengths), -1)
    allowed = (key_docs[None, :] == docs[:, None]) & (key_pos[None, :] <= positions[:, None])
    soft_query = soft_q.reshape(rows, kv_here, group, DH)
    scores = jnp.einsum(
        "tkgd,bksd->kgtbs", soft_query, window[:, :kv_here], preferred_element_type=jnp.float32
    ).reshape(kv_here, group, rows, span_rows) * DH ** (-0.5)
    top = jnp.max(jnp.where(allowed, scores, -1e30), axis=-1, keepdims=True)
    expd = jnp.where(allowed, jnp.exp(jnp.minimum(scores - top, 0.0)), 0.0)
    total = jnp.sum(expd, axis=-1)
    attended = jnp.einsum(
        "kgtbs,bksd->tkgd",
        expd.astype(jnp.bfloat16).reshape(kv_here, group, rows, SPAN + 1, rows),
        window[:, kv_here:],
        preferred_element_type=jnp.float32,
    )
    attended = attended / total.transpose(2, 0, 1)[..., None]
    soft_out = attended.reshape(rows, kv_here * group * DH).astype(jnp.bfloat16)
    return (lin_out, soft_out)


def solution(mesh):
    in_specs = (
        P(),
        P("ctx", "head"),
        P("ctx", "head"),
        P("ctx", "head"),
        P("head", "ctx"),
        P("ctx", "head"),
        P("head"),
        P("ctx", "head"),
        P("ctx", "head"),
        P("ctx", "head"),
    )
    out_specs = (P("ctx", "head"), P("ctx", "head"))
    return jax.shard_map(local, mesh=mesh, in_specs=in_specs, out_specs=out_specs, check_vma=False)
```

```python
import jax
import jax.numpy as jnp
from jax import lax
from jax.sharding import PartitionSpec as P

DH = 128
SPAN = 4


def from_behind(shard, axis, by):
    count = lax.axis_size(axis)
    pairs = [(i, i + by) for i in range(count) if 0 <= i + by < count]
    return lax.ppermute(shard, axis, pairs)


def all_sum(x, axis):
    count = lax.axis_size(axis)
    if count & (count - 1):
        me = lax.axis_index(axis)
        parts = [x]
        for by in range(1, count):
            parts.append(lax.ppermute(x, axis, [(i, (i + by) % count) for i in range(count)]))
        stacked = jnp.stack(parts)
        order = (me - jnp.arange(count)) % count
        return jnp.sum(stacked[order], axis=0)
    bit = 1
    while bit < count:
        x = x + lax.ppermute(x, axis, [(i, i ^ bit) for i in range(count)])
        bit *= 2
    return x


def document_of(positions, doc_lengths):
    ends = jnp.cumsum(doc_lengths)
    return jnp.sum((ends[None, :] <= positions[:, None]).astype(jnp.int32), axis=1)


def block_terms(query, lookup_array, values, decay, docs, before):
    rows = docs.shape[0]
    level = jnp.cumsum(decay, axis=1)
    order = jnp.arange(rows)
    same = (docs[:, None] == docs[None, :]) & (order[None, :] <= order[:, None])
    scores = jnp.einsum("thd,shd->hts", query, lookup_array, preferred_element_type=jnp.float32)
    fade = jnp.exp(jnp.minimum(level[:, :, None] - level[:, None, :], 0.0))
    weights = jnp.where(same[None], scores * fade, 0.0).astype(jnp.bfloat16)
    inner = jnp.einsum("hts,shd->thd", weights, values, preferred_element_type=jnp.float32)
    carried = docs == before
    closing = (docs == docs[-1]).astype(jnp.float32)
    tail = jnp.exp(level[:, -1:] - level) * closing[None, :]
    weighted = (lookup_array.astype(jnp.float32) * tail.T[:, :, None]).astype(jnp.bfloat16)
    state = jnp.einsum("shd,she->hde", weighted, values, preferred_element_type=jnp.float32)
    shrinkage_multiplier = jnp.exp(level[:, -1]) * carried[-1].astype(jnp.float32)
    return (inner, level, carried, shrinkage_multiplier, state)


def local(doc_lengths, lin_q, lin_k, lin_v, log_decay, out_gate, lin_gain, soft_q, soft_k, soft_v):
    rows = lin_q.shape[0]
    heads_here = lin_q.shape[1] // DH
    kv_here = soft_k.shape[1] // DH
    group = soft_q.shape[1] // (kv_here * DH)
    shard = lax.axis_index("ctx")
    positions = shard * rows + jnp.arange(rows, dtype=jnp.int32)
    docs = document_of(positions, doc_lengths)
    before = jnp.where(shard > 0, document_of(positions[:1] - 1, doc_lengths)[0], -1)
    query = lin_q.reshape(rows, heads_here, DH)
    lookup_array = lin_k.reshape(rows, heads_here, DH)
    values = lin_v.reshape(rows, heads_here, DH)
    inner, level, carried, shrinkage_multiplier, state = block_terms(
        query, lookup_array, values, log_decay, docs, before
    )
    count = lax.axis_size("ctx")
    odd = (shard % 2) == 1
    pair = jnp.concatenate(
        [soft_k.reshape(rows, kv_here, DH).transpose(1, 0, 2),
         soft_v.reshape(rows, kv_here, DH).transpose(1, 0, 2)],
        axis=0,
    ).reshape(-1, DH)
    n_pair = pair.shape[0]
    n_state = heads_here * DH
    state_rows = state.reshape(n_state, DH)
    factor_rows = jnp.pad(shrinkage_multiplier[None, :], ((0, 7), (0, DH - heads_here)))
    first = jnp.concatenate([state_rows, factor_rows], axis=0)
    got = lax.ppermute(first, "ctx", [(i, i ^ 1) for i in range(count)])
    state_mate = got[:n_state]
    factor_mate = got[n_state, :heads_here]
    state_cube = state_rows.reshape(state.shape)
    mate_cube = state_mate.reshape(state.shape)
    chip_state = jnp.where(
        odd,
        shrinkage_multiplier[:, None, None] * mate_cube + state_cube,
        factor_mate[:, None, None] * state_cube + mate_cube,
    )
    chip_factor = shrinkage_multiplier * factor_mate
    chip_top = chip_factor.astype(jnp.bfloat16)
    chip_rest = (chip_factor - chip_top.astype(jnp.float32)).astype(jnp.bfloat16)
    chip_rows = jnp.pad(jnp.stack([chip_top, chip_rest]), ((0, 14), (0, DH - heads_here)))
    packet = jnp.concatenate(
        [chip_state.astype(jnp.bfloat16).reshape(n_state, DH), chip_rows], axis=0
    )
    routes = [(i, i + 1) for i in range(1, count - 1, 2)] + [(i, i + 5) for i in range(0, count - 5, 2)]
    received = lax.ppermute(packet, "ctx", routes)
    pair_late, received = lax.optimization_barrier((pair, received))
    mate_packet = lax.ppermute(received, "ctx", [(i, i ^ 1) for i in range(count)])
    window = jnp.concatenate(
        [from_behind(pair_late, "ctx", step) for step in range(SPAN, 0, -1)] + [pair], axis=0
    ).reshape(SPAN + 1, 2 * kv_here, rows, DH)
    near = jnp.where(odd, mate_packet, received)
    far = jnp.where(odd, received, mate_packet)

    def unpack(got_packet):
        chip = got_packet[:n_state].reshape(state.shape).astype(jnp.float32)
        mult = got_packet[n_state, :heads_here].astype(jnp.float32) + got_packet[
            n_state + 1, :heads_here
        ].astype(jnp.float32)
        return chip, mult

    state_near, factor_near = unpack(near)
    state_far, _ = unpack(far)
    incoming_even = state_near + factor_near[:, None, None] * state_far
    incoming = jnp.where(odd, factor_mate[:, None, None] * incoming_even + mate_cube, incoming_even)
    incoming_b = incoming.astype(jnp.bfloat16)
    outer = jnp.einsum(
        "thd,hde->the", query, incoming_b, preferred_element_type=jnp.float32
    )
    outer = outer * (jnp.exp(level).T * carried[:, None].astype(jnp.float32))[:, :, None]
    mixed = inner + outer
    local_sq = jnp.sum(mixed * mixed, axis=(1, 2))
    total_sq = all_sum(local_sq, "head")
    mean_sq = total_sq / (lax.axis_size("head") * heads_here * DH)
    flat = mixed.reshape(rows, heads_here * DH)
    normed = (
        flat
        * lax.rsqrt(mean_sq + 1e-06)[:, None]
        * lin_gain[None, :]
        * jax.nn.sigmoid(out_gate.astype(jnp.float32))
    )
    lin_out = normed.astype(jnp.bfloat16)
    span_rows = (SPAN + 1) * rows
    key_pos = shard * rows - SPAN * rows + jnp.arange(span_rows, dtype=jnp.int32)
    key_docs = jnp.where(key_pos >= 0, document_of(key_pos, doc_lengths), -1)
    allowed = (key_docs[None, :] == docs[:, None]) & (key_pos[None, :] <= positions[:, None])
    soft_query = soft_q.reshape(rows, kv_here, group, DH)
    scores = jnp.einsum(
        "tkgd,bksd->kgtbs", soft_query, window[:, :kv_here], preferred_element_type=jnp.float32
    ).reshape(kv_here, group, rows, span_rows) * DH ** (-0.5)
    top = jnp.max(jnp.where(allowed, scores, -1e30), axis=-1, keepdims=True)
    expd = jnp.where(allowed, jnp.exp(jnp.minimum(scores - top, 0.0)), 0.0)
    total = jnp.sum(expd, axis=-1)
    attended = jnp.einsum(
        "kgtbs,bksd->tkgd",
        expd.astype(jnp.bfloat16).reshape(kv_here, group, rows, SPAN + 1, rows),
        window[:, kv_here:],
        preferred_element_type=jnp.float32,
    )
    attended = attended / total.transpose(2, 0, 1)[..., None]
    soft_out = attended.reshape(rows, kv_here * group * DH).astype(jnp.bfloat16)
    return (lin_out, soft_out)


def solution(mesh):
    in_specs = (
        P(),
        P("ctx", "head"),
        P("ctx", "head"),
        P("ctx", "head"),
        P("head", "ctx"),
        P("ctx", "head"),
        P("head"),
        P("ctx", "head"),
        P("ctx", "head"),
        P("ctx", "head"),
    )
    out_specs = (P("ctx", "head"), P("ctx", "head"))
    return jax.shard_map(local, mesh=mesh, in_specs=in_specs, out_specs=out_specs, check_vma=False)
```

```python
import jax
import jax.numpy as jnp
from jax import lax
from jax.sharding import PartitionSpec as P

DH = 128
SPAN = 4


def from_behind(shard, axis, by):
    count = lax.axis_size(axis)
    pairs = [(i, i + by) for i in range(count) if 0 <= i + by < count]
    return lax.ppermute(shard, axis, pairs)


def all_sum(x, axis):
    count = lax.axis_size(axis)
    if count & (count - 1):
        me = lax.axis_index(axis)
        parts = [x]
        for by in range(1, count):
            parts.append(lax.ppermute(x, axis, [(i, (i + by) % count) for i in range(count)]))
        stacked = jnp.stack(parts)
        order = (me - jnp.arange(count)) % count
        return jnp.sum(stacked[order], axis=0)
    bit = 1
    while bit < count:
        x = x + lax.ppermute(x, axis, [(i, i ^ bit) for i in range(count)])
        bit *= 2
    return x


def document_of(positions, doc_lengths):
    ends = jnp.cumsum(doc_lengths)
    return jnp.sum((ends[None, :] <= positions[:, None]).astype(jnp.int32), axis=1)


def block_terms(query, lookup_array, values, decay, docs, before):
    rows = docs.shape[0]
    level = jnp.cumsum(decay, axis=1)
    order = jnp.arange(rows)
    same = (docs[:, None] == docs[None, :]) & (order[None, :] <= order[:, None])
    scores = jnp.einsum("thd,shd->hts", query, lookup_array, preferred_element_type=jnp.float32)
    fade = jnp.exp(jnp.minimum(level[:, :, None] - level[:, None, :], 0.0))
    weights = jnp.where(same[None], scores * fade, 0.0).astype(jnp.bfloat16)
    inner = jnp.einsum("hts,shd->thd", weights, values, preferred_element_type=jnp.float32)
    carried = docs == before
    closing = (docs == docs[-1]).astype(jnp.float32)
    tail = jnp.exp(level[:, -1:] - level) * closing[None, :]
    weighted = (lookup_array.astype(jnp.float32) * tail.T[:, :, None]).astype(jnp.bfloat16)
    state = jnp.einsum("shd,she->hde", weighted, values, preferred_element_type=jnp.float32)
    shrinkage_multiplier = jnp.exp(level[:, -1]) * carried[-1].astype(jnp.float32)
    return (inner, level, carried, shrinkage_multiplier, state)


def local(doc_lengths, lin_q, lin_k, lin_v, log_decay, out_gate, lin_gain, soft_q, soft_k, soft_v):
    rows = lin_q.shape[0]
    heads_here = lin_q.shape[1] // DH
    kv_here = soft_k.shape[1] // DH
    group = soft_q.shape[1] // (kv_here * DH)
    shard = lax.axis_index("ctx")
    positions = shard * rows + jnp.arange(rows, dtype=jnp.int32)
    docs = document_of(positions, doc_lengths)
    before = jnp.where(shard > 0, document_of(positions[:1] - 1, doc_lengths)[0], -1)
    query = lin_q.reshape(rows, heads_here, DH)
    lookup_array = lin_k.reshape(rows, heads_here, DH)
    values = lin_v.reshape(rows, heads_here, DH)
    inner, level, carried, shrinkage_multiplier, state = block_terms(
        query, lookup_array, values, log_decay, docs, before
    )
    count = lax.axis_size("ctx")
    odd = (shard % 2) == 1
    pair = jnp.concatenate(
        [soft_k.reshape(rows, kv_here, DH).transpose(1, 0, 2),
         soft_v.reshape(rows, kv_here, DH).transpose(1, 0, 2)],
        axis=0,
    ).reshape(-1, DH)
    n_pair = pair.shape[0]
    n_state = heads_here * DH
    state_rows = state.reshape(n_state, DH)
    factor_rows = jnp.pad(shrinkage_multiplier[None, :], ((0, 7), (0, DH - heads_here)))
    swap = [(i, i ^ 1) for i in range(count)]
    routes = [(i, i + 1) for i in range(1, count - 1, 2)] + [(i, i + 5) for i in range(0, count - 5, 2)]
    pair_mate = lax.ppermute(pair, "ctx", swap)
    chip_pair = jnp.concatenate(
        [jnp.where(odd, pair_mate, pair), jnp.where(odd, pair, pair_mate)], axis=0
    )
    pairs_got = lax.ppermute(chip_pair, "ctx", routes)
    pairs_other = lax.ppermute(pairs_got, "ctx", swap)
    pairs_near = jnp.where(odd, pairs_other, pairs_got)
    pairs_far = jnp.where(odd, pairs_got, pairs_other)
    window_even = jnp.concatenate([pairs_far, pairs_near], axis=0)
    window_odd = jnp.concatenate([pairs_far[n_pair:], pairs_near, pair_mate], axis=0)
    window = jnp.concatenate([jnp.where(odd, window_odd, window_even), pair], axis=0)
    window = window.reshape(SPAN + 1, 2 * kv_here, rows, DH)
    first = jnp.concatenate([state_rows, factor_rows], axis=0)
    got = lax.ppermute(first, "ctx", swap)
    state_mate = got[:n_state]
    factor_mate = got[n_state, :heads_here]
    state_cube = state_rows.reshape(state.shape)
    mate_cube = state_mate.reshape(state.shape)
    chip_state = jnp.where(
        odd,
        shrinkage_multiplier[:, None, None] * mate_cube + state_cube,
        factor_mate[:, None, None] * state_cube + mate_cube,
    )
    chip_factor = shrinkage_multiplier * factor_mate
    chip_top = chip_factor.astype(jnp.bfloat16)
    chip_rest = (chip_factor - chip_top.astype(jnp.float32)).astype(jnp.bfloat16)
    chip_rows = jnp.pad(jnp.stack([chip_top, chip_rest]), ((0, 14), (0, DH - heads_here)))
    packet = jnp.concatenate(
        [chip_state.astype(jnp.bfloat16).reshape(n_state, DH), chip_rows], axis=0
    )
    received = lax.ppermute(packet, "ctx", routes)
    mate_packet = lax.ppermute(received, "ctx", swap)
    near = jnp.where(odd, mate_packet, received)
    far = jnp.where(odd, received, mate_packet)

    def unpack(got_packet):
        chip = got_packet[:n_state].reshape(state.shape).astype(jnp.float32)
        mult = got_packet[n_state, :heads_here].astype(jnp.float32) + got_packet[
            n_state + 1, :heads_here
        ].astype(jnp.float32)
        return chip, mult

    state_near, factor_near = unpack(near)
    state_far, _ = unpack(far)
    incoming_even = state_near + factor_near[:, None, None] * state_far
    incoming = jnp.where(odd, factor_mate[:, None, None] * incoming_even + mate_cube, incoming_even)
    incoming_b = incoming.astype(jnp.bfloat16)
    outer = jnp.einsum(
        "thd,hde->the", query, incoming_b, preferred_element_type=jnp.float32
    )
    outer = outer * (jnp.exp(level).T * carried[:, None].astype(jnp.float32))[:, :, None]
    mixed = inner + outer
    local_sq = jnp.sum(mixed * mixed, axis=(1, 2))
    total_sq = all_sum(local_sq, "head")
    mean_sq = total_sq / (lax.axis_size("head") * heads_here * DH)
    flat = mixed.reshape(rows, heads_here * DH)
    normed = (
        flat
        * lax.rsqrt(mean_sq + 1e-06)[:, None]
        * lin_gain[None, :]
        * jax.nn.sigmoid(out_gate.astype(jnp.float32))
    )
    lin_out = normed.astype(jnp.bfloat16)
    span_rows = (SPAN + 1) * rows
    key_pos = shard * rows - SPAN * rows + jnp.arange(span_rows, dtype=jnp.int32)
    key_docs = jnp.where(key_pos >= 0, document_of(key_pos, doc_lengths), -1)
    allowed = (key_docs[None, :] == docs[:, None]) & (key_pos[None, :] <= positions[:, None])
    soft_query = soft_q.reshape(rows, kv_here, group, DH)
    scores = jnp.einsum(
        "tkgd,bksd->kgtbs", soft_query, window[:, :kv_here], preferred_element_type=jnp.float32
    ).reshape(kv_here, group, rows, span_rows) * DH ** (-0.5)
    top = jnp.max(jnp.where(allowed, scores, -1e30), axis=-1, keepdims=True)
    expd = jnp.where(allowed, jnp.exp(jnp.minimum(scores - top, 0.0)), 0.0)
    total = jnp.sum(expd, axis=-1)
    attended = jnp.einsum(
        "kgtbs,bksd->tkgd",
        expd.astype(jnp.bfloat16).reshape(kv_here, group, rows, SPAN + 1, rows),
        window[:, kv_here:],
        preferred_element_type=jnp.float32,
    )
    attended = attended / total.transpose(2, 0, 1)[..., None]
    soft_out = attended.reshape(rows, kv_here * group * DH).astype(jnp.bfloat16)
    return (lin_out, soft_out)


def solution(mesh):
    in_specs = (
        P(),
        P("ctx", "head"),
        P("ctx", "head"),
        P("ctx", "head"),
        P("head", "ctx"),
        P("ctx", "head"),
        P("head"),
        P("ctx", "head"),
        P("ctx", "head"),
        P("ctx", "head"),
    )
    out_specs = (P("ctx", "head"), P("ctx", "head"))
    return jax.shard_map(local, mesh=mesh, in_specs=in_specs, out_specs=out_specs, check_vma=False)
```

```python
import jax
import jax.numpy as jnp
from jax import lax
from jax.sharding import PartitionSpec as P

DH = 128
SPAN = 4


def from_behind(shard, axis, by):
    count = lax.axis_size(axis)
    pairs = [(i, i + by) for i in range(count) if 0 <= i + by < count]
    return lax.ppermute(shard, axis, pairs)


def all_sum(x, axis):
    count = lax.axis_size(axis)
    if count & (count - 1):
        me = lax.axis_index(axis)
        parts = [x]
        for by in range(1, count):
            parts.append(lax.ppermute(x, axis, [(i, (i + by) % count) for i in range(count)]))
        stacked = jnp.stack(parts)
        order = (me - jnp.arange(count)) % count
        return jnp.sum(stacked[order], axis=0)
    bit = 1
    while bit < count:
        x = x + lax.ppermute(x, axis, [(i, i ^ bit) for i in range(count)])
        bit *= 2
    return x


def document_of(positions, doc_lengths):
    ends = jnp.cumsum(doc_lengths)
    return jnp.sum((ends[None, :] <= positions[:, None]).astype(jnp.int32), axis=1)


def block_terms(query, lookup_array, values, decay, docs, before):
    rows = docs.shape[0]
    level = jnp.cumsum(decay, axis=1)
    order = jnp.arange(rows)
    same = (docs[:, None] == docs[None, :]) & (order[None, :] <= order[:, None])
    scores = jnp.einsum("thd,shd->hts", query, lookup_array, preferred_element_type=jnp.float32)
    fade = jnp.exp(jnp.minimum(level[:, :, None] - level[:, None, :], 0.0))
    weights = jnp.where(same[None], scores * fade, 0.0).astype(jnp.bfloat16)
    inner = jnp.einsum("hts,shd->thd", weights, values, preferred_element_type=jnp.float32)
    carried = docs == before
    closing = (docs == docs[-1]).astype(jnp.float32)
    tail = jnp.exp(level[:, -1:] - level) * closing[None, :]
    weighted = (lookup_array.astype(jnp.float32) * tail.T[:, :, None]).astype(jnp.bfloat16)
    state = jnp.einsum("shd,she->hde", weighted, values, preferred_element_type=jnp.float32)
    shrinkage_multiplier = jnp.exp(level[:, -1]) * carried[-1].astype(jnp.float32)
    return (inner, level, carried, shrinkage_multiplier, state)


def local(doc_lengths, lin_q, lin_k, lin_v, log_decay, out_gate, lin_gain, soft_q, soft_k, soft_v):
    rows = lin_q.shape[0]
    heads_here = lin_q.shape[1] // DH
    kv_here = soft_k.shape[1] // DH
    group = soft_q.shape[1] // (kv_here * DH)
    shard = lax.axis_index("ctx")
    positions = shard * rows + jnp.arange(rows, dtype=jnp.int32)
    docs = document_of(positions, doc_lengths)
    before = jnp.where(shard > 0, document_of(positions[:1] - 1, doc_lengths)[0], -1)
    query = lin_q.reshape(rows, heads_here, DH)
    lookup_array = lin_k.reshape(rows, heads_here, DH)
    values = lin_v.reshape(rows, heads_here, DH)
    inner, level, carried, shrinkage_multiplier, state = block_terms(
        query, lookup_array, values, log_decay, docs, before
    )
    count = lax.axis_size("ctx")
    odd = (shard % 2) == 1
    pair = jnp.concatenate([soft_k, soft_v], axis=1)
    kv_width = soft_k.shape[1]
    n_state = heads_here * DH
    state_rows = state.reshape(n_state, DH)
    factor_rows = jnp.pad(shrinkage_multiplier[None, :], ((0, 7), (0, DH - heads_here)))
    window = jnp.concatenate(
        [from_behind(pair, "ctx", step) for step in range(SPAN, 0, -1)] + [pair], axis=0
    )
    all_keys = window[:, :kv_width].reshape(-1, kv_here, DH)
    all_values = window[:, kv_width:].reshape(-1, kv_here, DH)
    first = jnp.concatenate([state_rows, factor_rows], axis=0)
    got = lax.ppermute(first, "ctx", [(i, i ^ 1) for i in range(count)])
    state_mate = got[:n_state]
    factor_mate = got[n_state, :heads_here]
    state_cube = state_rows.reshape(state.shape)
    mate_cube = state_mate.reshape(state.shape)
    chip_state = jnp.where(
        odd,
        shrinkage_multiplier[:, None, None] * mate_cube + state_cube,
        factor_mate[:, None, None] * state_cube + mate_cube,
    )
    chip_factor = shrinkage_multiplier * factor_mate
    chip_top = chip_factor.astype(jnp.bfloat16)
    chip_rest = (chip_factor - chip_top.astype(jnp.float32)).astype(jnp.bfloat16)
    chip_rows = jnp.pad(jnp.stack([chip_top, chip_rest]), ((0, 14), (0, DH - heads_here)))
    packet = jnp.concatenate(
        [chip_state.astype(jnp.bfloat16).reshape(n_state, DH), chip_rows], axis=0
    )
    routes = [(i, i + 1) for i in range(1, count - 1, 2)] + [(i, i + 5) for i in range(0, count - 5, 2)]
    received = lax.ppermute(packet, "ctx", routes)
    mate_packet = lax.ppermute(received, "ctx", [(i, i ^ 1) for i in range(count)])
    near = jnp.where(odd, mate_packet, received)
    far = jnp.where(odd, received, mate_packet)

    def unpack(got_packet):
        chip = got_packet[:n_state].reshape(state.shape).astype(jnp.float32)
        mult = got_packet[n_state, :heads_here].astype(jnp.float32) + got_packet[
            n_state + 1, :heads_here
        ].astype(jnp.float32)
        return chip, mult

    state_near, factor_near = unpack(near)
    state_far, _ = unpack(far)
    incoming_even = state_near + factor_near[:, None, None] * state_far
    incoming = jnp.where(odd, factor_mate[:, None, None] * incoming_even + mate_cube, incoming_even)
    incoming_b = incoming.astype(jnp.bfloat16)
    outer = jnp.einsum(
        "thd,hde->the", query, incoming_b, preferred_element_type=jnp.float32
    )
    outer = outer * (jnp.exp(level).T * carried[:, None].astype(jnp.float32))[:, :, None]
    mixed = inner + outer
    local_sq = jnp.sum(mixed * mixed, axis=(1, 2))
    total_sq = all_sum(local_sq, "head")
    mean_sq = total_sq / (lax.axis_size("head") * heads_here * DH)
    flat = mixed.reshape(rows, heads_here * DH)
    normed = (
        flat
        * lax.rsqrt(mean_sq + 1e-06)[:, None]
        * lin_gain[None, :]
        * jax.nn.sigmoid(out_gate.astype(jnp.float32))
    )
    lin_out = normed.astype(jnp.bfloat16)
    span_rows = (SPAN + 1) * rows
    key_pos = shard * rows - SPAN * rows + jnp.arange(span_rows, dtype=jnp.int32)
    key_docs = jnp.where(key_pos >= 0, document_of(key_pos, doc_lengths), -1)
    allowed = (key_docs[None, :] == docs[:, None]) & (key_pos[None, :] <= positions[:, None])
    soft_query = soft_q.reshape(rows, kv_here, group, DH)
    scores = jnp.einsum(
        "tkgd,skd->kgts", soft_query, all_keys, preferred_element_type=jnp.float32
    ) * DH ** (-0.5)
    top = jnp.max(jnp.where(allowed, scores, -1e30), axis=-1, keepdims=True)
    expd = jnp.where(allowed, jnp.exp(jnp.minimum(scores - top, 0.0)), 0.0)
    total = jnp.sum(expd, axis=-1)
    attended = jnp.einsum(
        "kgts,skd->tkgd", expd.astype(jnp.bfloat16), all_values, preferred_element_type=jnp.float32
    )
    attended = attended / total.transpose(2, 0, 1)[..., None]
    soft_out = attended.reshape(rows, kv_here * group * DH).astype(jnp.bfloat16)
    return (lin_out, soft_out)


def solution(mesh):
    in_specs = (
        P(),
        P("ctx", "head"),
        P("ctx", "head"),
        P("ctx", "head"),
        P("head", "ctx"),
        P("ctx", "head"),
        P("head"),
        P("ctx", "head"),
        P("ctx", "head"),
        P("ctx", "head"),
    )
    out_specs = (P("ctx", "head"), P("ctx", "head"))
    return jax.shard_map(local, mesh=mesh, in_specs=in_specs, out_specs=out_specs, check_vma=False)
```

```python
import jax
import jax.numpy as jnp
from jax import lax
from jax.sharding import PartitionSpec as P

DH = 128
SPAN = 4


def from_behind(shard, axis, by):
    count = lax.axis_size(axis)
    pairs = [(i, i + by) for i in range(count) if 0 <= i + by < count]
    return lax.ppermute(shard, axis, pairs)


def all_sum(x, axis):
    count = lax.axis_size(axis)
    if count & (count - 1):
        me = lax.axis_index(axis)
        parts = [x]
        for by in range(1, count):
            parts.append(lax.ppermute(x, axis, [(i, (i + by) % count) for i in range(count)]))
        stacked = jnp.stack(parts)
        order = (me - jnp.arange(count)) % count
        return jnp.sum(stacked[order], axis=0)
    bit = 1
    while bit < count:
        x = x + lax.ppermute(x, axis, [(i, i ^ bit) for i in range(count)])
        bit *= 2
    return x


def document_of(positions, doc_lengths):
    count = doc_lengths.shape[0]
    upto = jnp.arange(count)[:, None] <= jnp.arange(count)[None, :]
    ends = jnp.sum(jnp.where(upto, doc_lengths[:, None], 0), axis=0)
    return jnp.sum((ends[None, :] <= positions[:, None]).astype(jnp.int32), axis=1)


def block_terms(query, lookup_array, values, decay, docs, before):
    rows = docs.shape[0]
    level = jnp.cumsum(decay, axis=1)
    order = jnp.arange(rows)
    same = (docs[:, None] == docs[None, :]) & (order[None, :] <= order[:, None])
    scores = jnp.einsum("thd,shd->hts", query, lookup_array, preferred_element_type=jnp.float32)
    fade = jnp.exp(jnp.minimum(level[:, :, None] - level[:, None, :], 0.0))
    weights = jnp.where(same[None], scores * fade, 0.0).astype(jnp.bfloat16)
    inner = jnp.einsum("hts,shd->thd", weights, values, preferred_element_type=jnp.float32)
    carried = docs == before
    closing = (docs == docs[-1]).astype(jnp.float32)
    tail = jnp.exp(level[:, -1:] - level) * closing[None, :]
    weighted = (lookup_array.astype(jnp.float32) * tail.T[:, :, None]).astype(jnp.bfloat16)
    state = jnp.einsum("shd,she->hde", weighted, values, preferred_element_type=jnp.float32)
    shrinkage_multiplier = jnp.exp(level[:, -1]) * carried[-1].astype(jnp.float32)
    return (inner, level, carried, shrinkage_multiplier, state)


def local(doc_lengths, lin_q, lin_k, lin_v, log_decay, out_gate, lin_gain, soft_q, soft_k, soft_v):
    rows = lin_q.shape[0]
    heads_here = lin_q.shape[1] // DH
    kv_here = soft_k.shape[1] // DH
    group = soft_q.shape[1] // (kv_here * DH)
    shard = lax.axis_index("ctx")
    positions = shard * rows + jnp.arange(rows, dtype=jnp.int32)
    docs = document_of(positions, doc_lengths)
    before = jnp.where(shard > 0, document_of(positions[:1] - 1, doc_lengths)[0], -1)
    query = lin_q.reshape(rows, heads_here, DH)
    lookup_array = lin_k.reshape(rows, heads_here, DH)
    values = lin_v.reshape(rows, heads_here, DH)
    inner, level, carried, shrinkage_multiplier, state = block_terms(
        query, lookup_array, values, log_decay, docs, before
    )
    count = lax.axis_size("ctx")
    odd = (shard % 2) == 1
    pair = jnp.concatenate(
        [soft_k.reshape(rows, kv_here, DH).transpose(1, 0, 2),
         soft_v.reshape(rows, kv_here, DH).transpose(1, 0, 2)],
        axis=0,
    ).reshape(-1, DH)
    n_pair = pair.shape[0]
    n_state = heads_here * DH
    state_rows = state.reshape(n_state, DH)
    swap = [(i, i ^ 1) for i in range(count)]
    decay_mate = lax.ppermute(log_decay, "ctx", swap)
    mate_start = (shard ^ 1) * rows
    mate_ends = document_of(jnp.stack([mate_start - 1, mate_start + rows - 1]), doc_lengths)
    mate_carried = (mate_ends[1] == jnp.where(mate_start > 0, mate_ends[0], -1)).astype(jnp.float32)
    factor_mate = jnp.exp(jnp.cumsum(decay_mate, axis=1)[:, -1]) * mate_carried
    window = jnp.concatenate(
        [from_behind(pair, "ctx", step) for step in range(SPAN, 0, -1)] + [pair], axis=0
    ).reshape(SPAN + 1, 2 * kv_here, rows, DH)
    state_mate = lax.ppermute(state_rows, "ctx", swap)
    state_cube = state_rows.reshape(state.shape)
    mate_cube = state_mate.reshape(state.shape)
    chip_state = jnp.where(
        odd,
        shrinkage_multiplier[:, None, None] * mate_cube + state_cube,
        factor_mate[:, None, None] * state_cube + mate_cube,
    )
    chip_factor = shrinkage_multiplier * factor_mate
    chip_top = chip_factor.astype(jnp.bfloat16)
    chip_rest = (chip_factor - chip_top.astype(jnp.float32)).astype(jnp.bfloat16)
    chip_rows = jnp.pad(jnp.stack([chip_top, chip_rest]), ((0, 14), (0, DH - heads_here)))
    packet = jnp.concatenate(
        [chip_state.astype(jnp.bfloat16).reshape(n_state, DH), chip_rows], axis=0
    )
    routes = [(i, i + 1) for i in range(1, count - 1, 2)] + [(i, i + 5) for i in range(0, count - 5, 2)]
    received = lax.ppermute(packet, "ctx", routes)
    mate_packet = lax.ppermute(received, "ctx", swap)
    near = jnp.where(odd, mate_packet, received)
    far = jnp.where(odd, received, mate_packet)

    def unpack(got_packet):
        chip = got_packet[:n_state].reshape(state.shape).astype(jnp.float32)
        mult = got_packet[n_state, :heads_here].astype(jnp.float32) + got_packet[
            n_state + 1, :heads_here
        ].astype(jnp.float32)
        return chip, mult

    state_near, factor_near = unpack(near)
    state_far, _ = unpack(far)
    incoming_even = state_near + factor_near[:, None, None] * state_far
    incoming = jnp.where(odd, factor_mate[:, None, None] * incoming_even + mate_cube, incoming_even)
    incoming_b = incoming.astype(jnp.bfloat16)
    outer = jnp.einsum(
        "thd,hde->the", query, incoming_b, preferred_element_type=jnp.float32
    )
    outer = outer * (jnp.exp(level).T * carried[:, None].astype(jnp.float32))[:, :, None]
    mixed = inner + outer
    local_sq = jnp.sum(mixed * mixed, axis=(1, 2))
    total_sq = all_sum(local_sq, "head")
    mean_sq = total_sq / (lax.axis_size("head") * heads_here * DH)
    flat = mixed.reshape(rows, heads_here * DH)
    normed = (
        flat
        * lax.rsqrt(mean_sq + 1e-06)[:, None]
        * lin_gain[None, :]
        * jax.nn.sigmoid(out_gate.astype(jnp.float32))
    )
    lin_out = normed.astype(jnp.bfloat16)
    span_rows = (SPAN + 1) * rows
    key_pos = shard * rows - SPAN * rows + jnp.arange(span_rows, dtype=jnp.int32)
    key_docs = jnp.where(key_pos >= 0, document_of(key_pos, doc_lengths), -1)
    allowed = (key_docs[None, :] == docs[:, None]) & (key_pos[None, :] <= positions[:, None])
    soft_query = soft_q.reshape(rows, kv_here, group, DH)
    scores = jnp.einsum(
        "tkgd,bksd->kgtbs", soft_query, window[:, :kv_here], preferred_element_type=jnp.float32
    ).reshape(kv_here, group, rows, span_rows) * DH ** (-0.5)
    top = jnp.max(jnp.where(allowed, scores, -1e30), axis=-1, keepdims=True)
    expd = jnp.where(allowed, jnp.exp(jnp.minimum(scores - top, 0.0)), 0.0)
    total = jnp.sum(expd, axis=-1)
    attended = jnp.einsum(
        "kgtbs,bksd->tkgd",
        expd.astype(jnp.bfloat16).reshape(kv_here, group, rows, SPAN + 1, rows),
        window[:, kv_here:],
        preferred_element_type=jnp.float32,
    )
    attended = attended / total.transpose(2, 0, 1)[..., None]
    soft_out = attended.reshape(rows, kv_here * group * DH).astype(jnp.bfloat16)
    return (lin_out, soft_out)


def solution(mesh):
    in_specs = (
        P(),
        P("ctx", "head"),
        P("ctx", "head"),
        P("ctx", "head"),
        P("head", "ctx"),
        P("ctx", "head"),
        P("head"),
        P("ctx", "head"),
        P("ctx", "head"),
        P("ctx", "head"),
    )
    out_specs = (P("ctx", "head"), P("ctx", "head"))
    return jax.shard_map(local, mesh=mesh, in_specs=in_specs, out_specs=out_specs, check_vma=False)
```

```python
import jax
import jax.numpy as jnp
from jax import lax
from jax.sharding import PartitionSpec as P

DH = 128
SPAN = 4


def from_behind(shard, axis, by):
    count = lax.axis_size(axis)
    pairs = [(i, i + by) for i in range(count) if 0 <= i + by < count]
    return lax.ppermute(shard, axis, pairs)


def all_sum(x, axis):
    count = lax.axis_size(axis)
    if count & (count - 1):
        me = lax.axis_index(axis)
        parts = [x]
        for by in range(1, count):
            parts.append(lax.ppermute(x, axis, [(i, (i + by) % count) for i in range(count)]))
        stacked = jnp.stack(parts)
        order = (me - jnp.arange(count)) % count
        return jnp.sum(stacked[order], axis=0)
    bit = 1
    while bit < count:
        x = x + lax.ppermute(x, axis, [(i, i ^ bit) for i in range(count)])
        bit *= 2
    return x


def document_of(positions, doc_lengths):
    ends = jnp.cumsum(doc_lengths)
    return jnp.sum((ends[None, :] <= positions[:, None]).astype(jnp.int32), axis=1)


def block_terms(query, lookup_array, values, decay, docs, before):
    rows = docs.shape[0]
    level = jnp.cumsum(decay, axis=1)
    order = jnp.arange(rows)
    same = (docs[:, None] == docs[None, :]) & (order[None, :] <= order[:, None])
    scores = jnp.einsum("thd,shd->hts", query, lookup_array, preferred_element_type=jnp.float32)
    fade = jnp.exp(jnp.minimum(level[:, :, None] - level[:, None, :], 0.0))
    weights = jnp.where(same[None], scores * fade, 0.0).astype(jnp.bfloat16)
    inner = jnp.einsum("hts,shd->thd", weights, values, preferred_element_type=jnp.float32)
    carried = docs == before
    closing = (docs == docs[-1]).astype(jnp.float32)
    tail = jnp.exp(level[:, -1:] - level) * closing[None, :]
    weighted = (lookup_array.astype(jnp.float32) * tail.T[:, :, None]).astype(jnp.bfloat16)
    state = jnp.einsum("shd,she->hde", weighted, values, preferred_element_type=jnp.float32)
    shrinkage_multiplier = jnp.exp(level[:, -1]) * carried[-1].astype(jnp.float32)
    return (inner, level, carried, shrinkage_multiplier, state)


def local(doc_lengths, lin_q, lin_k, lin_v, log_decay, out_gate, lin_gain, soft_q, soft_k, soft_v):
    rows = lin_q.shape[0]
    heads_here = lin_q.shape[1] // DH
    kv_here = soft_k.shape[1] // DH
    group = soft_q.shape[1] // (kv_here * DH)
    shard = lax.axis_index("ctx")
    positions = shard * rows + jnp.arange(rows, dtype=jnp.int32)
    docs = document_of(positions, doc_lengths)
    before = jnp.where(shard > 0, document_of(positions[:1] - 1, doc_lengths)[0], -1)
    query = lin_q.reshape(rows, heads_here, DH)
    lookup_array = lin_k.reshape(rows, heads_here, DH)
    values = lin_v.reshape(rows, heads_here, DH)
    inner, level, carried, shrinkage_multiplier, state = block_terms(
        query, lookup_array, values, log_decay, docs, before
    )
    count = lax.axis_size("ctx")
    odd = (shard % 2) == 1
    pair = jnp.concatenate(
        [soft_k.reshape(rows, kv_here, DH).transpose(1, 0, 2),
         soft_v.reshape(rows, kv_here, DH).transpose(1, 0, 2)],
        axis=0,
    ).reshape(-1, DH)
    n_pair = pair.shape[0]
    n_state = heads_here * DH
    state_rows = state.reshape(n_state, DH)
    factor_rows = jnp.pad(shrinkage_multiplier[None, :], ((0, 7), (0, DH - heads_here)))
    window = jnp.concatenate(
        [from_behind(pair, "ctx", step) for step in range(SPAN, 0, -1)] + [pair], axis=0
    ).reshape(SPAN + 1, 2 * kv_here, rows, DH)
    first = jnp.concatenate([state_rows, factor_rows], axis=0)
    got = lax.ppermute(first, "ctx", [(i, i ^ 1) for i in range(count)])
    state_mate = got[:n_state]
    factor_mate = got[n_state, :heads_here]
    state_cube = state_rows.reshape(state.shape)
    mate_cube = state_mate.reshape(state.shape)
    chip_state = jnp.where(
        odd,
        shrinkage_multiplier[:, None, None] * mate_cube + state_cube,
        factor_mate[:, None, None] * state_cube + mate_cube,
    )
    chip_factor = shrinkage_multiplier * factor_mate
    chip_top = chip_factor.astype(jnp.bfloat16)
    chip_rest = (chip_factor - chip_top.astype(jnp.float32)).astype(jnp.bfloat16)
    chip_rows = jnp.pad(jnp.stack([chip_top, chip_rest]), ((0, 14), (0, DH - heads_here)))
    packet = jnp.concatenate(
        [chip_state.astype(jnp.bfloat16).reshape(n_state, DH), chip_rows], axis=0
    )
    routes = [(i, i + 1) for i in range(1, count - 1, 2)] + [(i, i + 5) for i in range(0, count - 5, 2)]
    received = lax.ppermute(packet, "ctx", routes)
    span_rows = (SPAN + 1) * rows
    key_pos = shard * rows - SPAN * rows + jnp.arange(span_rows, dtype=jnp.int32)
    key_docs = jnp.where(key_pos >= 0, document_of(key_pos, doc_lengths), -1)
    allowed = (key_docs[None, :] == docs[:, None]) & (key_pos[None, :] <= positions[:, None])
    soft_query = soft_q.reshape(rows, kv_here, group, DH)
    scores = jnp.einsum(
        "tkgd,bksd->kgtbs", soft_query, window[:, :kv_here], preferred_element_type=jnp.float32
    ).reshape(kv_here, group, rows, span_rows) * DH ** (-0.5)
    top = jnp.max(jnp.where(allowed, scores, -1e30), axis=-1, keepdims=True)
    expd = jnp.where(allowed, jnp.exp(jnp.minimum(scores - top, 0.0)), 0.0)
    total = jnp.sum(expd, axis=-1)
    attended = jnp.einsum(
        "kgtbs,bksd->tkgd",
        expd.astype(jnp.bfloat16).reshape(kv_here, group, rows, SPAN + 1, rows),
        window[:, kv_here:],
        preferred_element_type=jnp.float32,
    )
    attended = attended / total.transpose(2, 0, 1)[..., None]
    soft_out = attended.reshape(rows, kv_here * group * DH).astype(jnp.bfloat16)
    soft_out, received = lax.optimization_barrier((soft_out, received))
    mate_packet = lax.ppermute(received, "ctx", [(i, i ^ 1) for i in range(count)])
    near = jnp.where(odd, mate_packet, received)
    far = jnp.where(odd, received, mate_packet)

    def unpack(got_packet):
        chip = got_packet[:n_state].reshape(state.shape).astype(jnp.float32)
        mult = got_packet[n_state, :heads_here].astype(jnp.float32) + got_packet[
            n_state + 1, :heads_here
        ].astype(jnp.float32)
        return chip, mult

    state_near, factor_near = unpack(near)
    state_far, _ = unpack(far)
    incoming_even = state_near + factor_near[:, None, None] * state_far
    incoming = jnp.where(odd, factor_mate[:, None, None] * incoming_even + mate_cube, incoming_even)
    incoming_b = incoming.astype(jnp.bfloat16)
    outer = jnp.einsum(
        "thd,hde->the", query, incoming_b, preferred_element_type=jnp.float32
    )
    outer = outer * (jnp.exp(level).T * carried[:, None].astype(jnp.float32))[:, :, None]
    mixed = inner + outer
    local_sq = jnp.sum(mixed * mixed, axis=(1, 2))
    total_sq = all_sum(local_sq, "head")
    mean_sq = total_sq / (lax.axis_size("head") * heads_here * DH)
    flat = mixed.reshape(rows, heads_here * DH)
    normed = (
        flat
        * lax.rsqrt(mean_sq + 1e-06)[:, None]
        * lin_gain[None, :]
        * jax.nn.sigmoid(out_gate.astype(jnp.float32))
    )
    lin_out = normed.astype(jnp.bfloat16)
    return (lin_out, soft_out)


def solution(mesh):
    in_specs = (
        P(),
        P("ctx", "head"),
        P("ctx", "head"),
        P("ctx", "head"),
        P("head", "ctx"),
        P("ctx", "head"),
        P("head"),
        P("ctx", "head"),
        P("ctx", "head"),
        P("ctx", "head"),
    )
    out_specs = (P("ctx", "head"), P("ctx", "head"))
    return jax.shard_map(local, mesh=mesh, in_specs=in_specs, out_specs=out_specs, check_vma=False)
```

```python
import jax
import jax.numpy as jnp
from jax import lax
from jax.sharding import PartitionSpec as P

DH = 128
SPAN = 4


def from_behind(shard, axis, by):
    count = lax.axis_size(axis)
    pairs = [(i, i + by) for i in range(count) if 0 <= i + by < count]
    return lax.ppermute(shard, axis, pairs)


def all_sum(x, axis):
    count = lax.axis_size(axis)
    if count & (count - 1):
        me = lax.axis_index(axis)
        parts = [x]
        for by in range(1, count):
            parts.append(lax.ppermute(x, axis, [(i, (i + by) % count) for i in range(count)]))
        stacked = jnp.stack(parts)
        order = (me - jnp.arange(count)) % count
        return jnp.sum(stacked[order], axis=0)
    bit = 1
    while bit < count:
        x = x + lax.ppermute(x, axis, [(i, i ^ bit) for i in range(count)])
        bit *= 2
    return x


def document_of(positions, doc_lengths):
    ends = jnp.cumsum(doc_lengths)
    return jnp.sum((ends[None, :] <= positions[:, None]).astype(jnp.int32), axis=1)


def block_terms(query, lookup_array, values, decay, docs, before):
    rows = docs.shape[0]
    level = jnp.cumsum(decay, axis=1)
    order = jnp.arange(rows)
    same = (docs[:, None] == docs[None, :]) & (order[None, :] <= order[:, None])
    scores = jnp.einsum("thd,shd->hts", query, lookup_array, preferred_element_type=jnp.float32)
    fade = jnp.exp(jnp.minimum(level[:, :, None] - level[:, None, :], 0.0))
    weights = jnp.where(same[None], scores * fade, 0.0).astype(jnp.bfloat16)
    inner = jnp.einsum("hts,shd->thd", weights, values, preferred_element_type=jnp.float32)
    carried = docs == before
    closing = (docs == docs[-1]).astype(jnp.float32)
    tail = jnp.exp(level[:, -1:] - level) * closing[None, :]
    weighted = (lookup_array.astype(jnp.float32) * tail.T[:, :, None]).astype(jnp.bfloat16)
    state = jnp.einsum("shd,she->hde", weighted, values, preferred_element_type=jnp.float32)
    shrinkage_multiplier = jnp.exp(level[:, -1]) * carried[-1].astype(jnp.float32)
    return (inner, level, carried, shrinkage_multiplier, state)


def local(doc_lengths, lin_q, lin_k, lin_v, log_decay, out_gate, lin_gain, soft_q, soft_k, soft_v):
    rows = lin_q.shape[0]
    heads_here = lin_q.shape[1] // DH
    kv_here = soft_k.shape[1] // DH
    group = soft_q.shape[1] // (kv_here * DH)
    shard = lax.axis_index("ctx")
    positions = shard * rows + jnp.arange(rows, dtype=jnp.int32)
    docs = document_of(positions, doc_lengths)
    before = jnp.where(shard > 0, document_of(positions[:1] - 1, doc_lengths)[0], -1)
    query = lin_q.reshape(rows, heads_here, DH)
    lookup_array = lin_k.reshape(rows, heads_here, DH)
    values = lin_v.reshape(rows, heads_here, DH)
    inner, level, carried, shrinkage_multiplier, state = block_terms(
        query, lookup_array, values, log_decay, docs, before
    )
    count = lax.axis_size("ctx")
    odd = (shard % 2) == 1
    pair = jnp.concatenate(
        [soft_k.reshape(rows, kv_here, DH).transpose(1, 0, 2),
         soft_v.reshape(rows, kv_here, DH).transpose(1, 0, 2)],
        axis=0,
    ).reshape(-1, DH)
    n_pair = pair.shape[0]
    n_state = heads_here * DH
    state_rows = state.reshape(n_state, DH)
    window = jnp.concatenate(
        [from_behind(pair, "ctx", step) for step in range(SPAN, 0, -1)] + [pair], axis=0
    ).reshape(SPAN + 1, 2 * kv_here, rows, DH)
    state_mate, factor_mate = lax.ppermute(
        (state_rows, shrinkage_multiplier), "ctx", [(i, i ^ 1) for i in range(count)]
    )
    state_cube = state_rows.reshape(state.shape)
    mate_cube = state_mate.reshape(state.shape)
    chip_state = jnp.where(
        odd,
        shrinkage_multiplier[:, None, None] * mate_cube + state_cube,
        factor_mate[:, None, None] * state_cube + mate_cube,
    )
    chip_factor = shrinkage_multiplier * factor_mate
    chip_top = chip_factor.astype(jnp.bfloat16)
    chip_rest = (chip_factor - chip_top.astype(jnp.float32)).astype(jnp.bfloat16)
    chip_rows = jnp.pad(jnp.stack([chip_top, chip_rest]), ((0, 14), (0, DH - heads_here)))
    packet = jnp.concatenate(
        [chip_state.astype(jnp.bfloat16).reshape(n_state, DH), chip_rows], axis=0
    )
    routes = [(i, i + 1) for i in range(1, count - 1, 2)] + [(i, i + 5) for i in range(0, count - 5, 2)]
    received = lax.ppermute(packet, "ctx", routes)
    mate_packet = lax.ppermute(received, "ctx", [(i, i ^ 1) for i in range(count)])
    near = jnp.where(odd, mate_packet, received)
    far = jnp.where(odd, received, mate_packet)

    def unpack(got_packet):
        chip = got_packet[:n_state].reshape(state.shape).astype(jnp.float32)
        mult = got_packet[n_state, :heads_here].astype(jnp.float32) + got_packet[
            n_state + 1, :heads_here
        ].astype(jnp.float32)
        return chip, mult

    state_near, factor_near = unpack(near)
    state_far, _ = unpack(far)
    incoming_even = state_near + factor_near[:, None, None] * state_far
    incoming = jnp.where(odd, factor_mate[:, None, None] * incoming_even + mate_cube, incoming_even)
    incoming_b = incoming.astype(jnp.bfloat16)
    outer = jnp.einsum(
        "thd,hde->the", query, incoming_b, preferred_element_type=jnp.float32
    )
    outer = outer * (jnp.exp(level).T * carried[:, None].astype(jnp.float32))[:, :, None]
    mixed = inner + outer
    local_sq = jnp.sum(mixed * mixed, axis=(1, 2))
    total_sq = all_sum(local_sq, "head")
    mean_sq = total_sq / (lax.axis_size("head") * heads_here * DH)
    flat = mixed.reshape(rows, heads_here * DH)
    normed = (
        flat
        * lax.rsqrt(mean_sq + 1e-06)[:, None]
        * lin_gain[None, :]
        * jax.nn.sigmoid(out_gate.astype(jnp.float32))
    )
    lin_out = normed.astype(jnp.bfloat16)
    span_rows = (SPAN + 1) * rows
    key_pos = shard * rows - SPAN * rows + jnp.arange(span_rows, dtype=jnp.int32)
    key_docs = jnp.where(key_pos >= 0, document_of(key_pos, doc_lengths), -1)
    allowed = (key_docs[None, :] == docs[:, None]) & (key_pos[None, :] <= positions[:, None])
    soft_query = soft_q.reshape(rows, kv_here, group, DH)
    scores = jnp.einsum(
        "tkgd,bksd->kgtbs", soft_query, window[:, :kv_here], preferred_element_type=jnp.float32
    ).reshape(kv_here, group, rows, span_rows) * DH ** (-0.5)
    top = jnp.max(jnp.where(allowed, scores, -1e30), axis=-1, keepdims=True)
    expd = jnp.where(allowed, jnp.exp(jnp.minimum(scores - top, 0.0)), 0.0)
    total = jnp.sum(expd, axis=-1)
    attended = jnp.einsum(
        "kgtbs,bksd->tkgd",
        expd.astype(jnp.bfloat16).reshape(kv_here, group, rows, SPAN + 1, rows),
        window[:, kv_here:],
        preferred_element_type=jnp.float32,
    )
    attended = attended / total.transpose(2, 0, 1)[..., None]
    soft_out = attended.reshape(rows, kv_here * group * DH).astype(jnp.bfloat16)
    return (lin_out, soft_out)


def solution(mesh):
    in_specs = (
        P(),
        P("ctx", "head"),
        P("ctx", "head"),
        P("ctx", "head"),
        P("head", "ctx"),
        P("ctx", "head"),
        P("head"),
        P("ctx", "head"),
        P("ctx", "head"),
        P("ctx", "head"),
    )
    out_specs = (P("ctx", "head"), P("ctx", "head"))
    return jax.shard_map(local, mesh=mesh, in_specs=in_specs, out_specs=out_specs, check_vma=False)
```

```python
import jax
import jax.numpy as jnp
from jax import lax
from jax.sharding import PartitionSpec as P

DH = 128
SPAN = 4


def from_behind(shard, axis, by):
    count = lax.axis_size(axis)
    pairs = [(i, i + by) for i in range(count) if 0 <= i + by < count]
    return lax.ppermute(shard, axis, pairs)


def all_sum(x, axis):
    count = lax.axis_size(axis)
    if count & (count - 1):
        me = lax.axis_index(axis)
        parts = [x]
        for by in range(1, count):
            parts.append(lax.ppermute(x, axis, [(i, (i + by) % count) for i in range(count)]))
        stacked = jnp.stack(parts)
        order = (me - jnp.arange(count)) % count
        return jnp.sum(stacked[order], axis=0)
    bit = 1
    while bit < count:
        x = x + lax.ppermute(x, axis, [(i, i ^ bit) for i in range(count)])
        bit *= 2
    return x


def document_of(positions, doc_lengths):
    ends = jnp.cumsum(doc_lengths)
    return jnp.sum((ends[None, :] <= positions[:, None]).astype(jnp.int32), axis=1)


def block_terms(query, lookup_array, values, decay, docs, before):
    rows = docs.shape[0]
    level = jnp.cumsum(decay, axis=1)
    order = jnp.arange(rows)
    same = (docs[:, None] == docs[None, :]) & (order[None, :] <= order[:, None])
    scores = jnp.einsum("thd,shd->hts", query, lookup_array, preferred_element_type=jnp.float32)
    fade = jnp.exp(jnp.minimum(level[:, :, None] - level[:, None, :], 0.0))
    weights = jnp.where(same[None], scores * fade, 0.0).astype(jnp.bfloat16)
    inner = jnp.einsum("hts,shd->thd", weights, values, preferred_element_type=jnp.float32)
    carried = docs == before
    closing = (docs == docs[-1]).astype(jnp.float32)
    tail = jnp.exp(level[:, -1:] - level) * closing[None, :]
    weighted = (lookup_array.astype(jnp.float32) * tail.T[:, :, None]).astype(jnp.bfloat16)
    state = jnp.einsum("shd,she->hde", weighted, values, preferred_element_type=jnp.float32)
    shrinkage_multiplier = jnp.exp(level[:, -1]) * carried[-1].astype(jnp.float32)
    return (inner, level, carried, shrinkage_multiplier, state)


def local(doc_lengths, lin_q, lin_k, lin_v, log_decay, out_gate, lin_gain, soft_q, soft_k, soft_v):
    rows = lin_q.shape[0]
    heads_here = lin_q.shape[1] // DH
    kv_here = soft_k.shape[1] // DH
    group = soft_q.shape[1] // (kv_here * DH)
    shard = lax.axis_index("ctx")
    positions = shard * rows + jnp.arange(rows, dtype=jnp.int32)
    docs = document_of(positions, doc_lengths)
    before = jnp.where(shard > 0, document_of(positions[:1] - 1, doc_lengths)[0], -1)
    query = lin_q.reshape(rows, heads_here, DH)
    lookup_array = lin_k.reshape(rows, heads_here, DH)
    values = lin_v.reshape(rows, heads_here, DH)
    inner, level, carried, shrinkage_multiplier, state = block_terms(
        query, lookup_array, values, log_decay, docs, before
    )
    count = lax.axis_size("ctx")
    odd = (shard % 2) == 1
    pair = jnp.concatenate(
        [soft_k.reshape(rows, kv_here, DH).transpose(1, 0, 2),
         soft_v.reshape(rows, kv_here, DH).transpose(1, 0, 2)],
        axis=0,
    ).reshape(-1, DH)
    n_pair = pair.shape[0]
    n_state = heads_here * DH
    state_rows = state.reshape(n_state, DH)
    factor_rows = jnp.pad(shrinkage_multiplier[None, :], ((0, 7), (0, DH - heads_here)))
    window = jnp.concatenate(
        [from_behind(pair, "ctx", step) for step in range(SPAN, 0, -1)] + [pair], axis=0
    ).reshape(SPAN + 1, 2 * kv_here, rows, DH)
    first = jnp.concatenate([state_rows, factor_rows], axis=0)
    got = lax.ppermute(first, "ctx", [(i, i ^ 1) for i in range(count)])
    state_mate = got[:n_state]
    factor_mate = got[n_state, :heads_here]
    state_cube = state_rows.reshape(state.shape)
    mate_cube = state_mate.reshape(state.shape)
    chip_state = jnp.where(
        odd,
        shrinkage_multiplier[:, None, None] * mate_cube + state_cube,
        factor_mate[:, None, None] * state_cube + mate_cube,
    )
    chip_factor = shrinkage_multiplier * factor_mate
    chip_top = chip_factor.astype(jnp.bfloat16)
    chip_rest = (chip_factor - chip_top.astype(jnp.float32)).astype(jnp.bfloat16)
    chip_rows = jnp.pad(jnp.stack([chip_top, chip_rest]), ((0, 14), (0, DH - heads_here)))
    packet = jnp.concatenate(
        [chip_state.astype(jnp.bfloat16).reshape(n_state, DH), chip_rows], axis=0
    )
    routes = [(i, i + 1) for i in range(1, count - 1, 2)] + [(i, i + 5) for i in range(0, count - 5, 2)]
    packet, soft_q = lax.optimization_barrier((packet, soft_q))
    received = lax.ppermute(packet, "ctx", routes)
    span_rows = (SPAN + 1) * rows
    key_pos = shard * rows - SPAN * rows + jnp.arange(span_rows, dtype=jnp.int32)
    key_docs = jnp.where(key_pos >= 0, document_of(key_pos, doc_lengths), -1)
    allowed = (key_docs[None, :] == docs[:, None]) & (key_pos[None, :] <= positions[:, None])
    soft_query = soft_q.reshape(rows, kv_here, group, DH)
    scores = jnp.einsum(
        "tkgd,bksd->kgtbs", soft_query, window[:, :kv_here], preferred_element_type=jnp.float32
    ).reshape(kv_here, group, rows, span_rows) * DH ** (-0.5)
    top = jnp.max(jnp.where(allowed, scores, -1e30), axis=-1, keepdims=True)
    expd = jnp.where(allowed, jnp.exp(jnp.minimum(scores - top, 0.0)), 0.0)
    total = jnp.sum(expd, axis=-1)
    attended = jnp.einsum(
        "kgtbs,bksd->tkgd",
        expd.astype(jnp.bfloat16).reshape(kv_here, group, rows, SPAN + 1, rows),
        window[:, kv_here:],
        preferred_element_type=jnp.float32,
    )
    attended = attended / total.transpose(2, 0, 1)[..., None]
    soft_out = attended.reshape(rows, kv_here * group * DH).astype(jnp.bfloat16)
    soft_out, received = lax.optimization_barrier((soft_out, received))
    mate_packet = lax.ppermute(received, "ctx", [(i, i ^ 1) for i in range(count)])
    near = jnp.where(odd, mate_packet, received)
    far = jnp.where(odd, received, mate_packet)

    def unpack(got_packet):
        chip = got_packet[:n_state].reshape(state.shape).astype(jnp.float32)
        mult = got_packet[n_state, :heads_here].astype(jnp.float32) + got_packet[
            n_state + 1, :heads_here
        ].astype(jnp.float32)
        return chip, mult

    state_near, factor_near = unpack(near)
    state_far, _ = unpack(far)
    incoming_even = state_near + factor_near[:, None, None] * state_far
    incoming = jnp.where(odd, factor_mate[:, None, None] * incoming_even + mate_cube, incoming_even)
    incoming_b = incoming.astype(jnp.bfloat16)
    outer = jnp.einsum(
        "thd,hde->the", query, incoming_b, preferred_element_type=jnp.float32
    )
    outer = outer * (jnp.exp(level).T * carried[:, None].astype(jnp.float32))[:, :, None]
    mixed = inner + outer
    local_sq = jnp.sum(mixed * mixed, axis=(1, 2))
    total_sq = all_sum(local_sq, "head")
    mean_sq = total_sq / (lax.axis_size("head") * heads_here * DH)
    flat = mixed.reshape(rows, heads_here * DH)
    normed = (
        flat
        * lax.rsqrt(mean_sq + 1e-06)[:, None]
        * lin_gain[None, :]
        * jax.nn.sigmoid(out_gate.astype(jnp.float32))
    )
    lin_out = normed.astype(jnp.bfloat16)
    return (lin_out, soft_out)


def solution(mesh):
    in_specs = (
        P(),
        P("ctx", "head"),
        P("ctx", "head"),
        P("ctx", "head"),
        P("head", "ctx"),
        P("ctx", "head"),
        P("head"),
        P("ctx", "head"),
        P("ctx", "head"),
        P("ctx", "head"),
    )
    out_specs = (P("ctx", "head"), P("ctx", "head"))
    return jax.shard_map(local, mesh=mesh, in_specs=in_specs, out_specs=out_specs, check_vma=False)
```

```python
import jax
import jax.numpy as jnp
from jax import lax
from jax.sharding import PartitionSpec as P

DH = 128
SPAN = 4


def from_behind(shard, axis, by):
    count = lax.axis_size(axis)
    pairs = [(i, i + by) for i in range(count) if 0 <= i + by < count]
    return lax.ppermute(shard, axis, pairs)


def all_sum(x, axis):
    count = lax.axis_size(axis)
    if count & (count - 1):
        me = lax.axis_index(axis)
        parts = [x]
        for by in range(1, count):
            parts.append(lax.ppermute(x, axis, [(i, (i + by) % count) for i in range(count)]))
        stacked = jnp.stack(parts)
        order = (me - jnp.arange(count)) % count
        return jnp.sum(stacked[order], axis=0)
    bit = 1
    while bit < count:
        x = x + lax.ppermute(x, axis, [(i, i ^ bit) for i in range(count)])
        bit *= 2
    return x


def document_of(positions, doc_lengths):
    ends = jnp.cumsum(doc_lengths)
    return jnp.sum((ends[None, :] <= positions[:, None]).astype(jnp.int32), axis=1)


def block_terms(query, lookup_array, values, decay, docs, before):
    rows = docs.shape[0]
    level = jnp.cumsum(decay, axis=1)
    order = jnp.arange(rows)
    same = (docs[:, None] == docs[None, :]) & (order[None, :] <= order[:, None])
    scores = jnp.einsum("thd,shd->hts", query, lookup_array, preferred_element_type=jnp.float32)
    fade = jnp.exp(jnp.minimum(level[:, :, None] - level[:, None, :], 0.0))
    weights = jnp.where(same[None], scores * fade, 0.0).astype(jnp.bfloat16)
    inner = jnp.einsum("hts,shd->thd", weights, values, preferred_element_type=jnp.float32)
    carried = docs == before
    closing = (docs == docs[-1]).astype(jnp.float32)
    tail = jnp.exp(level[:, -1:] - level) * closing[None, :]
    weighted = (lookup_array.astype(jnp.float32) * tail.T[:, :, None]).astype(jnp.bfloat16)
    state = jnp.einsum("shd,she->hde", weighted, values, preferred_element_type=jnp.float32)
    shrinkage_multiplier = jnp.exp(level[:, -1]) * carried[-1].astype(jnp.float32)
    return (inner, level, carried, shrinkage_multiplier, state)


def local(doc_lengths, lin_q, lin_k, lin_v, log_decay, out_gate, lin_gain, soft_q, soft_k, soft_v):
    rows = lin_q.shape[0]
    heads_here = lin_q.shape[1] // DH
    kv_here = soft_k.shape[1] // DH
    group = soft_q.shape[1] // (kv_here * DH)
    shard = lax.axis_index("ctx")
    positions = shard * rows + jnp.arange(rows, dtype=jnp.int32)
    docs = document_of(positions, doc_lengths)
    before = jnp.where(shard > 0, document_of(positions[:1] - 1, doc_lengths)[0], -1)
    query = lin_q.reshape(rows, heads_here, DH)
    lookup_array = lin_k.reshape(rows, heads_here, DH)
    values = lin_v.reshape(rows, heads_here, DH)
    inner, level, carried, shrinkage_multiplier, state = block_terms(
        query, lookup_array, values, log_decay, docs, before
    )
    count = lax.axis_size("ctx")
    odd = (shard % 2) == 1
    pair = jnp.concatenate([soft_k, soft_v], axis=1)
    kv_width = soft_k.shape[1]
    n_state = heads_here * DH
    state_rows = state.reshape(n_state, DH)
    factor_rows = jnp.pad(shrinkage_multiplier[None, :], ((0, 7), (0, DH - heads_here)))
    window = jnp.concatenate(
        [from_behind(pair, "ctx", step) for step in range(SPAN, 0, -1)] + [pair], axis=0
    )
    first = jnp.concatenate([state_rows, factor_rows], axis=0)
    got = lax.ppermute(first, "ctx", [(i, i ^ 1) for i in range(count)])
    state_mate = got[:n_state]
    factor_mate = got[n_state, :heads_here]
    state_cube = state_rows.reshape(state.shape)
    mate_cube = state_mate.reshape(state.shape)
    chip_state = jnp.where(
        odd,
        shrinkage_multiplier[:, None, None] * mate_cube + state_cube,
        factor_mate[:, None, None] * state_cube + mate_cube,
    )
    chip_factor = shrinkage_multiplier * factor_mate
    chip_top = chip_factor.astype(jnp.bfloat16)
    chip_rest = (chip_factor - chip_top.astype(jnp.float32)).astype(jnp.bfloat16)
    chip_rows = jnp.pad(jnp.stack([chip_top, chip_rest]), ((0, 14), (0, DH - heads_here)))
    packet = jnp.concatenate(
        [chip_state.astype(jnp.bfloat16).reshape(n_state, DH), chip_rows], axis=0
    )
    routes = [(i, i + 1) for i in range(1, count - 1, 2)] + [(i, i + 5) for i in range(0, count - 5, 2)]
    packet, soft_q = lax.optimization_barrier((packet, soft_q))
    received = lax.ppermute(packet, "ctx", routes)
    span_rows = (SPAN + 1) * rows
    key_pos = shard * rows - SPAN * rows + jnp.arange(span_rows, dtype=jnp.int32)
    key_docs = jnp.where(key_pos >= 0, document_of(key_pos, doc_lengths), -1)
    allowed = (key_docs[None, :] == docs[:, None]) & (key_pos[None, :] <= positions[:, None])
    soft_query = soft_q.reshape(rows, kv_here, group, DH)
    all_keys = window[:, :kv_width].reshape(span_rows, kv_here, DH)
    all_values = window[:, kv_width:].reshape(span_rows, kv_here, DH)
    scores = jnp.einsum(
        "tkgd,skd->kgts", soft_query, all_keys, preferred_element_type=jnp.float32
    ) * DH ** (-0.5)
    top = jnp.max(jnp.where(allowed, scores, -1e30), axis=-1, keepdims=True)
    expd = jnp.where(allowed, jnp.exp(jnp.minimum(scores - top, 0.0)), 0.0)
    total = jnp.sum(expd, axis=-1)
    attended = jnp.einsum(
        "kgts,skd->tkgd", expd.astype(jnp.bfloat16), all_values, preferred_element_type=jnp.float32
    )
    attended = attended / total.transpose(2, 0, 1)[..., None]
    soft_out = attended.reshape(rows, kv_here * group * DH).astype(jnp.bfloat16)
    soft_out, received = lax.optimization_barrier((soft_out, received))
    mate_packet = lax.ppermute(received, "ctx", [(i, i ^ 1) for i in range(count)])
    near = jnp.where(odd, mate_packet, received)
    far = jnp.where(odd, received, mate_packet)

    def unpack(got_packet):
        chip = got_packet[:n_state].reshape(state.shape).astype(jnp.float32)
        mult = got_packet[n_state, :heads_here].astype(jnp.float32) + got_packet[
            n_state + 1, :heads_here
        ].astype(jnp.float32)
        return chip, mult

    state_near, factor_near = unpack(near)
    state_far, _ = unpack(far)
    incoming_even = state_near + factor_near[:, None, None] * state_far
    incoming = jnp.where(odd, factor_mate[:, None, None] * incoming_even + mate_cube, incoming_even)
    incoming_b = incoming.astype(jnp.bfloat16)
    outer = jnp.einsum(
        "thd,hde->the", query, incoming_b, preferred_element_type=jnp.float32
    )
    outer = outer * (jnp.exp(level).T * carried[:, None].astype(jnp.float32))[:, :, None]
    mixed = inner + outer
    local_sq = jnp.sum(mixed * mixed, axis=(1, 2))
    total_sq = all_sum(local_sq, "head")
    mean_sq = total_sq / (lax.axis_size("head") * heads_here * DH)
    flat = mixed.reshape(rows, heads_here * DH)
    normed = (
        flat
        * lax.rsqrt(mean_sq + 1e-06)[:, None]
        * lin_gain[None, :]
        * jax.nn.sigmoid(out_gate.astype(jnp.float32))
    )
    lin_out = normed.astype(jnp.bfloat16)
    return (lin_out, soft_out)


def solution(mesh):
    in_specs = (
        P(),
        P("ctx", "head"),
        P("ctx", "head"),
        P("ctx", "head"),
        P("head", "ctx"),
        P("ctx", "head"),
        P("head"),
        P("ctx", "head"),
        P("ctx", "head"),
        P("ctx", "head"),
    )
    out_specs = (P("ctx", "head"), P("ctx", "head"))
    return jax.shard_map(local, mesh=mesh, in_specs=in_specs, out_specs=out_specs, check_vma=False)
```

```python
import jax
import jax.numpy as jnp
from jax import lax
from jax.sharding import PartitionSpec as P

DH = 128
SPAN = 4


def from_behind(shard, axis, by):
    count = lax.axis_size(axis)
    pairs = [(i, i + by) for i in range(count) if 0 <= i + by < count]
    return lax.ppermute(shard, axis, pairs)


def all_sum(x, axis):
    count = lax.axis_size(axis)
    me = lax.axis_index(axis)
    parts = [x]
    for by in range(1, count):
        parts.append(lax.ppermute(x, axis, [(i, (i + by) % count) for i in range(count)]))
    stacked = jnp.stack(parts)
    order = (me - jnp.arange(count)) % count
    return jnp.sum(stacked[order], axis=0)


def document_of(positions, doc_lengths):
    ends = jnp.cumsum(doc_lengths)
    return jnp.sum((ends[None, :] <= positions[:, None]).astype(jnp.int32), axis=1)


def block_terms(query, lookup_array, values, decay, docs, before):
    rows = docs.shape[0]
    level = jnp.cumsum(decay, axis=1)
    order = jnp.arange(rows)
    same = (docs[:, None] == docs[None, :]) & (order[None, :] <= order[:, None])
    scores = jnp.einsum("thd,shd->hts", query, lookup_array, preferred_element_type=jnp.float32)
    fade = jnp.exp(jnp.minimum(level[:, :, None] - level[:, None, :], 0.0))
    weights = jnp.where(same[None], scores * fade, 0.0).astype(jnp.bfloat16)
    inner = jnp.einsum("hts,shd->thd", weights, values, preferred_element_type=jnp.float32)
    carried = docs == before
    closing = (docs == docs[-1]).astype(jnp.float32)
    tail = jnp.exp(level[:, -1:] - level) * closing[None, :]
    weighted = (lookup_array.astype(jnp.float32) * tail.T[:, :, None]).astype(jnp.bfloat16)
    state = jnp.einsum("shd,she->hde", weighted, values, preferred_element_type=jnp.float32)
    shrinkage_multiplier = jnp.exp(level[:, -1]) * carried[-1].astype(jnp.float32)
    return (inner, level, carried, shrinkage_multiplier, state)


def local(doc_lengths, lin_q, lin_k, lin_v, log_decay, out_gate, lin_gain, soft_q, soft_k, soft_v):
    rows = lin_q.shape[0]
    heads_here = lin_q.shape[1] // DH
    kv_here = soft_k.shape[1] // DH
    group = soft_q.shape[1] // (kv_here * DH)
    shard = lax.axis_index("ctx")
    positions = shard * rows + jnp.arange(rows, dtype=jnp.int32)
    docs = document_of(positions, doc_lengths)
    before = jnp.where(shard > 0, document_of(positions[:1] - 1, doc_lengths)[0], -1)
    query = lin_q.reshape(rows, heads_here, DH)
    lookup_array = lin_k.reshape(rows, heads_here, DH)
    values = lin_v.reshape(rows, heads_here, DH)
    inner, level, carried, shrinkage_multiplier, state = block_terms(
        query, lookup_array, values, log_decay, docs, before
    )
    count = lax.axis_size("ctx")
    odd = (shard % 2) == 1
    pair = jnp.concatenate([soft_k, soft_v], axis=1)
    kv_width = soft_k.shape[1]
    n_state = heads_here * DH
    state_rows = state.reshape(n_state, DH)
    factor_rows = jnp.pad(shrinkage_multiplier[None, :], ((0, 7), (0, DH - heads_here)))
    window = jnp.concatenate(
        [from_behind(pair, "ctx", step) for step in range(SPAN, 0, -1)] + [pair], axis=0
    )
    first = jnp.concatenate([state_rows, factor_rows], axis=0)
    got = lax.ppermute(first, "ctx", [(i, i ^ 1) for i in range(count)])
    state_mate = got[:n_state]
    factor_mate = got[n_state, :heads_here]
    state_cube = state_rows.reshape(state.shape)
    mate_cube = state_mate.reshape(state.shape)
    chip_state = jnp.where(
        odd,
        shrinkage_multiplier[:, None, None] * mate_cube + state_cube,
        factor_mate[:, None, None] * state_cube + mate_cube,
    )
    chip_factor = shrinkage_multiplier * factor_mate
    chip_top = chip_factor.astype(jnp.bfloat16)
    chip_rest = (chip_factor - chip_top.astype(jnp.float32)).astype(jnp.bfloat16)
    chip_rows = jnp.pad(jnp.stack([chip_top, chip_rest]), ((0, 14), (0, DH - heads_here)))
    packet = jnp.concatenate(
        [chip_state.astype(jnp.bfloat16).reshape(n_state, DH), chip_rows], axis=0
    )
    routes = [(i, i + 1) for i in range(1, count - 1, 2)] + [(i, i + 5) for i in range(0, count - 5, 2)]
    packet, soft_q = lax.optimization_barrier((packet, soft_q))
    received = lax.ppermute(packet, "ctx", routes)
    span_rows = (SPAN + 1) * rows
    key_pos = shard * rows - SPAN * rows + jnp.arange(span_rows, dtype=jnp.int32)
    key_docs = jnp.where(key_pos >= 0, document_of(key_pos, doc_lengths), -1)
    allowed = (key_docs[None, :] == docs[:, None]) & (key_pos[None, :] <= positions[:, None])
    soft_query = soft_q.reshape(rows, kv_here, group, DH)
    all_keys = window[:, :kv_width].reshape(span_rows, kv_here, DH)
    all_values = window[:, kv_width:].reshape(span_rows, kv_here, DH)
    scores = jnp.einsum(
        "tkgd,skd->kgts", soft_query, all_keys, preferred_element_type=jnp.float32
    ) * DH ** (-0.5)
    top = jnp.max(jnp.where(allowed, scores, -1e30), axis=-1, keepdims=True)
    expd = jnp.where(allowed, jnp.exp(jnp.minimum(scores - top, 0.0)), 0.0)
    total = jnp.sum(expd, axis=-1)
    attended = jnp.einsum(
        "kgts,skd->tkgd", expd.astype(jnp.bfloat16), all_values, preferred_element_type=jnp.float32
    )
    attended = attended / total.transpose(2, 0, 1)[..., None]
    soft_out = attended.reshape(rows, kv_here * group * DH).astype(jnp.bfloat16)
    soft_out, received = lax.optimization_barrier((soft_out, received))
    mate_packet = lax.ppermute(received, "ctx", [(i, i ^ 1) for i in range(count)])
    near = jnp.where(odd, mate_packet, received)
    far = jnp.where(odd, received, mate_packet)

    def unpack(got_packet):
        chip = got_packet[:n_state].reshape(state.shape).astype(jnp.float32)
        mult = got_packet[n_state, :heads_here].astype(jnp.float32) + got_packet[
            n_state + 1, :heads_here
        ].astype(jnp.float32)
        return chip, mult

    state_near, factor_near = unpack(near)
    state_far, _ = unpack(far)
    incoming_even = state_near + factor_near[:, None, None] * state_far
    incoming = jnp.where(odd, factor_mate[:, None, None] * incoming_even + mate_cube, incoming_even)
    incoming_b = incoming.astype(jnp.bfloat16)
    outer = jnp.einsum(
        "thd,hde->the", query, incoming_b, preferred_element_type=jnp.float32
    )
    outer = outer * (jnp.exp(level).T * carried[:, None].astype(jnp.float32))[:, :, None]
    mixed = inner + outer
    local_sq = jnp.sum(mixed * mixed, axis=(1, 2))
    total_sq = all_sum(local_sq, "head")
    mean_sq = total_sq / (lax.axis_size("head") * heads_here * DH)
    flat = mixed.reshape(rows, heads_here * DH)
    normed = (
        flat
        * lax.rsqrt(mean_sq + 1e-06)[:, None]
        * lin_gain[None, :]
        * jax.nn.sigmoid(out_gate.astype(jnp.float32))
    )
    lin_out = normed.astype(jnp.bfloat16)
    return (lin_out, soft_out)


def solution(mesh):
    in_specs = (
        P(),
        P("ctx", "head"),
        P("ctx", "head"),
        P("ctx", "head"),
        P("head", "ctx"),
        P("ctx", "head"),
        P("head"),
        P("ctx", "head"),
        P("ctx", "head"),
        P("ctx", "head"),
    )
    out_specs = (P("ctx", "head"), P("ctx", "head"))
    return jax.shard_map(local, mesh=mesh, in_specs=in_specs, out_specs=out_specs, check_vma=False)
```

```python
import jax
import jax.numpy as jnp
from jax import lax
from jax.sharding import PartitionSpec as P

DH = 128
SPAN = 4


def from_behind(shard, axis, by):
    count = lax.axis_size(axis)
    pairs = [(i, i + by) for i in range(count) if 0 <= i + by < count]
    return lax.ppermute(shard, axis, pairs)


def all_sum(x, axis):
    count = lax.axis_size(axis)
    if count & (count - 1):
        me = lax.axis_index(axis)
        parts = [x]
        for by in range(1, count):
            parts.append(lax.ppermute(x, axis, [(i, (i + by) % count) for i in range(count)]))
        stacked = jnp.stack(parts)
        order = (me - jnp.arange(count)) % count
        return jnp.sum(stacked[order], axis=0)
    bit = 1
    while bit < count:
        x = x + lax.ppermute(x, axis, [(i, i ^ bit) for i in range(count)])
        bit *= 2
    return x


def document_of(positions, doc_lengths):
    ends = jnp.cumsum(doc_lengths)
    return jnp.sum((ends[None, :] <= positions[:, None]).astype(jnp.int32), axis=1)


def block_terms(query, lookup_array, values, decay, docs, before, last):
    rows = docs.shape[0]
    level = jnp.cumsum(decay, axis=1)
    order = jnp.arange(rows)
    same = (docs[:, None] == docs[None, :]) & (order[None, :] <= order[:, None])
    scores = jnp.einsum("thd,shd->hts", query, lookup_array, preferred_element_type=jnp.float32)
    fade = jnp.exp(jnp.minimum(level[:, :, None] - level[:, None, :], 0.0))
    weights = jnp.where(same[None], scores * fade, 0.0).astype(jnp.bfloat16)
    inner = jnp.einsum("hts,shd->thd", weights, values, preferred_element_type=jnp.float32)
    carried = docs == before
    closing = (docs == last).astype(jnp.float32)
    tail = jnp.exp(level[:, -1:] - level) * closing[None, :]
    weighted = (lookup_array.astype(jnp.float32) * tail.T[:, :, None]).astype(jnp.bfloat16)
    state = jnp.einsum("shd,she->hde", weighted, values, preferred_element_type=jnp.float32)
    shrinkage_multiplier = jnp.exp(level[:, -1]) * (last == before).astype(jnp.float32)
    return (inner, level, carried, shrinkage_multiplier, state)


def local(doc_lengths, lin_q, lin_k, lin_v, log_decay, out_gate, lin_gain, soft_q, soft_k, soft_v):
    rows = lin_q.shape[0]
    heads_here = lin_q.shape[1] // DH
    kv_here = soft_k.shape[1] // DH
    group = soft_q.shape[1] // (kv_here * DH)
    shard = lax.axis_index("ctx")
    positions = shard * rows + jnp.arange(rows, dtype=jnp.int32)
    ends = jnp.cumsum(doc_lengths)
    docs = jnp.sum((ends[None, :] <= positions[:, None]).astype(jnp.int32), axis=1)
    last = jnp.sum((ends <= shard * rows + rows - 1).astype(jnp.int32))
    before = jnp.where(shard > 0, jnp.sum((ends <= shard * rows - 1).astype(jnp.int32)), -1)
    query = lin_q.reshape(rows, heads_here, DH)
    lookup_array = lin_k.reshape(rows, heads_here, DH)
    values = lin_v.reshape(rows, heads_here, DH)
    inner, level, carried, shrinkage_multiplier, state = block_terms(
        query, lookup_array, values, log_decay, docs, before, last
    )
    count = lax.axis_size("ctx")
    odd = (shard % 2) == 1
    pair = jnp.concatenate([soft_k, soft_v], axis=1)
    kv_width = soft_k.shape[1]
    n_state = heads_here * DH
    state_rows = state.reshape(n_state, DH)
    factor_rows = jnp.pad(shrinkage_multiplier[None, :], ((0, 7), (0, DH - heads_here)))
    window = jnp.concatenate(
        [from_behind(pair, "ctx", step) for step in range(SPAN, 0, -1)] + [pair], axis=0
    )
    first = jnp.concatenate([state_rows, factor_rows], axis=0)
    got = lax.ppermute(first, "ctx", [(i, i ^ 1) for i in range(count)])
    state_mate = got[:n_state]
    factor_mate = got[n_state, :heads_here]
    state_cube = state_rows.reshape(state.shape)
    mate_cube = state_mate.reshape(state.shape)
    chip_state = jnp.where(
        odd,
        shrinkage_multiplier[:, None, None] * mate_cube + state_cube,
        factor_mate[:, None, None] * state_cube + mate_cube,
    )
    chip_factor = shrinkage_multiplier * factor_mate
    chip_top = chip_factor.astype(jnp.bfloat16)
    chip_rest = (chip_factor - chip_top.astype(jnp.float32)).astype(jnp.bfloat16)
    chip_rows = jnp.pad(jnp.stack([chip_top, chip_rest]), ((0, 14), (0, DH - heads_here)))
    packet = jnp.concatenate(
        [chip_state.astype(jnp.bfloat16).reshape(n_state, DH), chip_rows], axis=0
    )
    routes = [(i, i + 1) for i in range(1, count - 1, 2)] + [(i, i + 5) for i in range(0, count - 5, 2)]
    packet, soft_q = lax.optimization_barrier((packet, soft_q))
    received = lax.ppermute(packet, "ctx", routes)
    span_rows = (SPAN + 1) * rows
    key_pos = shard * rows - SPAN * rows + jnp.arange(span_rows, dtype=jnp.int32)
    key_docs = jnp.where(key_pos >= 0, document_of(key_pos, doc_lengths), -1)
    allowed = (key_docs[None, :] == docs[:, None]) & (key_pos[None, :] <= positions[:, None])
    soft_query = soft_q.reshape(rows, kv_here, group, DH)
    all_keys = window[:, :kv_width].reshape(span_rows, kv_here, DH)
    all_values = window[:, kv_width:].reshape(span_rows, kv_here, DH)
    scores = jnp.einsum(
        "tkgd,skd->kgts", soft_query, all_keys, preferred_element_type=jnp.float32
    ) * DH ** (-0.5)
    top = jnp.max(jnp.where(allowed, scores, -1e30), axis=-1, keepdims=True)
    expd = jnp.where(allowed, jnp.exp(jnp.minimum(scores - top, 0.0)), 0.0)
    total = jnp.sum(expd, axis=-1)
    attended = jnp.einsum(
        "kgts,skd->tkgd", expd.astype(jnp.bfloat16), all_values, preferred_element_type=jnp.float32
    )
    attended = attended / total.transpose(2, 0, 1)[..., None]
    soft_out = attended.reshape(rows, kv_here * group * DH).astype(jnp.bfloat16)
    soft_out, received = lax.optimization_barrier((soft_out, received))
    mate_packet = lax.ppermute(received, "ctx", [(i, i ^ 1) for i in range(count)])
    near = jnp.where(odd, mate_packet, received)
    far = jnp.where(odd, received, mate_packet)

    def unpack(got_packet):
        chip = got_packet[:n_state].reshape(state.shape).astype(jnp.float32)
        mult = got_packet[n_state, :heads_here].astype(jnp.float32) + got_packet[
            n_state + 1, :heads_here
        ].astype(jnp.float32)
        return chip, mult

    state_near, factor_near = unpack(near)
    state_far, _ = unpack(far)
    incoming_even = state_near + factor_near[:, None, None] * state_far
    incoming = jnp.where(odd, factor_mate[:, None, None] * incoming_even + mate_cube, incoming_even)
    incoming_b = incoming.astype(jnp.bfloat16)
    outer = jnp.einsum(
        "thd,hde->the", query, incoming_b, preferred_element_type=jnp.float32
    )
    outer = outer * (jnp.exp(level).T * carried[:, None].astype(jnp.float32))[:, :, None]
    mixed = inner + outer
    local_sq = jnp.sum(mixed * mixed, axis=(1, 2))
    total_sq = all_sum(local_sq, "head")
    mean_sq = total_sq / (lax.axis_size("head") * heads_here * DH)
    flat = mixed.reshape(rows, heads_here * DH)
    normed = (
        flat
        * lax.rsqrt(mean_sq + 1e-06)[:, None]
        * lin_gain[None, :]
        * jax.nn.sigmoid(out_gate.astype(jnp.float32))
    )
    lin_out = normed.astype(jnp.bfloat16)
    return (lin_out, soft_out)


def solution(mesh):
    in_specs = (
        P(),
        P("ctx", "head"),
        P("ctx", "head"),
        P("ctx", "head"),
        P("head", "ctx"),
        P("ctx", "head"),
        P("head"),
        P("ctx", "head"),
        P("ctx", "head"),
        P("ctx", "head"),
    )
    out_specs = (P("ctx", "head"), P("ctx", "head"))
    return jax.shard_map(local, mesh=mesh, in_specs=in_specs, out_specs=out_specs, check_vma=False)
```

```python
import jax
import jax.numpy as jnp
from jax import lax
from jax.sharding import PartitionSpec as P

DH = 128
SPAN = 4


def from_behind(shard, axis, by):
    count = lax.axis_size(axis)
    pairs = [(i, i + by) for i in range(count) if 0 <= i + by < count]
    return lax.ppermute(shard, axis, pairs)


def all_sum(x, axis):
    count = lax.axis_size(axis)
    if count & (count - 1):
        me = lax.axis_index(axis)
        parts = [x]
        for by in range(1, count):
            parts.append(lax.ppermute(x, axis, [(i, (i + by) % count) for i in range(count)]))
        stacked = jnp.stack(parts)
        order = (me - jnp.arange(count)) % count
        return jnp.sum(stacked[order], axis=0)
    bit = 1
    while bit < count:
        x = x + lax.ppermute(x, axis, [(i, i ^ bit) for i in range(count)])
        bit *= 2
    return x


def document_of(positions, doc_lengths):
    ends = jnp.cumsum(doc_lengths)
    return jnp.sum((ends[None, :] <= positions[:, None]).astype(jnp.int32), axis=1)


def block_terms(query, lookup_array, values, decay, docs, before, last):
    rows = docs.shape[0]
    level = jnp.cumsum(decay, axis=1)
    order = jnp.arange(rows)
    same = (docs[:, None] == docs[None, :]) & (order[None, :] <= order[:, None])
    scores = jnp.einsum("thd,shd->hts", query, lookup_array, preferred_element_type=jnp.float32)
    fade = jnp.exp(jnp.minimum(level[:, :, None] - level[:, None, :], 0.0))
    weights = jnp.where(same[None], scores * fade, 0.0).astype(jnp.bfloat16)
    inner = jnp.einsum("hts,shd->thd", weights, values, preferred_element_type=jnp.float32)
    carried = docs == before
    closing = (docs == last).astype(jnp.float32)
    tail = jnp.exp(level[:, -1:] - level) * closing[None, :]
    weighted = (lookup_array.astype(jnp.float32) * tail.T[:, :, None]).astype(jnp.bfloat16)
    state = jnp.einsum("shd,she->hde", weighted, values, preferred_element_type=jnp.float32)
    shrinkage_multiplier = jnp.exp(level[:, -1]) * (last == before).astype(jnp.float32)
    return (inner, level, carried, shrinkage_multiplier, state)


def local(doc_lengths, lin_q, lin_k, lin_v, log_decay, out_gate, lin_gain, soft_q, soft_k, soft_v):
    rows = lin_q.shape[0]
    heads_here = lin_q.shape[1] // DH
    kv_here = soft_k.shape[1] // DH
    group = soft_q.shape[1] // (kv_here * DH)
    shard = lax.axis_index("ctx")
    positions = shard * rows + jnp.arange(rows, dtype=jnp.int32)
    ends = jnp.cumsum(doc_lengths)
    docs = jnp.sum((ends[None, :] <= positions[:, None]).astype(jnp.int32), axis=1)
    last = jnp.sum((ends <= shard * rows + rows - 1).astype(jnp.int32))
    before = jnp.where(shard > 0, jnp.sum((ends <= shard * rows - 1).astype(jnp.int32)), -1)
    query = lin_q.reshape(rows, heads_here, DH)
    lookup_array = lin_k.reshape(rows, heads_here, DH)
    values = lin_v.reshape(rows, heads_here, DH)
    inner, level, carried, shrinkage_multiplier, state = block_terms(
        query, lookup_array, values, log_decay, docs, before, last
    )
    count = lax.axis_size("ctx")
    odd = (shard % 2) == 1
    pair = jnp.concatenate([soft_k, soft_v], axis=1)
    kv_width = soft_k.shape[1]
    n_state = heads_here * DH
    state_rows = state.reshape(n_state, DH)
    factor_rows = jnp.pad(shrinkage_multiplier[None, :], ((0, 7), (0, DH - heads_here)))
    pair_mate = lax.ppermute(pair, "ctx", [(i, i ^ 1) for i in range(count)])
    chip_pair = jnp.concatenate(
        [jnp.where(odd, pair_mate, pair), jnp.where(odd, pair, pair_mate)], axis=0
    )
    chip_near = from_behind(chip_pair, "ctx", 2)
    chip_far = from_behind(chip_pair, "ctx", 4)
    window_even = jnp.concatenate([chip_far, chip_near], axis=0)
    window_odd = jnp.concatenate([chip_far[rows:], chip_near, pair_mate], axis=0)
    window = jnp.concatenate([jnp.where(odd, window_odd, window_even), pair], axis=0)
    first = jnp.concatenate([state_rows, factor_rows], axis=0)
    got = lax.ppermute(first, "ctx", [(i, i ^ 1) for i in range(count)])
    state_mate = got[:n_state]
    factor_mate = got[n_state, :heads_here]
    state_cube = state_rows.reshape(state.shape)
    mate_cube = state_mate.reshape(state.shape)
    chip_state = jnp.where(
        odd,
        shrinkage_multiplier[:, None, None] * mate_cube + state_cube,
        factor_mate[:, None, None] * state_cube + mate_cube,
    )
    chip_factor = shrinkage_multiplier * factor_mate
    chip_top = chip_factor.astype(jnp.bfloat16)
    chip_rest = (chip_factor - chip_top.astype(jnp.float32)).astype(jnp.bfloat16)
    chip_rows = jnp.pad(jnp.stack([chip_top, chip_rest]), ((0, 14), (0, DH - heads_here)))
    packet = jnp.concatenate(
        [chip_state.astype(jnp.bfloat16).reshape(n_state, DH), chip_rows], axis=0
    )
    routes = [(i, i + 1) for i in range(1, count - 1, 2)] + [(i, i + 5) for i in range(0, count - 5, 2)]
    packet, soft_q = lax.optimization_barrier((packet, soft_q))
    received = lax.ppermute(packet, "ctx", routes)
    span_rows = (SPAN + 1) * rows
    key_pos = shard * rows - SPAN * rows + jnp.arange(span_rows, dtype=jnp.int32)
    key_docs = jnp.where(key_pos >= 0, document_of(key_pos, doc_lengths), -1)
    allowed = (key_docs[None, :] == docs[:, None]) & (key_pos[None, :] <= positions[:, None])
    soft_query = soft_q.reshape(rows, kv_here, group, DH)
    all_keys = window[:, :kv_width].reshape(span_rows, kv_here, DH)
    all_values = window[:, kv_width:].reshape(span_rows, kv_here, DH)
    scores = jnp.einsum(
        "tkgd,skd->kgts", soft_query, all_keys, preferred_element_type=jnp.float32
    ) * DH ** (-0.5)
    top = jnp.max(jnp.where(allowed, scores, -1e30), axis=-1, keepdims=True)
    expd = jnp.where(allowed, jnp.exp(jnp.minimum(scores - top, 0.0)), 0.0)
    total = jnp.sum(expd, axis=-1)
    attended = jnp.einsum(
        "kgts,skd->tkgd", expd.astype(jnp.bfloat16), all_values, preferred_element_type=jnp.float32
    )
    attended = attended / total.transpose(2, 0, 1)[..., None]
    soft_out = attended.reshape(rows, kv_here * group * DH).astype(jnp.bfloat16)
    soft_out, received = lax.optimization_barrier((soft_out, received))
    mate_packet = lax.ppermute(received, "ctx", [(i, i ^ 1) for i in range(count)])
    near = jnp.where(odd, mate_packet, received)
    far = jnp.where(odd, received, mate_packet)

    def unpack(got_packet):
        chip = got_packet[:n_state].reshape(state.shape).astype(jnp.float32)
        mult = got_packet[n_state, :heads_here].astype(jnp.float32) + got_packet[
            n_state + 1, :heads_here
        ].astype(jnp.float32)
        return chip, mult

    state_near, factor_near = unpack(near)
    state_far, _ = unpack(far)
    incoming_even = state_near + factor_near[:, None, None] * state_far
    incoming = jnp.where(odd, factor_mate[:, None, None] * incoming_even + mate_cube, incoming_even)
    incoming_b = incoming.astype(jnp.bfloat16)
    outer = jnp.einsum(
        "thd,hde->the", query, incoming_b, preferred_element_type=jnp.float32
    )
    outer = outer * (jnp.exp(level).T * carried[:, None].astype(jnp.float32))[:, :, None]
    mixed = inner + outer
    local_sq = jnp.sum(mixed * mixed, axis=(1, 2))
    total_sq = all_sum(local_sq, "head")
    mean_sq = total_sq / (lax.axis_size("head") * heads_here * DH)
    flat = mixed.reshape(rows, heads_here * DH)
    normed = (
        flat
        * lax.rsqrt(mean_sq + 1e-06)[:, None]
        * lin_gain[None, :]
        * jax.nn.sigmoid(out_gate.astype(jnp.float32))
    )
    lin_out = normed.astype(jnp.bfloat16)
    return (lin_out, soft_out)


def solution(mesh):
    in_specs = (
        P(),
        P("ctx", "head"),
        P("ctx", "head"),
        P("ctx", "head"),
        P("head", "ctx"),
        P("ctx", "head"),
        P("head"),
        P("ctx", "head"),
        P("ctx", "head"),
        P("ctx", "head"),
    )
    out_specs = (P("ctx", "head"), P("ctx", "head"))
    return jax.shard_map(local, mesh=mesh, in_specs=in_specs, out_specs=out_specs, check_vma=False)
```

```python
import jax
import jax.numpy as jnp
from jax import lax
from jax.sharding import PartitionSpec as P

DH = 128
SPAN = 4


def from_behind(shard, axis, by):
    count = lax.axis_size(axis)
    pairs = [(i, i + by) for i in range(count) if 0 <= i + by < count]
    return lax.ppermute(shard, axis, pairs)


def all_sum(x, axis):
    count = lax.axis_size(axis)
    if count & (count - 1):
        me = lax.axis_index(axis)
        parts = [x]
        for by in range(1, count):
            parts.append(lax.ppermute(x, axis, [(i, (i + by) % count) for i in range(count)]))
        stacked = jnp.stack(parts)
        order = (me - jnp.arange(count)) % count
        return jnp.sum(stacked[order], axis=0)
    bit = 1
    while bit < count:
        x = x + lax.ppermute(x, axis, [(i, i ^ bit) for i in range(count)])
        bit *= 2
    return x


def document_of(positions, doc_lengths):
    ends = jnp.cumsum(doc_lengths)
    return jnp.sum((ends[None, :] <= positions[:, None]).astype(jnp.int32), axis=1)


def block_terms(query, lookup_array, values, decay, docs, before, last):
    rows = docs.shape[0]
    span = decay.shape[1]
    upto = (jnp.arange(span)[:, None] <= jnp.arange(span)[None, :]).astype(jnp.float32)
    level = jnp.dot(decay, upto, precision=lax.Precision.HIGHEST)
    order = jnp.arange(rows)
    same = (docs[:, None] == docs[None, :]) & (order[None, :] <= order[:, None])
    scores = jnp.einsum("thd,shd->hts", query, lookup_array, preferred_element_type=jnp.float32)
    fade = jnp.exp(jnp.minimum(level[:, :, None] - level[:, None, :], 0.0))
    weights = jnp.where(same[None], scores * fade, 0.0).astype(jnp.bfloat16)
    inner = jnp.einsum("hts,shd->thd", weights, values, preferred_element_type=jnp.float32)
    carried = docs == before
    closing = (docs == last).astype(jnp.float32)
    tail = jnp.exp(level[:, -1:] - level) * closing[None, :]
    weighted = (lookup_array.astype(jnp.float32) * tail.T[:, :, None]).astype(jnp.bfloat16)
    state = jnp.einsum("shd,she->hde", weighted, values, preferred_element_type=jnp.float32)
    shrinkage_multiplier = jnp.exp(level[:, -1]) * (last == before).astype(jnp.float32)
    return (inner, level, carried, shrinkage_multiplier, state)


def local(doc_lengths, lin_q, lin_k, lin_v, log_decay, out_gate, lin_gain, soft_q, soft_k, soft_v):
    rows = lin_q.shape[0]
    heads_here = lin_q.shape[1] // DH
    kv_here = soft_k.shape[1] // DH
    group = soft_q.shape[1] // (kv_here * DH)
    shard = lax.axis_index("ctx")
    positions = shard * rows + jnp.arange(rows, dtype=jnp.int32)
    ends = jnp.cumsum(doc_lengths)
    docs = jnp.sum((ends[None, :] <= positions[:, None]).astype(jnp.int32), axis=1)
    last = jnp.sum((ends <= shard * rows + rows - 1).astype(jnp.int32))
    before = jnp.where(shard > 0, jnp.sum((ends <= shard * rows - 1).astype(jnp.int32)), -1)
    query = lin_q.reshape(rows, heads_here, DH)
    lookup_array = lin_k.reshape(rows, heads_here, DH)
    values = lin_v.reshape(rows, heads_here, DH)
    inner, level, carried, shrinkage_multiplier, state = block_terms(
        query, lookup_array, values, log_decay, docs, before, last
    )
    count = lax.axis_size("ctx")
    odd = (shard % 2) == 1
    pair = jnp.concatenate([soft_k, soft_v], axis=1)
    kv_width = soft_k.shape[1]
    n_state = heads_here * DH
    state_rows = state.reshape(n_state, DH)
    factor_rows = jnp.pad(shrinkage_multiplier[None, :], ((0, 7), (0, DH - heads_here)))
    window = jnp.concatenate(
        [from_behind(pair, "ctx", step) for step in range(SPAN, 0, -1)] + [pair], axis=0
    )
    first = jnp.concatenate([state_rows, factor_rows], axis=0)
    got = lax.ppermute(first, "ctx", [(i, i ^ 1) for i in range(count)])
    state_mate = got[:n_state]
    factor_mate = got[n_state, :heads_here]
    state_cube = state_rows.reshape(state.shape)
    mate_cube = state_mate.reshape(state.shape)
    chip_state = jnp.where(
        odd,
        shrinkage_multiplier[:, None, None] * mate_cube + state_cube,
        factor_mate[:, None, None] * state_cube + mate_cube,
    )
    chip_factor = shrinkage_multiplier * factor_mate
    chip_top = chip_factor.astype(jnp.bfloat16)
    chip_rest = (chip_factor - chip_top.astype(jnp.float32)).astype(jnp.bfloat16)
    chip_rows = jnp.pad(jnp.stack([chip_top, chip_rest]), ((0, 14), (0, DH - heads_here)))
    packet = jnp.concatenate(
        [chip_state.astype(jnp.bfloat16).reshape(n_state, DH), chip_rows], axis=0
    )
    routes = [(i, i + 1) for i in range(1, count - 1, 2)] + [(i, i + 5) for i in range(0, count - 5, 2)]
    packet, soft_q = lax.optimization_barrier((packet, soft_q))
    received = lax.ppermute(packet, "ctx", routes)
    span_rows = (SPAN + 1) * rows
    key_pos = shard * rows - SPAN * rows + jnp.arange(span_rows, dtype=jnp.int32)
    key_docs = jnp.where(key_pos >= 0, document_of(key_pos, doc_lengths), -1)
    allowed = (key_docs[None, :] == docs[:, None]) & (key_pos[None, :] <= positions[:, None])
    soft_query = soft_q.reshape(rows, kv_here, group, DH)
    all_keys = window[:, :kv_width].reshape(span_rows, kv_here, DH)
    all_values = window[:, kv_width:].reshape(span_rows, kv_here, DH)
    scores = jnp.einsum(
        "tkgd,skd->kgts", soft_query, all_keys, preferred_element_type=jnp.float32
    ) * DH ** (-0.5)
    top = jnp.max(jnp.where(allowed, scores, -1e30), axis=-1, keepdims=True)
    expd = jnp.where(allowed, jnp.exp(jnp.minimum(scores - top, 0.0)), 0.0)
    total = jnp.sum(expd, axis=-1)
    attended = jnp.einsum(
        "kgts,skd->tkgd", expd.astype(jnp.bfloat16), all_values, preferred_element_type=jnp.float32
    )
    attended = attended / total.transpose(2, 0, 1)[..., None]
    soft_out = attended.reshape(rows, kv_here * group * DH).astype(jnp.bfloat16)
    soft_out, received = lax.optimization_barrier((soft_out, received))
    mate_packet = lax.ppermute(received, "ctx", [(i, i ^ 1) for i in range(count)])
    near = jnp.where(odd, mate_packet, received)
    far = jnp.where(odd, received, mate_packet)

    def unpack(got_packet):
        chip = got_packet[:n_state].reshape(state.shape).astype(jnp.float32)
        mult = got_packet[n_state, :heads_here].astype(jnp.float32) + got_packet[
            n_state + 1, :heads_here
        ].astype(jnp.float32)
        return chip, mult

    state_near, factor_near = unpack(near)
    state_far, _ = unpack(far)
    incoming_even = state_near + factor_near[:, None, None] * state_far
    incoming = jnp.where(odd, factor_mate[:, None, None] * incoming_even + mate_cube, incoming_even)
    incoming_b = incoming.astype(jnp.bfloat16)
    outer = jnp.einsum(
        "thd,hde->the", query, incoming_b, preferred_element_type=jnp.float32
    )
    outer = outer * (jnp.exp(level).T * carried[:, None].astype(jnp.float32))[:, :, None]
    mixed = inner + outer
    local_sq = jnp.sum(mixed * mixed, axis=(1, 2))
    total_sq = all_sum(local_sq, "head")
    mean_sq = total_sq / (lax.axis_size("head") * heads_here * DH)
    flat = mixed.reshape(rows, heads_here * DH)
    normed = (
        flat
        * lax.rsqrt(mean_sq + 1e-06)[:, None]
        * lin_gain[None, :]
        * jax.nn.sigmoid(out_gate.astype(jnp.float32))
    )
    lin_out = normed.astype(jnp.bfloat16)
    return (lin_out, soft_out)


def solution(mesh):
    in_specs = (
        P(),
        P("ctx", "head"),
        P("ctx", "head"),
        P("ctx", "head"),
        P("head", "ctx"),
        P("ctx", "head"),
        P("head"),
        P("ctx", "head"),
        P("ctx", "head"),
        P("ctx", "head"),
    )
    out_specs = (P("ctx", "head"), P("ctx", "head"))
    return jax.shard_map(local, mesh=mesh, in_specs=in_specs, out_specs=out_specs, check_vma=False)
```

```python
import jax
import jax.numpy as jnp
from jax import lax
from jax.sharding import PartitionSpec as P

DH = 128
SPAN = 4


def from_behind(shard, axis, by):
    count = lax.axis_size(axis)
    pairs = [(i, i + by) for i in range(count) if 0 <= i + by < count]
    return lax.ppermute(shard, axis, pairs)


def all_sum(x, axis):
    count = lax.axis_size(axis)
    if count & (count - 1):
        me = lax.axis_index(axis)
        parts = [x]
        for by in range(1, count):
            parts.append(lax.ppermute(x, axis, [(i, (i + by) % count) for i in range(count)]))
        stacked = jnp.stack(parts)
        order = (me - jnp.arange(count)) % count
        return jnp.sum(stacked[order], axis=0)
    bit = 1
    while bit < count:
        x = x + lax.ppermute(x, axis, [(i, i ^ bit) for i in range(count)])
        bit *= 2
    return x


def document_of(positions, doc_lengths):
    ends = jnp.cumsum(doc_lengths)
    return jnp.sum((ends[None, :] <= positions[:, None]).astype(jnp.int32), axis=1)


def block_terms(query, lookup_array, values, decay, docs, before, last):
    rows = docs.shape[0]
    level = jnp.cumsum(decay, axis=1)
    order = jnp.arange(rows)
    same = (docs[:, None] == docs[None, :]) & (order[None, :] <= order[:, None])
    scores = jnp.einsum("thd,shd->hts", query, lookup_array, preferred_element_type=jnp.float32)
    fade = jnp.exp(jnp.minimum(level[:, :, None] - level[:, None, :], 0.0))
    weights = jnp.where(same[None], scores * fade, 0.0).astype(jnp.bfloat16)
    inner = jnp.einsum("hts,shd->thd", weights, values, preferred_element_type=jnp.float32)
    carried = docs == before
    closing = (docs == last).astype(jnp.float32)
    tail = jnp.exp(level[:, -1:] - level) * closing[None, :]
    weighted = (lookup_array.astype(jnp.float32) * tail.T[:, :, None]).astype(jnp.bfloat16)
    state = jnp.einsum("shd,she->hde", weighted, values, preferred_element_type=jnp.float32)
    shrinkage_multiplier = jnp.exp(level[:, -1]) * (last == before).astype(jnp.float32)
    return (inner, level, carried, shrinkage_multiplier, state)


def local(doc_lengths, lin_q, lin_k, lin_v, log_decay, out_gate, lin_gain, soft_q, soft_k, soft_v):
    rows = lin_q.shape[0]
    heads_here = lin_q.shape[1] // DH
    kv_here = soft_k.shape[1] // DH
    group = soft_q.shape[1] // (kv_here * DH)
    shard = lax.axis_index("ctx")
    positions = shard * rows + jnp.arange(rows, dtype=jnp.int32)
    ends = jnp.cumsum(doc_lengths)
    docs = jnp.sum((ends[None, :] <= positions[:, None]).astype(jnp.int32), axis=1)
    last = jnp.sum((ends <= shard * rows + rows - 1).astype(jnp.int32))
    before = jnp.where(shard > 0, jnp.sum((ends <= shard * rows - 1).astype(jnp.int32)), -1)
    query = lin_q.reshape(rows, heads_here, DH)
    lookup_array = lin_k.reshape(rows, heads_here, DH)
    values = lin_v.reshape(rows, heads_here, DH)
    inner, level, carried, shrinkage_multiplier, state = block_terms(
        query, lookup_array, values, log_decay, docs, before, last
    )
    count = lax.axis_size("ctx")
    odd = (shard % 2) == 1
    pair = jnp.concatenate([soft_k, soft_v], axis=0)
    kv_width = soft_k.shape[1]
    n_state = heads_here * DH
    state_rows = state.reshape(n_state, DH)
    factor_rows = jnp.pad(shrinkage_multiplier[None, :], ((0, 7), (0, DH - heads_here)))
    window = jnp.concatenate(
        [from_behind(pair, "ctx", step) for step in range(SPAN, 0, -1)] + [pair], axis=0
    )
    first = jnp.concatenate([state_rows, factor_rows], axis=0)
    got = lax.ppermute(first, "ctx", [(i, i ^ 1) for i in range(count)])
    state_mate = got[:n_state]
    factor_mate = got[n_state, :heads_here]
    state_cube = state_rows.reshape(state.shape)
    mate_cube = state_mate.reshape(state.shape)
    chip_state = jnp.where(
        odd,
        shrinkage_multiplier[:, None, None] * mate_cube + state_cube,
        factor_mate[:, None, None] * state_cube + mate_cube,
    )
    chip_factor = shrinkage_multiplier * factor_mate
    chip_top = chip_factor.astype(jnp.bfloat16)
    chip_rest = (chip_factor - chip_top.astype(jnp.float32)).astype(jnp.bfloat16)
    chip_rows = jnp.pad(jnp.stack([chip_top, chip_rest]), ((0, 14), (0, DH - heads_here)))
    packet = jnp.concatenate(
        [chip_state.astype(jnp.bfloat16).reshape(n_state, DH), chip_rows], axis=0
    )
    routes = [(i, i + 1) for i in range(1, count - 1, 2)] + [(i, i + 5) for i in range(0, count - 5, 2)]
    packet, soft_q = lax.optimization_barrier((packet, soft_q))
    received = lax.ppermute(packet, "ctx", routes)
    span_rows = (SPAN + 1) * rows
    key_pos = shard * rows - SPAN * rows + jnp.arange(span_rows, dtype=jnp.int32)
    key_docs = jnp.where(key_pos >= 0, document_of(key_pos, doc_lengths), -1)
    allowed = (key_docs[None, :] == docs[:, None]) & (key_pos[None, :] <= positions[:, None])
    soft_query = soft_q.reshape(rows, kv_here, group, DH)
    paired = window.reshape(SPAN + 1, 2, rows, kv_width)
    all_keys = paired[:, 0].reshape(span_rows, kv_here, DH)
    all_values = paired[:, 1].reshape(span_rows, kv_here, DH)
    scores = jnp.einsum(
        "tkgd,skd->kgts", soft_query, all_keys, preferred_element_type=jnp.float32
    ) * DH ** (-0.5)
    top = jnp.max(jnp.where(allowed, scores, -1e30), axis=-1, keepdims=True)
    expd = jnp.where(allowed, jnp.exp(jnp.minimum(scores - top, 0.0)), 0.0)
    total = jnp.sum(expd, axis=-1)
    attended = jnp.einsum(
        "kgts,skd->tkgd", expd.astype(jnp.bfloat16), all_values, preferred_element_type=jnp.float32
    )
    attended = attended / total.transpose(2, 0, 1)[..., None]
    soft_out = attended.reshape(rows, kv_here * group * DH).astype(jnp.bfloat16)
    soft_out, received = lax.optimization_barrier((soft_out, received))
    mate_packet = lax.ppermute(received, "ctx", [(i, i ^ 1) for i in range(count)])
    near = jnp.where(odd, mate_packet, received)
    far = jnp.where(odd, received, mate_packet)

    def unpack(got_packet):
        chip = got_packet[:n_state].reshape(state.shape).astype(jnp.float32)
        mult = got_packet[n_state, :heads_here].astype(jnp.float32) + got_packet[
            n_state + 1, :heads_here
        ].astype(jnp.float32)
        return chip, mult

    state_near, factor_near = unpack(near)
    state_far, _ = unpack(far)
    incoming_even = state_near + factor_near[:, None, None] * state_far
    incoming = jnp.where(odd, factor_mate[:, None, None] * incoming_even + mate_cube, incoming_even)
    incoming_b = incoming.astype(jnp.bfloat16)
    outer = jnp.einsum(
        "thd,hde->the", query, incoming_b, preferred_element_type=jnp.float32
    )
    outer = outer * (jnp.exp(level).T * carried[:, None].astype(jnp.float32))[:, :, None]
    mixed = inner + outer
    local_sq = jnp.sum(mixed * mixed, axis=(1, 2))
    total_sq = all_sum(local_sq, "head")
    mean_sq = total_sq / (lax.axis_size("head") * heads_here * DH)
    flat = mixed.reshape(rows, heads_here * DH)
    normed = (
        flat
        * lax.rsqrt(mean_sq + 1e-06)[:, None]
        * lin_gain[None, :]
        * jax.nn.sigmoid(out_gate.astype(jnp.float32))
    )
    lin_out = normed.astype(jnp.bfloat16)
    return (lin_out, soft_out)


def solution(mesh):
    in_specs = (
        P(),
        P("ctx", "head"),
        P("ctx", "head"),
        P("ctx", "head"),
        P("head", "ctx"),
        P("ctx", "head"),
        P("head"),
        P("ctx", "head"),
        P("ctx", "head"),
        P("ctx", "head"),
    )
    out_specs = (P("ctx", "head"), P("ctx", "head"))
    return jax.shard_map(local, mesh=mesh, in_specs=in_specs, out_specs=out_specs, check_vma=False)
```

```python
import jax
import jax.numpy as jnp
from jax import lax
from jax.sharding import PartitionSpec as P

DH = 128
SPAN = 4


def from_behind(shard, axis, by):
    count = lax.axis_size(axis)
    pairs = [(i, i + by) for i in range(count) if 0 <= i + by < count]
    return lax.ppermute(shard, axis, pairs)


def all_sum(x, axis):
    count = lax.axis_size(axis)
    if count & (count - 1):
        me = lax.axis_index(axis)
        parts = [x]
        for by in range(1, count):
            parts.append(lax.ppermute(x, axis, [(i, (i + by) % count) for i in range(count)]))
        stacked = jnp.stack(parts)
        order = (me - jnp.arange(count)) % count
        return jnp.sum(stacked[order], axis=0)
    bit = 1
    while bit < count:
        x = x + lax.ppermute(x, axis, [(i, i ^ bit) for i in range(count)])
        bit *= 2
    return x


def document_of(positions, doc_lengths):
    ends = jnp.cumsum(doc_lengths)
    return jnp.sum((ends[None, :] <= positions[:, None]).astype(jnp.int32), axis=1)


def block_terms(query, lookup_array, values, decay, docs, before, last):
    rows = docs.shape[0]
    span = decay.shape[1]
    upto = (jnp.arange(span)[:, None] <= jnp.arange(span)[None, :]).astype(jnp.float32)
    level = jnp.dot(decay, upto, precision=lax.Precision.HIGHEST)
    order = jnp.arange(rows)
    same = (docs[:, None] == docs[None, :]) & (order[None, :] <= order[:, None])
    scores = jnp.einsum("thd,shd->hts", query, lookup_array, preferred_element_type=jnp.float32)
    fade = jnp.exp(jnp.minimum(level[:, :, None] - level[:, None, :], 0.0))
    weights = jnp.where(same[None], scores * fade, 0.0).astype(jnp.bfloat16)
    inner = jnp.einsum("hts,shd->thd", weights, values, preferred_element_type=jnp.float32)
    carried = docs == before
    closing = (docs == last).astype(jnp.float32)
    tail = jnp.exp(level[:, -1:] - level) * closing[None, :]
    weighted = (lookup_array.astype(jnp.float32) * tail.T[:, :, None]).astype(jnp.bfloat16)
    state = jnp.einsum("shd,she->hde", weighted, values, preferred_element_type=jnp.float32)
    shrinkage_multiplier = jnp.exp(level[:, -1]) * (last == before).astype(jnp.float32)
    return (inner, level, carried, shrinkage_multiplier, state)


def local(doc_lengths, lin_q, lin_k, lin_v, log_decay, out_gate, lin_gain, soft_q, soft_k, soft_v):
    rows = lin_q.shape[0]
    heads_here = lin_q.shape[1] // DH
    kv_here = soft_k.shape[1] // DH
    group = soft_q.shape[1] // (kv_here * DH)
    shard = lax.axis_index("ctx")
    positions = shard * rows + jnp.arange(rows, dtype=jnp.int32)
    ends = jnp.cumsum(doc_lengths)
    docs = jnp.sum((ends[None, :] <= positions[:, None]).astype(jnp.int32), axis=1)
    last = jnp.sum((ends <= shard * rows + rows - 1).astype(jnp.int32))
    before = jnp.where(shard > 0, jnp.sum((ends <= shard * rows - 1).astype(jnp.int32)), -1)
    query = lin_q.reshape(rows, heads_here, DH)
    lookup_array = lin_k.reshape(rows, heads_here, DH)
    values = lin_v.reshape(rows, heads_here, DH)
    inner, level, carried, shrinkage_multiplier, state = block_terms(
        query, lookup_array, values, log_decay, docs, before, last
    )
    count = lax.axis_size("ctx")
    odd = (shard % 2) == 1
    pair = jnp.concatenate([soft_k, soft_v], axis=0)
    kv_width = soft_k.shape[1]
    n_state = heads_here * DH
    state_rows = state.reshape(n_state, DH)
    factor_rows = jnp.pad(shrinkage_multiplier[None, :], ((0, 7), (0, DH - heads_here)))
    window = jnp.concatenate(
        [from_behind(pair, "ctx", step) for step in range(SPAN, 0, -1)] + [pair], axis=0
    )
    first = jnp.concatenate([state_rows, factor_rows], axis=0)
    got = lax.ppermute(first, "ctx", [(i, i ^ 1) for i in range(count)])
    state_mate = got[:n_state]
    factor_mate = got[n_state, :heads_here]
    state_cube = state_rows.reshape(state.shape)
    mate_cube = state_mate.reshape(state.shape)
    chip_state = jnp.where(
        odd,
        shrinkage_multiplier[:, None, None] * mate_cube + state_cube,
        factor_mate[:, None, None] * state_cube + mate_cube,
    )
    chip_factor = shrinkage_multiplier * factor_mate
    chip_top = chip_factor.astype(jnp.bfloat16)
    chip_rest = (chip_factor - chip_top.astype(jnp.float32)).astype(jnp.bfloat16)
    chip_rows = jnp.pad(jnp.stack([chip_top, chip_rest]), ((0, 14), (0, DH - heads_here)))
    packet = jnp.concatenate(
        [chip_state.astype(jnp.bfloat16).reshape(n_state, DH), chip_rows], axis=0
    )
    routes = [(i, i + 1) for i in range(1, count - 1, 2)] + [(i, i + 5) for i in range(0, count - 5, 2)]
    packet, soft_q = lax.optimization_barrier((packet, soft_q))
    received = lax.ppermute(packet, "ctx", routes)
    span_rows = (SPAN + 1) * rows
    key_pos = shard * rows - SPAN * rows + jnp.arange(span_rows, dtype=jnp.int32)
    key_docs = jnp.where(key_pos >= 0, document_of(key_pos, doc_lengths), -1)
    allowed = (key_docs[None, :] == docs[:, None]) & (key_pos[None, :] <= positions[:, None])
    soft_query = soft_q.reshape(rows, kv_here, group, DH)
    paired = window.reshape(SPAN + 1, 2, rows, kv_width)
    all_keys = paired[:, 0].reshape(span_rows, kv_here, DH)
    all_values = paired[:, 1].reshape(span_rows, kv_here, DH)
    scores = jnp.einsum(
        "tkgd,skd->kgts", soft_query, all_keys, preferred_element_type=jnp.float32
    ) * DH ** (-0.5)
    top = jnp.max(jnp.where(allowed, scores, -1e30), axis=-1, keepdims=True)
    expd = jnp.where(allowed, jnp.exp(jnp.minimum(scores - top, 0.0)), 0.0)
    total = jnp.sum(expd, axis=-1)
    attended = jnp.einsum(
        "kgts,skd->tkgd", expd.astype(jnp.bfloat16), all_values, preferred_element_type=jnp.float32
    )
    attended = attended / total.transpose(2, 0, 1)[..., None]
    soft_out = attended.reshape(rows, kv_here * group * DH).astype(jnp.bfloat16)
    soft_out, received = lax.optimization_barrier((soft_out, received))
    mate_packet = lax.ppermute(received, "ctx", [(i, i ^ 1) for i in range(count)])
    near = jnp.where(odd, mate_packet, received)
    far = jnp.where(odd, received, mate_packet)

    def unpack(got_packet):
        chip = got_packet[:n_state].reshape(state.shape).astype(jnp.float32)
        mult = got_packet[n_state, :heads_here].astype(jnp.float32) + got_packet[
            n_state + 1, :heads_here
        ].astype(jnp.float32)
        return chip, mult

    state_near, factor_near = unpack(near)
    state_far, _ = unpack(far)
    incoming_even = state_near + factor_near[:, None, None] * state_far
    incoming = jnp.where(odd, factor_mate[:, None, None] * incoming_even + mate_cube, incoming_even)
    incoming_b = incoming.astype(jnp.bfloat16)
    outer = jnp.einsum(
        "thd,hde->the", query, incoming_b, preferred_element_type=jnp.float32
    )
    outer = outer * (jnp.exp(level).T * carried[:, None].astype(jnp.float32))[:, :, None]
    mixed = inner + outer
    local_sq = jnp.sum(mixed * mixed, axis=(1, 2))
    total_sq = all_sum(local_sq, "head")
    mean_sq = total_sq / (lax.axis_size("head") * heads_here * DH)
    flat = mixed.reshape(rows, heads_here * DH)
    normed = (
        flat
        * lax.rsqrt(mean_sq + 1e-06)[:, None]
        * lin_gain[None, :]
        * jax.nn.sigmoid(out_gate.astype(jnp.float32))
    )
    lin_out = normed.astype(jnp.bfloat16)
    return (lin_out, soft_out)


def solution(mesh):
    in_specs = (
        P(),
        P("ctx", "head"),
        P("ctx", "head"),
        P("ctx", "head"),
        P("head", "ctx"),
        P("ctx", "head"),
        P("head"),
        P("ctx", "head"),
        P("ctx", "head"),
        P("ctx", "head"),
    )
    out_specs = (P("ctx", "head"), P("ctx", "head"))
    return jax.shard_map(local, mesh=mesh, in_specs=in_specs, out_specs=out_specs, check_vma=False)
```

```python
import jax
import jax.numpy as jnp
from jax import lax
from jax.sharding import PartitionSpec as P

DH = 128
SPAN = 4


def from_behind(shard, axis, by):
    count = lax.axis_size(axis)
    pairs = [(i, i + by) for i in range(count) if 0 <= i + by < count]
    return lax.ppermute(shard, axis, pairs)


def all_sum(x, axis):
    count = lax.axis_size(axis)
    if count & (count - 1):
        me = lax.axis_index(axis)
        parts = [x]
        for by in range(1, count):
            parts.append(lax.ppermute(x, axis, [(i, (i + by) % count) for i in range(count)]))
        stacked = jnp.stack(parts)
        order = (me - jnp.arange(count)) % count
        return jnp.sum(stacked[order], axis=0)
    bit = 1
    while bit < count:
        x = x + lax.ppermute(x, axis, [(i, i ^ bit) for i in range(count)])
        bit *= 2
    return x


def document_of(positions, doc_lengths):
    ends = jnp.cumsum(doc_lengths)
    return jnp.sum((ends[None, :] <= positions[:, None]).astype(jnp.int32), axis=1)


def block_terms(query, lookup_array, values, decay, docs, before, last):
    rows = docs.shape[0]
    level = jnp.cumsum(decay, axis=1)
    order = jnp.arange(rows)
    same = (docs[:, None] == docs[None, :]) & (order[None, :] <= order[:, None])
    scores = jnp.einsum("thd,shd->hts", query, lookup_array, preferred_element_type=jnp.float32)
    fade = jnp.exp(jnp.minimum(level[:, :, None] - level[:, None, :], 0.0))
    weights = jnp.where(same[None], scores * fade, 0.0).astype(jnp.bfloat16)
    inner = jnp.einsum("hts,shd->thd", weights, values, preferred_element_type=jnp.float32)
    carried = docs == before
    closing = (docs == last).astype(jnp.float32)
    tail = jnp.exp(level[:, -1:] - level) * closing[None, :]
    weighted = (lookup_array.astype(jnp.float32) * tail.T[:, :, None]).astype(jnp.bfloat16)
    state = jnp.einsum("shd,she->hde", weighted, values, preferred_element_type=jnp.float32)
    shrinkage_multiplier = jnp.exp(level[:, -1]) * (last == before).astype(jnp.float32)
    return (inner, level, carried, shrinkage_multiplier, state)


def local(doc_lengths, lin_q, lin_k, lin_v, log_decay, out_gate, lin_gain, soft_q, soft_k, soft_v):
    rows = lin_q.shape[0]
    heads_here = lin_q.shape[1] // DH
    kv_here = soft_k.shape[1] // DH
    group = soft_q.shape[1] // (kv_here * DH)
    shard = lax.axis_index("ctx")
    positions = shard * rows + jnp.arange(rows, dtype=jnp.int32)
    ends = jnp.cumsum(doc_lengths)
    docs = jnp.sum((ends[None, :] <= positions[:, None]).astype(jnp.int32), axis=1)
    last = jnp.sum((ends <= shard * rows + rows - 1).astype(jnp.int32))
    before = jnp.where(shard > 0, jnp.sum((ends <= shard * rows - 1).astype(jnp.int32)), -1)
    query = lin_q.reshape(rows, heads_here, DH)
    lookup_array = lin_k.reshape(rows, heads_here, DH)
    values = lin_v.reshape(rows, heads_here, DH)
    inner, level, carried, shrinkage_multiplier, state = block_terms(
        query, lookup_array, values, log_decay, docs, before, last
    )
    count = lax.axis_size("ctx")
    odd = (shard % 2) == 1
    pair = jnp.stack([soft_k, soft_v])
    kv_width = soft_k.shape[1]
    n_state = heads_here * DH
    state_rows = state.reshape(n_state, DH)
    factor_rows = jnp.pad(shrinkage_multiplier[None, :], ((0, 7), (0, DH - heads_here)))
    window = jnp.concatenate(
        [from_behind(pair, "ctx", step) for step in range(SPAN, 0, -1)] + [pair], axis=0
    )
    first = jnp.concatenate([state_rows, factor_rows], axis=0)
    got = lax.ppermute(first, "ctx", [(i, i ^ 1) for i in range(count)])
    state_mate = got[:n_state]
    factor_mate = got[n_state, :heads_here]
    state_cube = state_rows.reshape(state.shape)
    mate_cube = state_mate.reshape(state.shape)
    chip_state = jnp.where(
        odd,
        shrinkage_multiplier[:, None, None] * mate_cube + state_cube,
        factor_mate[:, None, None] * state_cube + mate_cube,
    )
    chip_factor = shrinkage_multiplier * factor_mate
    chip_top = chip_factor.astype(jnp.bfloat16)
    chip_rest = (chip_factor - chip_top.astype(jnp.float32)).astype(jnp.bfloat16)
    chip_rows = jnp.pad(jnp.stack([chip_top, chip_rest]), ((0, 14), (0, DH - heads_here)))
    packet = jnp.concatenate(
        [chip_state.astype(jnp.bfloat16).reshape(n_state, DH), chip_rows], axis=0
    )
    routes = [(i, i + 1) for i in range(1, count - 1, 2)] + [(i, i + 5) for i in range(0, count - 5, 2)]
    packet, soft_q = lax.optimization_barrier((packet, soft_q))
    received = lax.ppermute(packet, "ctx", routes)
    span_rows = (SPAN + 1) * rows
    key_pos = shard * rows - SPAN * rows + jnp.arange(span_rows, dtype=jnp.int32)
    key_docs = jnp.where(key_pos >= 0, document_of(key_pos, doc_lengths), -1)
    allowed = (key_docs[None, :] == docs[:, None]) & (key_pos[None, :] <= positions[:, None])
    soft_query = soft_q.reshape(rows, kv_here, group, DH)
    paired = window.reshape(SPAN + 1, 2, rows, kv_width)
    all_keys = paired[:, 0].reshape(span_rows, kv_here, DH)
    all_values = paired[:, 1].reshape(span_rows, kv_here, DH)
    scores = jnp.einsum(
        "tkgd,skd->kgts", soft_query, all_keys, preferred_element_type=jnp.float32
    ) * DH ** (-0.5)
    top = jnp.max(jnp.where(allowed, scores, -1e30), axis=-1, keepdims=True)
    expd = jnp.where(allowed, jnp.exp(jnp.minimum(scores - top, 0.0)), 0.0)
    total = jnp.sum(expd, axis=-1)
    attended = jnp.einsum(
        "kgts,skd->tkgd", expd.astype(jnp.bfloat16), all_values, preferred_element_type=jnp.float32
    )
    attended = attended / total.transpose(2, 0, 1)[..., None]
    soft_out = attended.reshape(rows, kv_here * group * DH).astype(jnp.bfloat16)
    soft_out, received = lax.optimization_barrier((soft_out, received))
    mate_packet = lax.ppermute(received, "ctx", [(i, i ^ 1) for i in range(count)])
    near = jnp.where(odd, mate_packet, received)
    far = jnp.where(odd, received, mate_packet)

    def unpack(got_packet):
        chip = got_packet[:n_state].reshape(state.shape).astype(jnp.float32)
        mult = got_packet[n_state, :heads_here].astype(jnp.float32) + got_packet[
            n_state + 1, :heads_here
        ].astype(jnp.float32)
        return chip, mult

    state_near, factor_near = unpack(near)
    state_far, _ = unpack(far)
    incoming_even = state_near + factor_near[:, None, None] * state_far
    incoming = jnp.where(odd, factor_mate[:, None, None] * incoming_even + mate_cube, incoming_even)
    incoming_b = incoming.astype(jnp.bfloat16)
    outer = jnp.einsum(
        "thd,hde->the", query, incoming_b, preferred_element_type=jnp.float32
    )
    outer = outer * (jnp.exp(level).T * carried[:, None].astype(jnp.float32))[:, :, None]
    mixed = inner + outer
    local_sq = jnp.sum(mixed * mixed, axis=(1, 2))
    total_sq = all_sum(local_sq, "head")
    mean_sq = total_sq / (lax.axis_size("head") * heads_here * DH)
    flat = mixed.reshape(rows, heads_here * DH)
    normed = (
        flat
        * lax.rsqrt(mean_sq + 1e-06)[:, None]
        * lin_gain[None, :]
        * jax.nn.sigmoid(out_gate.astype(jnp.float32))
    )
    lin_out = normed.astype(jnp.bfloat16)
    return (lin_out, soft_out)


def solution(mesh):
    in_specs = (
        P(),
        P("ctx", "head"),
        P("ctx", "head"),
        P("ctx", "head"),
        P("head", "ctx"),
        P("ctx", "head"),
        P("head"),
        P("ctx", "head"),
        P("ctx", "head"),
        P("ctx", "head"),
    )
    out_specs = (P("ctx", "head"), P("ctx", "head"))
    return jax.shard_map(local, mesh=mesh, in_specs=in_specs, out_specs=out_specs, check_vma=False)
```

```python
import jax
import jax.numpy as jnp
from jax import lax
from jax.sharding import PartitionSpec as P

DH = 128
SPAN = 4


def from_behind(shard, axis, by):
    count = lax.axis_size(axis)
    pairs = [(i, i + by) for i in range(count) if 0 <= i + by < count]
    return lax.ppermute(shard, axis, pairs)


def all_sum(x, axis):
    count = lax.axis_size(axis)
    if count & (count - 1):
        me = lax.axis_index(axis)
        parts = [x]
        for by in range(1, count):
            parts.append(lax.ppermute(x, axis, [(i, (i + by) % count) for i in range(count)]))
        stacked = jnp.stack(parts)
        order = (me - jnp.arange(count)) % count
        return jnp.sum(stacked[order], axis=0)
    bit = 1
    while bit < count:
        x = x + lax.ppermute(x, axis, [(i, i ^ bit) for i in range(count)])
        bit *= 2
    return x


def document_of(positions, doc_lengths):
    ends = jnp.cumsum(doc_lengths)
    return jnp.sum((ends[None, :] <= positions[:, None]).astype(jnp.int32), axis=1)


def block_terms(query, lookup_array, values, decay, docs, before, last):
    rows = docs.shape[0]
    level = jnp.cumsum(decay, axis=1)
    order = jnp.arange(rows)
    same = (docs[:, None] == docs[None, :]) & (order[None, :] <= order[:, None])
    scores = jnp.einsum("thd,shd->hts", query, lookup_array, preferred_element_type=jnp.float32)
    fade = jnp.exp(jnp.minimum(level[:, :, None] - level[:, None, :], 0.0))
    weights = jnp.where(same[None], scores * fade, 0.0).astype(jnp.bfloat16)
    inner = jnp.einsum("hts,shd->thd", weights, values, preferred_element_type=jnp.float32)
    carried = docs == before
    closing = (docs == last).astype(jnp.float32)
    tail = jnp.exp(level[:, -1:] - level) * closing[None, :]
    weighted = (lookup_array.astype(jnp.float32) * tail.T[:, :, None]).astype(jnp.bfloat16)
    state = jnp.einsum("shd,she->hde", weighted, values, preferred_element_type=jnp.float32)
    shrinkage_multiplier = jnp.exp(level[:, -1]) * (last == before).astype(jnp.float32)
    return (inner, level, carried, shrinkage_multiplier, state)


def local(doc_lengths, lin_q, lin_k, lin_v, log_decay, out_gate, lin_gain, soft_q, soft_k, soft_v):
    rows = lin_q.shape[0]
    heads_here = lin_q.shape[1] // DH
    kv_here = soft_k.shape[1] // DH
    group = soft_q.shape[1] // (kv_here * DH)
    shard = lax.axis_index("ctx")
    positions = shard * rows + jnp.arange(rows, dtype=jnp.int32)
    ends = jnp.cumsum(doc_lengths)
    docs = jnp.sum((ends[None, :] <= positions[:, None]).astype(jnp.int32), axis=1)
    last = jnp.sum((ends <= shard * rows + rows - 1).astype(jnp.int32))
    before = jnp.where(shard > 0, jnp.sum((ends <= shard * rows - 1).astype(jnp.int32)), -1)
    query = lin_q.reshape(rows, heads_here, DH)
    lookup_array = lin_k.reshape(rows, heads_here, DH)
    values = lin_v.reshape(rows, heads_here, DH)
    inner, level, carried, shrinkage_multiplier, state = block_terms(
        query, lookup_array, values, log_decay, docs, before, last
    )
    count = lax.axis_size("ctx")
    odd = (shard % 2) == 1
    pair = jnp.stack([soft_k, soft_v])
    kv_width = soft_k.shape[1]
    n_state = heads_here * DH
    state_rows = state.reshape(n_state, DH)
    decay_mate = lax.ppermute(log_decay, "ctx", [(i, i ^ 1) for i in range(count)])
    mate_start = (shard ^ 1) * rows
    mate_last = jnp.sum((ends <= mate_start + rows - 1).astype(jnp.int32))
    mate_before = jnp.where(mate_start > 0, jnp.sum((ends <= mate_start - 1).astype(jnp.int32)), -1)
    factor_mate = jnp.exp(jnp.cumsum(decay_mate, axis=1)[:, -1]) * (mate_last == mate_before).astype(
        jnp.float32
    )
    window = jnp.concatenate(
        [from_behind(pair, "ctx", step) for step in range(SPAN, 0, -1)] + [pair], axis=0
    )
    state_mate = lax.ppermute(state_rows, "ctx", [(i, i ^ 1) for i in range(count)])
    state_cube = state_rows.reshape(state.shape)
    mate_cube = state_mate.reshape(state.shape)
    chip_state = jnp.where(
        odd,
        shrinkage_multiplier[:, None, None] * mate_cube + state_cube,
        factor_mate[:, None, None] * state_cube + mate_cube,
    )
    chip_factor = shrinkage_multiplier * factor_mate
    chip_top = chip_factor.astype(jnp.bfloat16)
    chip_rest = (chip_factor - chip_top.astype(jnp.float32)).astype(jnp.bfloat16)
    chip_rows = jnp.pad(jnp.stack([chip_top, chip_rest]), ((0, 14), (0, DH - heads_here)))
    packet = jnp.concatenate(
        [chip_state.astype(jnp.bfloat16).reshape(n_state, DH), chip_rows], axis=0
    )
    routes = [(i, i + 1) for i in range(1, count - 1, 2)] + [(i, i + 5) for i in range(0, count - 5, 2)]
    packet, soft_q = lax.optimization_barrier((packet, soft_q))
    received = lax.ppermute(packet, "ctx", routes)
    span_rows = (SPAN + 1) * rows
    key_pos = shard * rows - SPAN * rows + jnp.arange(span_rows, dtype=jnp.int32)
    key_docs = jnp.where(key_pos >= 0, document_of(key_pos, doc_lengths), -1)
    allowed = (key_docs[None, :] == docs[:, None]) & (key_pos[None, :] <= positions[:, None])
    soft_query = soft_q.reshape(rows, kv_here, group, DH)
    paired = window.reshape(SPAN + 1, 2, rows, kv_width)
    all_keys = paired[:, 0].reshape(span_rows, kv_here, DH)
    all_values = paired[:, 1].reshape(span_rows, kv_here, DH)
    scores = jnp.einsum(
        "tkgd,skd->kgts", soft_query, all_keys, preferred_element_type=jnp.float32
    ) * DH ** (-0.5)
    top = jnp.max(jnp.where(allowed, scores, -1e30), axis=-1, keepdims=True)
    expd = jnp.where(allowed, jnp.exp(jnp.minimum(scores - top, 0.0)), 0.0)
    total = jnp.sum(expd, axis=-1)
    attended = jnp.einsum(
        "kgts,skd->tkgd", expd.astype(jnp.bfloat16), all_values, preferred_element_type=jnp.float32
    )
    attended = attended / total.transpose(2, 0, 1)[..., None]
    soft_out = attended.reshape(rows, kv_here * group * DH).astype(jnp.bfloat16)
    soft_out, received = lax.optimization_barrier((soft_out, received))
    mate_packet = lax.ppermute(received, "ctx", [(i, i ^ 1) for i in range(count)])
    near = jnp.where(odd, mate_packet, received)
    far = jnp.where(odd, received, mate_packet)

    def unpack(got_packet):
        chip = got_packet[:n_state].reshape(state.shape).astype(jnp.float32)
        mult = got_packet[n_state, :heads_here].astype(jnp.float32) + got_packet[
            n_state + 1, :heads_here
        ].astype(jnp.float32)
        return chip, mult

    state_near, factor_near = unpack(near)
    state_far, _ = unpack(far)
    incoming_even = state_near + factor_near[:, None, None] * state_far
    incoming = jnp.where(odd, factor_mate[:, None, None] * incoming_even + mate_cube, incoming_even)
    incoming_b = incoming.astype(jnp.bfloat16)
    outer = jnp.einsum(
        "thd,hde->the", query, incoming_b, preferred_element_type=jnp.float32
    )
    outer = outer * (jnp.exp(level).T * carried[:, None].astype(jnp.float32))[:, :, None]
    mixed = inner + outer
    local_sq = jnp.sum(mixed * mixed, axis=(1, 2))
    total_sq = all_sum(local_sq, "head")
    mean_sq = total_sq / (lax.axis_size("head") * heads_here * DH)
    flat = mixed.reshape(rows, heads_here * DH)
    normed = (
        flat
        * lax.rsqrt(mean_sq + 1e-06)[:, None]
        * lin_gain[None, :]
        * jax.nn.sigmoid(out_gate.astype(jnp.float32))
    )
    lin_out = normed.astype(jnp.bfloat16)
    return (lin_out, soft_out)


def solution(mesh):
    in_specs = (
        P(),
        P("ctx", "head"),
        P("ctx", "head"),
        P("ctx", "head"),
        P("head", "ctx"),
        P("ctx", "head"),
        P("head"),
        P("ctx", "head"),
        P("ctx", "head"),
        P("ctx", "head"),
    )
    out_specs = (P("ctx", "head"), P("ctx", "head"))
    return jax.shard_map(local, mesh=mesh, in_specs=in_specs, out_specs=out_specs, check_vma=False)
```

```python
import jax
import jax.numpy as jnp
from jax import lax
from jax.sharding import PartitionSpec as P

DH = 128
SPAN = 4


def from_behind(shard, axis, by):
    count = lax.axis_size(axis)
    pairs = [(i, i + by) for i in range(count) if 0 <= i + by < count]
    return lax.ppermute(shard, axis, pairs)


def all_sum(x, axis):
    count = lax.axis_size(axis)
    me = lax.axis_index(axis)
    parts = [x]
    for by in range(1, count):
        parts.append(lax.ppermute(x, axis, [(i, (i + by) % count) for i in range(count)]))
    stacked = jnp.stack(parts)
    order = (me - jnp.arange(count)) % count
    return jnp.sum(stacked[order], axis=0)


def document_of(positions, doc_lengths):
    ends = jnp.cumsum(doc_lengths)
    return jnp.sum((ends[None, :] <= positions[:, None]).astype(jnp.int32), axis=1)


def block_terms(query, lookup_array, values, decay, docs, before, last):
    rows = docs.shape[0]
    span = decay.shape[1]
    upto = (jnp.arange(span)[:, None] <= jnp.arange(span)[None, :]).astype(jnp.float32)
    level = jnp.dot(decay, upto, precision=lax.Precision.HIGHEST)
    order = jnp.arange(rows)
    same = (docs[:, None] == docs[None, :]) & (order[None, :] <= order[:, None])
    scores = jnp.einsum("thd,shd->hts", query, lookup_array, preferred_element_type=jnp.float32)
    fade = jnp.exp(jnp.minimum(level[:, :, None] - level[:, None, :], 0.0))
    weights = jnp.where(same[None], scores * fade, 0.0).astype(jnp.bfloat16)
    inner = jnp.einsum("hts,shd->thd", weights, values, preferred_element_type=jnp.float32)
    carried = docs == before
    closing = (docs == last).astype(jnp.float32)
    tail = jnp.exp(level[:, -1:] - level) * closing[None, :]
    weighted = (lookup_array.astype(jnp.float32) * tail.T[:, :, None]).astype(jnp.bfloat16)
    state = jnp.einsum("shd,she->hde", weighted, values, preferred_element_type=jnp.float32)
    shrinkage_multiplier = jnp.exp(level[:, -1]) * (last == before).astype(jnp.float32)
    return (inner, level, carried, shrinkage_multiplier, state)


def local(doc_lengths, lin_q, lin_k, lin_v, log_decay, out_gate, lin_gain, soft_q, soft_k, soft_v):
    rows = lin_q.shape[0]
    heads_here = lin_q.shape[1] // DH
    kv_here = soft_k.shape[1] // DH
    group = soft_q.shape[1] // (kv_here * DH)
    shard = lax.axis_index("ctx")
    positions = shard * rows + jnp.arange(rows, dtype=jnp.int32)
    ends = jnp.cumsum(doc_lengths)
    docs = jnp.sum((ends[None, :] <= positions[:, None]).astype(jnp.int32), axis=1)
    last = jnp.sum((ends <= shard * rows + rows - 1).astype(jnp.int32))
    before = jnp.where(shard > 0, jnp.sum((ends <= shard * rows - 1).astype(jnp.int32)), -1)
    query = lin_q.reshape(rows, heads_here, DH)
    lookup_array = lin_k.reshape(rows, heads_here, DH)
    values = lin_v.reshape(rows, heads_here, DH)
    inner, level, carried, shrinkage_multiplier, state = block_terms(
        query, lookup_array, values, log_decay, docs, before, last
    )
    count = lax.axis_size("ctx")
    odd = (shard % 2) == 1
    pair = jnp.stack([soft_k, soft_v])
    kv_width = soft_k.shape[1]
    n_state = heads_here * DH
    state_rows = state.reshape(n_state, DH)
    factor_rows = jnp.pad(shrinkage_multiplier[None, :], ((0, 7), (0, DH - heads_here)))
    window = jnp.concatenate(
        [from_behind(pair, "ctx", step) for step in range(SPAN, 0, -1)] + [pair], axis=0
    )
    first = jnp.concatenate([state_rows, factor_rows], axis=0)
    got = lax.ppermute(first, "ctx", [(i, i ^ 1) for i in range(count)])
    state_mate = got[:n_state]
    factor_mate = got[n_state, :heads_here]
    state_cube = state_rows.reshape(state.shape)
    mate_cube = state_mate.reshape(state.shape)
    chip_state = jnp.where(
        odd,
        shrinkage_multiplier[:, None, None] * mate_cube + state_cube,
        factor_mate[:, None, None] * state_cube + mate_cube,
    )
    chip_factor = shrinkage_multiplier * factor_mate
    chip_top = chip_factor.astype(jnp.bfloat16)
    chip_rest = (chip_factor - chip_top.astype(jnp.float32)).astype(jnp.bfloat16)
    chip_rows = jnp.pad(jnp.stack([chip_top, chip_rest]), ((0, 14), (0, DH - heads_here)))
    packet = jnp.concatenate(
        [chip_state.astype(jnp.bfloat16).reshape(n_state, DH), chip_rows], axis=0
    )
    routes = [(i, i + 1) for i in range(1, count - 1, 2)] + [(i, i + 5) for i in range(0, count - 5, 2)]
    packet, soft_q = lax.optimization_barrier((packet, soft_q))
    received = lax.ppermute(packet, "ctx", routes)
    span_rows = (SPAN + 1) * rows
    key_pos = shard * rows - SPAN * rows + jnp.arange(span_rows, dtype=jnp.int32)
    key_docs = jnp.where(key_pos >= 0, document_of(key_pos, doc_lengths), -1)
    allowed = (key_docs[None, :] == docs[:, None]) & (key_pos[None, :] <= positions[:, None])
    soft_query = soft_q.reshape(rows, kv_here, group, DH)
    paired = window.reshape(SPAN + 1, 2, rows, kv_width)
    all_keys = paired[:, 0].reshape(span_rows, kv_here, DH)
    all_values = paired[:, 1].reshape(span_rows, kv_here, DH)
    scores = jnp.einsum(
        "tkgd,skd->kgts", soft_query, all_keys, preferred_element_type=jnp.float32
    ) * DH ** (-0.5)
    top = jnp.max(jnp.where(allowed, scores, -1e30), axis=-1, keepdims=True)
    expd = jnp.where(allowed, jnp.exp(jnp.minimum(scores - top, 0.0)), 0.0)
    total = jnp.sum(expd, axis=-1)
    attended = jnp.einsum(
        "kgts,skd->tkgd", expd.astype(jnp.bfloat16), all_values, preferred_element_type=jnp.float32
    )
    attended = attended / total.transpose(2, 0, 1)[..., None]
    soft_out = attended.reshape(rows, kv_here * group * DH).astype(jnp.bfloat16)
    soft_out, received = lax.optimization_barrier((soft_out, received))
    mate_packet = lax.ppermute(received, "ctx", [(i, i ^ 1) for i in range(count)])
    near = jnp.where(odd, mate_packet, received)
    far = jnp.where(odd, received, mate_packet)

    def unpack(got_packet):
        chip = got_packet[:n_state].reshape(state.shape).astype(jnp.float32)
        mult = got_packet[n_state, :heads_here].astype(jnp.float32) + got_packet[
            n_state + 1, :heads_here
        ].astype(jnp.float32)
        return chip, mult

    state_near, factor_near = unpack(near)
    state_far, _ = unpack(far)
    incoming_even = state_near + factor_near[:, None, None] * state_far
    incoming = jnp.where(odd, factor_mate[:, None, None] * incoming_even + mate_cube, incoming_even)
    incoming_b = incoming.astype(jnp.bfloat16)
    outer = jnp.einsum(
        "thd,hde->the", query, incoming_b, preferred_element_type=jnp.float32
    )
    outer = outer * (jnp.exp(level).T * carried[:, None].astype(jnp.float32))[:, :, None]
    mixed = inner + outer
    local_sq = jnp.sum(mixed * mixed, axis=(1, 2))
    total_sq = all_sum(local_sq, "head")
    mean_sq = total_sq / (lax.axis_size("head") * heads_here * DH)
    flat = mixed.reshape(rows, heads_here * DH)
    normed = (
        flat
        * lax.rsqrt(mean_sq + 1e-06)[:, None]
        * lin_gain[None, :]
        * jax.nn.sigmoid(out_gate.astype(jnp.float32))
    )
    lin_out = normed.astype(jnp.bfloat16)
    return (lin_out, soft_out)


def solution(mesh):
    in_specs = (
        P(),
        P("ctx", "head"),
        P("ctx", "head"),
        P("ctx", "head"),
        P("head", "ctx"),
        P("ctx", "head"),
        P("head"),
        P("ctx", "head"),
        P("ctx", "head"),
        P("ctx", "head"),
    )
    out_specs = (P("ctx", "head"), P("ctx", "head"))
    return jax.shard_map(local, mesh=mesh, in_specs=in_specs, out_specs=out_specs, check_vma=False)
```
